32 devices in a mesh: groups: 2 (over x), slot: 16 (over z, y, core).
Axes of the slice: x: 2, y: 2, z: 4, core: 2. Of those that a mesh axis runs over, the one named last changes fastest.
Arguments:
- timesteps: int32 [32], P(('groups', 'slot')), parts along dimension 0, may hold values from 50 to 799
- prompt_ids: int32 [154], P('groups'), parts along dimension 0, may hold values from 0 to 49407
- start_latent: float32 [8, 4, 2, 128], P('groups'), parts along dimension 0, may hold values from -6 to 6
- iterate: float32 [32, 4, 4, 2, 128], P(('groups', 'slot')), parts along dimension 0, may hold values from -6 to 6
- fresh_noise: float32 [32, 4, 4, 2, 128], P(('groups', 'slot')), parts along dimension 0, may hold values from -6 to 6
- token_table: bfloat16 [49408, 1024], P('slot'), may hold values from -6 to 6
- empty_text: float32 [1024], replicated, may hold values from -6 to 6
- time_in: bfloat16 [320, 1280], replicated, may hold values from -0.3125 to 0.3125
- time_out: bfloat16 [1280, 320], replicated, may hold values from -0.15625 to 0.15625
- text_proj: bfloat16 [1024, 320], replicated, may hold values from -0.1875 to 0.1875
- conv_first: bfloat16 [9, 320, 4], replicated, may hold values from -1 to 1
- spatial_weights: bfloat16 [2, 9, 320, 320], replicated, may hold values from -0.109375 to 0.109375
- temporal_weights: bfloat16 [2, 3, 320, 320], replicated, may hold values from -0.1875 to 0.1875
- conv_last: bfloat16 [9, 4, 320], replicated, may hold values from -0.109375 to 0.109375
Outputs:
- new_iterate: float32 [32, 4, 4, 2, 128], P(('groups', 'slot')), parts along dimension 0
- final_latent: float32 [8, 4, 2, 128], P('groups'), parts along dimension 0
The draws below stay inside these ranges and needn't reach their ends.
There are 2 independent parts, one for each index of `groups`. The reference program is written for one: setup_inputs(seed, part) draws one part's arguments, and reference() takes and returns one part's arrays. A program takes and returns all parts, laid end to end along the dimension named above; an argument that names none is the same for every part. Nothing has to cross between parts.
All inputs are finite; a program needn't handle non-finite values.
Results may differ from the reference program's by a relative error of at most 0.012.
Values sent between devices are 32-bit elements; how exact they have to be, the bound alone decides.
No kernel may reach another device: no remote copies, remote signals or barrier semaphores. Data moves between devices by JAX's collectives and lax.ppermute only.
A program may use at most 64 MiB of HBM per device.

```python
import math
import jax
import jax.numpy as jnp
import numpy as np
from jax import lax

LAT = 4
CH = 320
TIME = 1280
TEXT = 1024
VOCAB = 49408
PROMPT = 77
GROUPS = 32
SECTIONS = 2
FRAMES = 4
ROWS = 2
COLS = 128
DT = 50
TMAX = 800
SLOTS = 16


def plant(values, own_key, smallest, top_value):
    shape = values.shape
    place = [jax.random.randint(jax.random.fold_in(own_key, axis), (), 0, shape[axis]) for axis in range(len(shape))]
    values = values.at[tuple(place)].set(smallest)
    longest = shape.index(max(shape))
    place[longest] = (place[longest] + 1) % shape[longest]
    return values.at[tuple(place)].set(top_value)


def shard_levels(own_key, extent, shards, least, largest):
    def one(position, blocks):
        draws = jax.random.uniform(jax.random.fold_in(jax.random.fold_in(own_key, 6), position), (blocks,), jnp.float32, least / len(shards), largest / len(shards))
        return jnp.repeat(jnp.exp(draws), extent[position] // blocks).reshape((-1,) + (1,) * (len(extent) - position - 1))

    factor_of = one(*shards[0])
    for cut in shards[1:]:
        factor_of = factor_of * one(*cut)
    return factor_of


def rank_table(count, skew):
    weights = [(1 << 20) // math.isqrt(grade ** skew) + 1 for grade in range(1, count + 1)]
    scale = 1 + sum(weights) // (1 << 30)
    return np.cumsum(np.array([max(1, weight // scale) for weight in weights]))


def ranked_ids(own_key, shape, amount, slope):
    table = rank_table(amount, slope)
    lot = jax.random.randint(jax.random.fold_in(own_key, 1), shape, 0, int(table[amount - 1]))
    grade = jnp.searchsorted(jnp.asarray(table, jnp.int32), lot, side="right")
    return jax.random.permutation(jax.random.fold_in(own_key, 2), amount)[grade].astype(jnp.int32)


def noise(key, shape, scale, bound, split=(), kind=jnp.bfloat16):
    level = shard_levels(key, shape, split, -0.22, 0.18) if split else 1.0
    array = jax.random.normal(key, shape, jnp.float32) * scale * level
    return jnp.minimum(jnp.maximum(array, -bound), bound).astype(kind)


def setup_inputs(seed: int = 0, part: int = 0) -> dict:
    key_of = jax.random.split(jax.random.key(seed), 15)
    own_keys = jax.random.split(jax.random.fold_in(key_of[14], part), 15)
    return {
        "timesteps": plant(jax.random.randint(own_keys[0], (SLOTS,), DT, TMAX), jax.random.fold_in(own_keys[0], 1), DT, TMAX - 1).astype(jnp.int32),
        "prompt_ids": plant(ranked_ids(own_keys[1], (PROMPT,), VOCAB, 2), jax.random.fold_in(own_keys[1], 3), 0, VOCAB - 1).astype(jnp.int32),
        "start_latent": noise(own_keys[2], (LAT, FRAMES, ROWS, COLS), 1.0, 6.0, (), jnp.float32),
        "iterate": noise(own_keys[3], (SLOTS, LAT, FRAMES, ROWS, COLS), 1.0, 6.0, ((0, 16),), jnp.float32),
        "fresh_noise": noise(own_keys[4], (SLOTS, LAT, FRAMES, ROWS, COLS), 1.0, 6.0, ((0, 16),), jnp.float32),
        "token_table": noise(key_of[5], (VOCAB, TEXT), 1.0, 6.0, ((0, 16),)),
        "empty_text": noise(key_of[6], (TEXT,), 1.0, 6.0, (), jnp.float32),
        "time_in": noise(key_of[7], (CH, TIME), CH ** -0.5, 0.3125),
        "time_out": noise(key_of[8], (TIME, CH), TIME ** -0.5, 0.15625),
        "text_proj": noise(key_of[9], (TEXT, CH), TEXT ** -0.5, 0.1875),
        "conv_first": noise(key_of[10], (9, CH, LAT), (9 * LAT) ** -0.5, 1.0),
        "spatial_weights": noise(key_of[11], (SECTIONS, 9, CH, CH), (9 * CH) ** -0.5, 0.109375),
        "temporal_weights": noise(key_of[12], (SECTIONS, 3, CH, CH), (3 * CH) ** -0.5, 0.1875),
        "conv_last": noise(key_of[13], (9, LAT, CH), (9 * CH) ** -0.5, 0.109375),
    }


NORM_EPS = 1e-05
GUIDANCE_SCALE = 5.0

def alpha_bar(step_value):
    phase_angle = (step_value / 1000.0 + 0.008) / 1.008 * (jnp.pi / 2.0)
    cosine = jnp.cos(phase_angle)
    return cosine * cosine

def layer_norm(values):
    average = jnp.mean(values)
    spread = jnp.mean((values - average) ** 2)
    return (values - average) * lax.rsqrt(spread + NORM_EPS)

def group_norm(values, axes):
    batch, channels = (values.shape[0], values.shape[1])
    shaped = values.reshape((batch, GROUPS, channels // GROUPS) + values.shape[2:])
    average = lax.optimization_barrier(jnp.mean(shaped, axis=axes, keepdims=True))
    spread = lax.optimization_barrier(jnp.mean((shaped - average) ** 2, axis=axes, keepdims=True))
    return ((shaped - average) * lax.rsqrt(spread + NORM_EPS)).reshape(values.shape)

def conv_space(inputs, weight):
    padded = jnp.pad(inputs.astype(jnp.float32), ((0, 0), (0, 0), (0, 0), (1, 1), (1, 1)))
    row_count, col_count = (inputs.shape[3], inputs.shape[4])
    result = None
    for tap_index in range(9):
        row_step = tap_index // 3
        col_step = tap_index % 3
        window = padded[:, :, :, row_step:row_step + row_count, col_step:col_step + col_count]
        term = jnp.einsum('oc,bcfrw->bofrw', weight[tap_index].astype(jnp.float32), window)
        result = term if result is None else result + term
    return result

def conv_time(inputs, weight):
    padded = jnp.pad(inputs.astype(jnp.float32), ((0, 0), (0, 0), (1, 1), (0, 0), (0, 0)))
    frame_count = inputs.shape[2]
    result = None
    for tap_index in range(3):
        window = padded[:, :, tap_index:tap_index + frame_count]
        term = jnp.einsum('oc,bcfrw->bofrw', weight[tap_index].astype(jnp.float32), window)
        result = term if result is None else result + term
    return result

def reference(timesteps, prompt_ids, start_latent, iterate, fresh_noise, token_table, empty_text, time_in, time_out, text_proj, conv_first, spatial_weights, temporal_weights, conv_last):
    token_rows = token_table[prompt_ids].astype(jnp.float32)
    pooled = lax.optimization_barrier(jnp.mean(token_rows, axis=0))
    text_pair = jnp.stack([layer_norm(pooled), layer_norm(empty_text)]).astype(jnp.bfloat16)
    text_vector = jnp.dot(text_pair, text_proj, preferred_element_type=jnp.float32)
    half_width = CH // 2
    frequency = jnp.exp(-jnp.log(10000.0) * jnp.arange(half_width, dtype=jnp.float32) / half_width)

    def slot_drift(packed):
        step_index, latent, fresh = packed
        step_value = step_index.astype(jnp.float32)
        angles = step_value * frequency
        feature = jnp.concatenate([jnp.cos(angles), jnp.sin(angles)]).astype(jnp.bfloat16)[None, :]
        hidden = jax.nn.silu(jnp.dot(feature, time_in, preferred_element_type=jnp.float32)).astype(jnp.bfloat16)
        time_vector = jnp.dot(hidden, time_out, preferred_element_type=jnp.float32)
        embedding = text_vector + time_vector
        state = (conv_space(latent.astype(jnp.bfloat16)[None], conv_first) + embedding[:, :, None, None, None]).astype(jnp.bfloat16)
        for section in range(SECTIONS):
            normed = jax.nn.silu(group_norm(state.astype(jnp.float32), (2, 4, 5))).astype(jnp.bfloat16)
            state = (state.astype(jnp.float32) + conv_space(normed, spatial_weights[section])).astype(jnp.bfloat16)
            normed = jax.nn.silu(group_norm(state.astype(jnp.float32), (2, 3, 4, 5))).astype(jnp.bfloat16)
            state = (state.astype(jnp.float32) + conv_time(normed, temporal_weights[section])).astype(jnp.bfloat16)
        normed = jax.nn.silu(group_norm(state.astype(jnp.float32), (2, 4, 5))).astype(jnp.bfloat16)
        predicted = conv_space(normed, conv_last)
        guided = predicted[1] + GUIDANCE_SCALE * (predicted[0] - predicted[1])
        alpha_now = alpha_bar(step_value)
        alpha_prev = alpha_bar(step_value - DT)
        scale_ratio = jnp.sqrt(alpha_prev / alpha_now)
        noise_square = (1.0 - alpha_prev) * (1.0 - alpha_now / alpha_prev) / (1.0 - alpha_now)
        kept_square = (1.0 - alpha_prev) * (alpha_now / alpha_prev - alpha_now) / (1.0 - alpha_now)
        eps_factor = jnp.sqrt(kept_square) - scale_ratio * jnp.sqrt(1.0 - alpha_now)
        return (scale_ratio - 1.0) * latent + eps_factor * guided + jnp.sqrt(noise_square) * fresh
    drifts = lax.map(slot_drift, (timesteps, iterate, fresh_noise))
    running = jnp.cumsum(drifts, axis=0)
    earlier = jnp.concatenate([jnp.zeros_like(drifts[:1]), running[:-1]], axis=0)
    new_iterate = start_latent[None] + earlier
    final_latent = start_latent + lax.optimization_barrier(jnp.sum(drifts, axis=0))
    return (new_iterate, final_latent)
```

```python
import jax
import jax.numpy as jnp
from jax import lax
from jax.sharding import PartitionSpec as P

GROUPS = 32
DT = 50


NORM_EPS = 1e-05
GUIDANCE_SCALE = 5.0


def alpha_bar(step_value):
    phase_angle = (step_value / 1000.0 + 0.008) / 1.008 * (jnp.pi / 2.0)
    cosine = jnp.cos(phase_angle)
    return cosine * cosine


def layer_norm(values):
    average = jnp.mean(values)
    spread = jnp.mean((values - average) ** 2)
    return (values - average) * lax.rsqrt(spread + NORM_EPS)


def group_norm(values, axes):
    batch, channels = (values.shape[0], values.shape[1])
    shaped = values.reshape((batch, GROUPS, channels // GROUPS) + values.shape[2:])
    average = jnp.mean(shaped, axis=axes, keepdims=True)
    spread = jnp.mean((shaped - average) ** 2, axis=axes, keepdims=True)
    return ((shaped - average) * lax.rsqrt(spread + NORM_EPS)).reshape(values.shape)


def shift_columns(inputs, offset):
    if offset == 0:
        return inputs
    blank = jnp.zeros(inputs.shape[:-1] + (1,), inputs.dtype)
    if offset == 1:
        return jnp.concatenate([inputs[..., 1:], blank], axis=-1)
    return jnp.concatenate([blank, inputs[..., :-1]], axis=-1)


def conv_space(inputs, weight):
    row_count = inputs.shape[3]
    result = None
    for col_step in range(3):
        moved = shift_columns(inputs, col_step - 1)
        padded = jnp.pad(moved, ((0, 0), (0, 0), (0, 0), (1, 1), (0, 0)))
        for row_step in range(3):
            window = padded[:, :, :, row_step : row_step + row_count]
            term = jnp.einsum(
                "oc,bcfrw->bofrw",
                weight[row_step * 3 + col_step],
                window,
                preferred_element_type=jnp.float32,
            )
            result = term if result is None else result + term
    return result


def conv_time(inputs, weight):
    padded = jnp.pad(inputs, ((0, 0), (0, 0), (1, 1), (0, 0), (0, 0)))
    frame_count = inputs.shape[2]
    result = None
    for tap_index in range(3):
        window = padded[:, :, tap_index : tap_index + frame_count]
        term = jnp.einsum(
            "oc,bcfrw->bofrw", weight[tap_index], window, preferred_element_type=jnp.float32
        )
        result = term if result is None else result + term
    return result


def local(
    timesteps,
    prompt_ids,
    start_latent,
    iterate,
    fresh_noise,
    token_table,
    empty_text,
    time_in,
    time_out,
    text_proj,
    conv_first,
    spatial_weights,
    temporal_weights,
    conv_last,
):
    shard_rows = token_table.shape[0]
    first_row = lax.axis_index("slot") * shard_rows
    local_ids = prompt_ids - first_row
    held = (local_ids >= 0) & (local_ids < shard_rows)
    rows = token_table[jnp.clip(local_ids, 0, shard_rows - 1)].astype(jnp.float32)
    partial = jnp.sum(jnp.where(held[:, None], rows, 0.0), axis=0)
    pooled = lax.psum(partial, "slot") / prompt_ids.shape[0]
    text_pair = jnp.stack([layer_norm(pooled), layer_norm(empty_text)]).astype(jnp.bfloat16)
    text_vector = jnp.dot(text_pair, text_proj, preferred_element_type=jnp.float32)
    half_width = time_in.shape[0] // 2
    frequency = jnp.exp(-jnp.log(10000.0) * jnp.arange(half_width, dtype=jnp.float32) / half_width)
    step_value = timesteps[0].astype(jnp.float32)
    angles = step_value * frequency
    feature = jnp.concatenate([jnp.cos(angles), jnp.sin(angles)]).astype(jnp.bfloat16)[None, :]
    hidden = jax.nn.silu(jnp.dot(feature, time_in, preferred_element_type=jnp.float32)).astype(
        jnp.bfloat16
    )
    time_vector = jnp.dot(hidden, time_out, preferred_element_type=jnp.float32)
    embedding = text_vector + time_vector
    latent = iterate[0]
    state = (
        conv_space(latent.astype(jnp.bfloat16)[None], conv_first)
        + embedding[:, :, None, None, None]
    ).astype(jnp.bfloat16)
    for section in range(spatial_weights.shape[0]):
        normed = jax.nn.silu(group_norm(state.astype(jnp.float32), (2, 4, 5))).astype(jnp.bfloat16)
        state = (state.astype(jnp.float32) + conv_space(normed, spatial_weights[section])).astype(
            jnp.bfloat16
        )
        normed = jax.nn.silu(group_norm(state.astype(jnp.float32), (2, 3, 4, 5))).astype(
            jnp.bfloat16
        )
        state = (state.astype(jnp.float32) + conv_time(normed, temporal_weights[section])).astype(
            jnp.bfloat16
        )
    normed = jax.nn.silu(group_norm(state.astype(jnp.float32), (2, 4, 5))).astype(jnp.bfloat16)
    predicted = conv_space(normed, conv_last)
    guided = predicted[1] + GUIDANCE_SCALE * (predicted[0] - predicted[1])
    alpha_now = alpha_bar(step_value)
    alpha_prev = alpha_bar(step_value - DT)
    scale_ratio = jnp.sqrt(alpha_prev / alpha_now)
    noise_square = (1.0 - alpha_prev) * (1.0 - alpha_now / alpha_prev) / (1.0 - alpha_now)
    kept_square = (1.0 - alpha_prev) * (alpha_now / alpha_prev - alpha_now) / (1.0 - alpha_now)
    eps_factor = jnp.sqrt(kept_square) - scale_ratio * jnp.sqrt(1.0 - alpha_now)
    drift_term = (
        (scale_ratio - 1.0) * latent + eps_factor * guided + jnp.sqrt(noise_square) * fresh_noise[0]
    )[None]
    everything = lax.all_gather(drift_term[0], "slot")
    lower = jnp.arange(everything.shape[0]) < lax.axis_index("slot")
    earlier = jnp.sum(jnp.where(lower[:, None, None, None, None], everything, 0.0), axis=0)
    new_iterate = start_latent[None] + earlier[None]
    final_latent = start_latent + jnp.sum(everything, axis=0)
    return (new_iterate, final_latent)


def solution(mesh):
    placed = (
        P(("groups", "slot")),
        P("groups"),
        P("groups", None, None, None),
        P(("groups", "slot"), None, None, None, None),
        P(("groups", "slot"), None, None, None, None),
        P("slot", None),
        P(),
        P(),
        P(),
        P(),
        P(),
        P(),
        P(),
        P(),
    )
    return jax.shard_map(
        local,
        mesh=mesh,
        in_specs=placed,
        out_specs=(P(("groups", "slot"), None, None, None, None), P("groups", None, None, None)),
        check_vma=False,
    )
```

```python
import jax
import jax.numpy as jnp
from jax import lax
from jax.sharding import PartitionSpec as P
from jax.experimental import pallas as pl
from jax.experimental.pallas import tpu as pltpu

GROUPS = 32
DT = 50


NORM_EPS = 1e-05
GUIDANCE_SCALE = 5.0


def alpha_bar(step_value):
    phase_angle = (step_value / 1000.0 + 0.008) / 1.008 * (jnp.pi / 2.0)
    cosine = jnp.cos(phase_angle)
    return cosine * cosine


def layer_norm(values):
    average = jnp.mean(values)
    spread = jnp.mean((values - average) ** 2)
    return (values - average) * lax.rsqrt(spread + NORM_EPS)


def group_norm(values, axes):
    batch, channels = (values.shape[0], values.shape[1])
    shaped = values.reshape((batch, GROUPS, channels // GROUPS) + values.shape[2:])
    average = jnp.mean(shaped, axis=axes, keepdims=True)
    spread = jnp.mean((shaped - average) ** 2, axis=axes, keepdims=True)
    return ((shaped - average) * lax.rsqrt(spread + NORM_EPS)).reshape(values.shape)


def shift_columns(inputs, offset):
    if offset == 0:
        return inputs
    blank = jnp.zeros(inputs.shape[:-1] + (1,), inputs.dtype)
    if offset == 1:
        return jnp.concatenate([inputs[..., 1:], blank], axis=-1)
    return jnp.concatenate([blank, inputs[..., :-1]], axis=-1)


def conv_space(inputs, weight):
    row_count = inputs.shape[3]
    result = None
    for col_step in range(3):
        moved = shift_columns(inputs, col_step - 1)
        padded = jnp.pad(moved, ((0, 0), (0, 0), (0, 0), (1, 1), (0, 0)))
        for row_step in range(3):
            window = padded[:, :, :, row_step : row_step + row_count]
            term = jnp.einsum(
                "oc,bcfrw->bofrw",
                weight[row_step * 3 + col_step],
                window,
                preferred_element_type=jnp.float32,
            )
            result = term if result is None else result + term
    return result


def conv_time(inputs, weight):
    padded = jnp.pad(inputs, ((0, 0), (0, 0), (1, 1), (0, 0), (0, 0)))
    frame_count = inputs.shape[2]
    result = None
    for tap_index in range(3):
        window = padded[:, :, tap_index : tap_index + frame_count]
        term = jnp.einsum(
            "oc,bcfrw->bofrw", weight[tap_index], window, preferred_element_type=jnp.float32
        )
        result = term if result is None else result + term
    return result


def unet_body(state_ref, wsp_ref, wt_ref, same_ref, batch_ref, out_ref):
    rows, blocks, cols, chans = state_ref.shape
    frames = blocks // 2
    same = same_ref[...]
    batch_mix = batch_ref[...]
    hi = lax.Precision.HIGHEST

    def group_stats(sums, count, mix):
        if mix is not None:
            sums = jnp.dot(mix, sums, precision=hi, preferred_element_type=jnp.float32)
        return jnp.dot(sums, same, precision=hi, preferred_element_type=jnp.float32) / count

    def norm_silu(x, mix, count):
        colsum = jnp.sum(x[0], axis=1) + jnp.sum(x[1], axis=1)
        mean = group_stats(colsum, count, mix)
        d = x - mean[None, :, None, :]
        sq = d * d
        var = group_stats(jnp.sum(sq[0], axis=1) + jnp.sum(sq[1], axis=1), count, mix)
        v = d * lax.rsqrt(var + NORM_EPS)[None, :, None, :]
        return (v / (1.0 + jnp.exp(-v))).astype(jnp.bfloat16)

    def mm(a, w):
        return lax.dot_general(a, w, (((1,), (1,)), ((), ())), preferred_element_type=jnp.float32)

    col = lax.broadcasted_iota(jnp.int32, (blocks, cols, chans), 1)

    def conv_sp(n, section):
        x0 = n[0].reshape(blocks * cols, chans)
        x1 = n[1].reshape(blocks * cols, chans)
        outs = []
        for row in range(rows):
            own, other = (x0, x1) if row == 0 else (x1, x0)
            other_dr = 1 if row == 0 else -1
            acc = None
            for dc in (-1, 0, 1):
                y = mm(own, wsp_ref[section, 3 + dc + 1]) + mm(other, wsp_ref[section, (other_dr + 1) * 3 + dc + 1])
                y = y.reshape(blocks, cols, chans)
                if dc == -1:
                    y = jnp.where(col == 0, 0.0, pltpu.roll(y, 1, 1))
                elif dc == 1:
                    y = jnp.where(col == cols - 1, 0.0, pltpu.roll(y, cols - 1, 1))
                acc = y if acc is None else acc + y
            outs.append(acc)
        return jnp.stack(outs)

    def conv_tm(n, section):
        n5 = n.reshape(rows, 2, frames, cols, chans)
        blank = jnp.zeros((rows, 2, 1, cols, chans), n.dtype)
        before = jnp.concatenate([blank, n5[:, :, :-1]], axis=2)
        after = jnp.concatenate([n5[:, :, 1:], blank], axis=2)
        flat = rows * blocks * cols
        acc = mm(before.reshape(flat, chans), wt_ref[section, 0])
        acc = acc + mm(n.reshape(flat, chans), wt_ref[section, 1])
        acc = acc + mm(after.reshape(flat, chans), wt_ref[section, 2])
        return acc.reshape(rows, blocks, cols, chans)

    per_frame = float(chans // GROUPS * rows * cols)
    per_sample = per_frame * frames
    state = state_ref[...]
    for section in range(wsp_ref.shape[0]):
        x = state.astype(jnp.float32)
        normed = norm_silu(x, None, per_frame)
        state = (x + conv_sp(normed, section)).astype(jnp.bfloat16)
        x = state.astype(jnp.float32)
        normed = norm_silu(x, batch_mix, per_sample)
        state = (x + conv_tm(normed, section)).astype(jnp.bfloat16)
    out_ref[...] = norm_silu(state.astype(jnp.float32), None, per_frame)


def unet_sections(state, spatial_weights, temporal_weights):
    rows, blocks, cols, chans = state.shape
    group = jnp.arange(chans) // (chans // GROUPS)
    same = (group[:, None] == group[None, :]).astype(jnp.float32)
    block_of = jnp.arange(blocks) // (blocks // 2)
    batch_mix = (block_of[:, None] == block_of[None, :]).astype(jnp.float32)
    return pl.pallas_call(
        unet_body,
        out_shape=jax.ShapeDtypeStruct(state.shape, jnp.bfloat16),
        compiler_params=pltpu.CompilerParams(vmem_limit_bytes=100 * 1024 * 1024 // 2),
    )(state, spatial_weights, temporal_weights, same, batch_mix)


def butterfly_sum(x, axis):
    peers = lax.axis_size(axis)
    if peers & (peers - 1):
        return jnp.sum(lax.all_gather(x, axis), axis=0)
    k = 1
    while k < peers:
        x = x + lax.ppermute(x, axis, [(i, i ^ k) for i in range(peers)])
        k *= 2
    return x


def butterfly_scan(x, axis):
    peers, me = lax.axis_size(axis), lax.axis_index(axis)
    if peers & (peers - 1):
        everything = lax.all_gather(x, axis)
        lower = (jnp.arange(peers) < me).reshape((peers,) + (1,) * x.ndim)
        return jnp.sum(jnp.where(lower, everything, 0.0), axis=0), jnp.sum(everything, axis=0)
    total, before = x, jnp.zeros_like(x)
    k = 1
    while k < peers:
        got = lax.ppermute(total, axis, [(i, i ^ k) for i in range(peers)])
        before = jnp.where((me & k) != 0, before + got, before)
        total = total + got
        k *= 2
    return before, total


def local(
    timesteps,
    prompt_ids,
    start_latent,
    iterate,
    fresh_noise,
    token_table,
    empty_text,
    time_in,
    time_out,
    text_proj,
    conv_first,
    spatial_weights,
    temporal_weights,
    conv_last,
):
    shard_rows = token_table.shape[0]
    first_row = lax.axis_index("slot") * shard_rows
    local_ids = prompt_ids - first_row
    held = (local_ids >= 0) & (local_ids < shard_rows)
    rows = token_table[jnp.clip(local_ids, 0, shard_rows - 1)].astype(jnp.float32)
    partial = jnp.sum(jnp.where(held[:, None], rows, 0.0), axis=0)
    pooled = butterfly_sum(partial, "slot") / prompt_ids.shape[0]
    text_pair = jnp.stack([layer_norm(pooled), layer_norm(empty_text)]).astype(jnp.bfloat16)
    text_vector = jnp.dot(text_pair, text_proj, preferred_element_type=jnp.float32)
    half_width = time_in.shape[0] // 2
    frequency = jnp.exp(-jnp.log(10000.0) * jnp.arange(half_width, dtype=jnp.float32) / half_width)
    step_value = timesteps[0].astype(jnp.float32)
    angles = step_value * frequency
    feature = jnp.concatenate([jnp.cos(angles), jnp.sin(angles)]).astype(jnp.bfloat16)[None, :]
    hidden = jax.nn.silu(jnp.dot(feature, time_in, preferred_element_type=jnp.float32)).astype(
        jnp.bfloat16
    )
    time_vector = jnp.dot(hidden, time_out, preferred_element_type=jnp.float32)
    embedding = text_vector + time_vector
    latent = iterate[0]
    state = (
        conv_space(latent.astype(jnp.bfloat16)[None], conv_first)
        + embedding[:, :, None, None, None]
    ).astype(jnp.bfloat16)
    batch, chans, frames, rows, cols = state.shape
    laid = state.transpose(3, 0, 2, 4, 1).reshape(rows, batch * frames, cols, chans)
    normed = unet_sections(laid, spatial_weights, temporal_weights)
    normed = normed.reshape(rows, batch, frames, cols, chans).transpose(1, 4, 2, 0, 3)
    predicted = conv_space(normed, conv_last)
    guided = predicted[1] + GUIDANCE_SCALE * (predicted[0] - predicted[1])
    alpha_now = alpha_bar(step_value)
    alpha_prev = alpha_bar(step_value - DT)
    scale_ratio = jnp.sqrt(alpha_prev / alpha_now)
    noise_square = (1.0 - alpha_prev) * (1.0 - alpha_now / alpha_prev) / (1.0 - alpha_now)
    kept_square = (1.0 - alpha_prev) * (alpha_now / alpha_prev - alpha_now) / (1.0 - alpha_now)
    eps_factor = jnp.sqrt(kept_square) - scale_ratio * jnp.sqrt(1.0 - alpha_now)
    drift_term = (
        (scale_ratio - 1.0) * latent + eps_factor * guided + jnp.sqrt(noise_square) * fresh_noise[0]
    )[None]
    earlier, total_drift = butterfly_scan(drift_term[0], "slot")
    new_iterate = start_latent[None] + earlier[None]
    final_latent = start_latent + total_drift
    return (new_iterate, final_latent)


def solution(mesh):
    placed = (
        P(("groups", "slot")),
        P("groups"),
        P("groups", None, None, None),
        P(("groups", "slot"), None, None, None, None),
        P(("groups", "slot"), None, None, None, None),
        P("slot", None),
        P(),
        P(),
        P(),
        P(),
        P(),
        P(),
        P(),
        P(),
    )
    return jax.shard_map(
        local,
        mesh=mesh,
        in_specs=placed,
        out_specs=(P(("groups", "slot"), None, None, None, None), P("groups", None, None, None)),
        check_vma=False,
    )
```

```python
import functools

import jax
import jax.numpy as jnp
from jax import lax
from jax.sharding import PartitionSpec as P
from jax.experimental import pallas as pl
from jax.experimental.pallas import tpu as pltpu

GROUPS = 32
DT = 50


NORM_EPS = 1e-05
GUIDANCE_SCALE = 5.0


def alpha_bar(step_value):
    phase_angle = (step_value / 1000.0 + 0.008) / 1.008 * (jnp.pi / 2.0)
    cosine = jnp.cos(phase_angle)
    return cosine * cosine


def layer_norm(values):
    average = jnp.mean(values)
    spread = jnp.mean((values - average) ** 2)
    return (values - average) * lax.rsqrt(spread + NORM_EPS)


def group_norm(values, axes):
    batch, channels = (values.shape[0], values.shape[1])
    shaped = values.reshape((batch, GROUPS, channels // GROUPS) + values.shape[2:])
    average = jnp.mean(shaped, axis=axes, keepdims=True)
    spread = jnp.mean((shaped - average) ** 2, axis=axes, keepdims=True)
    return ((shaped - average) * lax.rsqrt(spread + NORM_EPS)).reshape(values.shape)


def shift_columns(inputs, offset):
    if offset == 0:
        return inputs
    blank = jnp.zeros(inputs.shape[:-1] + (1,), inputs.dtype)
    if offset == 1:
        return jnp.concatenate([inputs[..., 1:], blank], axis=-1)
    return jnp.concatenate([blank, inputs[..., :-1]], axis=-1)


def conv_space(inputs, weight):
    row_count = inputs.shape[3]
    result = None
    for col_step in range(3):
        moved = shift_columns(inputs, col_step - 1)
        padded = jnp.pad(moved, ((0, 0), (0, 0), (0, 0), (1, 1), (0, 0)))
        for row_step in range(3):
            window = padded[:, :, :, row_step : row_step + row_count]
            term = jnp.einsum(
                "oc,bcfrw->bofrw",
                weight[row_step * 3 + col_step],
                window,
                preferred_element_type=jnp.float32,
            )
            result = term if result is None else result + term
    return result


def conv_time(inputs, weight):
    padded = jnp.pad(inputs, ((0, 0), (0, 0), (1, 1), (0, 0), (0, 0)))
    frame_count = inputs.shape[2]
    result = None
    for tap_index in range(3):
        window = padded[:, :, tap_index : tap_index + frame_count]
        term = jnp.einsum(
            "oc,bcfrw->bofrw", weight[tap_index], window, preferred_element_type=jnp.float32
        )
        result = term if result is None else result + term
    return result


def unet_body(state_ref, wsp_ref, wt_ref, same_ref, batch_ref, out_ref, *, batch):
    rows, blocks, cols, chans = state_ref.shape
    frames = blocks // batch
    same = same_ref[...]
    batch_mix = batch_ref[...]
    hi = lax.Precision.HIGHEST

    def group_stats(sums, count, mix):
        if mix is not None:
            sums = jnp.dot(mix, sums, precision=hi, preferred_element_type=jnp.float32)
        return jnp.dot(sums, same, precision=hi, preferred_element_type=jnp.float32) / count

    def norm_silu(x, mix, count):
        colsum = jnp.sum(x[0], axis=1) + jnp.sum(x[1], axis=1)
        mean = group_stats(colsum, count, mix)
        d = x - mean[None, :, None, :]
        sq = d * d
        var = group_stats(jnp.sum(sq[0], axis=1) + jnp.sum(sq[1], axis=1), count, mix)
        v = d * lax.rsqrt(var + NORM_EPS)[None, :, None, :]
        return (v / (1.0 + jnp.exp(-v))).astype(jnp.bfloat16)

    def mm(a, w):
        return lax.dot_general(a, w, (((1,), (1,)), ((), ())), preferred_element_type=jnp.float32)

    col = lax.broadcasted_iota(jnp.int32, (blocks, cols, chans), 1)

    def conv_sp(n, section):
        x0 = n[0].reshape(blocks * cols, chans)
        x1 = n[1].reshape(blocks * cols, chans)
        outs = []
        for row in range(rows):
            own, other = (x0, x1) if row == 0 else (x1, x0)
            other_dr = 1 if row == 0 else -1
            acc = None
            for dc in (-1, 0, 1):
                y = mm(own, wsp_ref[section, 3 + dc + 1]) + mm(other, wsp_ref[section, (other_dr + 1) * 3 + dc + 1])
                y = y.reshape(blocks, cols, chans)
                if dc == -1:
                    y = jnp.where(col == 0, 0.0, pltpu.roll(y, 1, 1))
                elif dc == 1:
                    y = jnp.where(col == cols - 1, 0.0, pltpu.roll(y, cols - 1, 1))
                acc = y if acc is None else acc + y
            outs.append(acc)
        return jnp.stack(outs)

    def conv_tm(n, section):
        n5 = n.reshape(rows, batch, frames, cols, chans)
        blank = jnp.zeros((rows, batch, 1, cols, chans), n.dtype)
        before = jnp.concatenate([blank, n5[:, :, :-1]], axis=2)
        after = jnp.concatenate([n5[:, :, 1:], blank], axis=2)
        flat = rows * blocks * cols
        acc = mm(before.reshape(flat, chans), wt_ref[section, 0])
        acc = acc + mm(n.reshape(flat, chans), wt_ref[section, 1])
        acc = acc + mm(after.reshape(flat, chans), wt_ref[section, 2])
        return acc.reshape(rows, blocks, cols, chans)

    per_frame = float(chans // GROUPS * rows * cols)
    per_sample = per_frame * frames
    state = state_ref[...]
    for section in range(wsp_ref.shape[0]):
        x = state.astype(jnp.float32)
        normed = norm_silu(x, None, per_frame)
        state = (x + conv_sp(normed, section)).astype(jnp.bfloat16)
        x = state.astype(jnp.float32)
        normed = norm_silu(x, batch_mix, per_sample)
        state = (x + conv_tm(normed, section)).astype(jnp.bfloat16)
    out_ref[...] = norm_silu(state.astype(jnp.float32), None, per_frame)


def unet_sections(state, spatial_weights, temporal_weights, batch):
    rows, blocks, cols, chans = state.shape
    group = jnp.arange(chans) // (chans // GROUPS)
    same = (group[:, None] == group[None, :]).astype(jnp.float32)
    block_of = jnp.arange(blocks) // (blocks // batch)
    batch_mix = (block_of[:, None] == block_of[None, :]).astype(jnp.float32)
    return pl.pallas_call(
        functools.partial(unet_body, batch=batch),
        out_shape=jax.ShapeDtypeStruct(state.shape, jnp.bfloat16),
        compiler_params=pltpu.CompilerParams(vmem_limit_bytes=100 * 1024 * 1024 // 2),
        cost_estimate=pl.CostEstimate(
            flops=2 * rows * blocks * cols * chans * chans * 9 * spatial_weights.shape[0],
            transcendentals=rows * blocks * cols * chans * 5,
            bytes_accessed=spatial_weights.size * 2 + temporal_weights.size * 2 + state.size * 4,
        ),
    )(state, spatial_weights, temporal_weights, same, batch_mix)


def butterfly_sum(x, axis):
    peers = lax.axis_size(axis)
    if peers & (peers - 1):
        return jnp.sum(lax.all_gather(x, axis), axis=0)
    k = 1
    while k < peers:
        x = x + lax.ppermute(x, axis, [(i, i ^ k) for i in range(peers)])
        k *= 2
    return x


def butterfly_scan(x, axis):
    peers, me = lax.axis_size(axis), lax.axis_index(axis)
    if peers & (peers - 1):
        everything = lax.all_gather(x, axis)
        lower = (jnp.arange(peers) < me).reshape((peers,) + (1,) * x.ndim)
        return jnp.sum(jnp.where(lower, everything, 0.0), axis=0), jnp.sum(everything, axis=0)
    total, before = x, jnp.zeros_like(x)
    k = 1
    while k < peers:
        got = lax.ppermute(total, axis, [(i, i ^ k) for i in range(peers)])
        before = jnp.where((me & k) != 0, before + got, before)
        total = total + got
        k *= 2
    return before, total


def local(
    timesteps,
    prompt_ids,
    start_latent,
    iterate,
    fresh_noise,
    token_table,
    empty_text,
    time_in,
    time_out,
    text_proj,
    conv_first,
    spatial_weights,
    temporal_weights,
    conv_last,
):
    shard_rows = token_table.shape[0]
    first_row = lax.axis_index("slot") * shard_rows
    local_ids = prompt_ids - first_row
    hits = local_ids[:, None] == jnp.arange(shard_rows, dtype=jnp.int32)[None, :]
    counts = jnp.sum(hits.astype(jnp.float32), axis=0).astype(jnp.bfloat16)[None]
    partial = jnp.dot(counts, token_table, preferred_element_type=jnp.float32)[0]
    pooled = butterfly_sum(partial, "slot") / prompt_ids.shape[0]
    text_cond = layer_norm(pooled).astype(jnp.bfloat16)[None]
    text_uncond = layer_norm(empty_text).astype(jnp.bfloat16)[None]
    vector_cond = jnp.dot(text_cond, text_proj, preferred_element_type=jnp.float32)
    vector_uncond = jnp.dot(text_uncond, text_proj, preferred_element_type=jnp.float32)
    half_width = time_in.shape[0] // 2
    frequency = jnp.exp(-jnp.log(10000.0) * jnp.arange(half_width, dtype=jnp.float32) / half_width)
    step_value = timesteps[0].astype(jnp.float32)
    angles = step_value * frequency
    feature = jnp.concatenate([jnp.cos(angles), jnp.sin(angles)]).astype(jnp.bfloat16)[None, :]
    hidden = jax.nn.silu(jnp.dot(feature, time_in, preferred_element_type=jnp.float32)).astype(
        jnp.bfloat16
    )
    time_vector = jnp.dot(hidden, time_out, preferred_element_type=jnp.float32)
    latent = iterate[0]
    first = conv_space(latent.astype(jnp.bfloat16)[None], conv_first)
    _, chans, frames, rows, cols = first.shape

    def run_sample(text_vector, first):
        embedding = text_vector + time_vector
        state = (first + embedding[:, :, None, None, None]).astype(jnp.bfloat16)
        laid = state.transpose(3, 0, 2, 4, 1).reshape(rows, frames, cols, chans)
        return unet_sections(laid, spatial_weights, temporal_weights, 1)

    normed_uncond = run_sample(vector_uncond, lax.optimization_barrier(first))
    normed_cond = run_sample(vector_cond, first)
    normed = jnp.stack([normed_cond, normed_uncond], axis=1)
    normed = normed.reshape(rows, 2, frames, cols, chans).transpose(1, 4, 2, 0, 3)
    predicted = conv_space(normed, conv_last)
    guided = predicted[1] + GUIDANCE_SCALE * (predicted[0] - predicted[1])
    alpha_now = alpha_bar(step_value)
    alpha_prev = alpha_bar(step_value - DT)
    scale_ratio = jnp.sqrt(alpha_prev / alpha_now)
    noise_square = (1.0 - alpha_prev) * (1.0 - alpha_now / alpha_prev) / (1.0 - alpha_now)
    kept_square = (1.0 - alpha_prev) * (alpha_now / alpha_prev - alpha_now) / (1.0 - alpha_now)
    eps_factor = jnp.sqrt(kept_square) - scale_ratio * jnp.sqrt(1.0 - alpha_now)
    drift_term = (
        (scale_ratio - 1.0) * latent + eps_factor * guided + jnp.sqrt(noise_square) * fresh_noise[0]
    )[None]
    earlier, total_drift = butterfly_scan(drift_term[0], "slot")
    new_iterate = start_latent[None] + earlier[None]
    final_latent = start_latent + total_drift
    return (new_iterate, final_latent)


def solution(mesh):
    placed = (
        P(("groups", "slot")),
        P("groups"),
        P("groups", None, None, None),
        P(("groups", "slot"), None, None, None, None),
        P(("groups", "slot"), None, None, None, None),
        P("slot", None),
        P(),
        P(),
        P(),
        P(),
        P(),
        P(),
        P(),
        P(),
    )
    return jax.shard_map(
        local,
        mesh=mesh,
        in_specs=placed,
        out_specs=(P(("groups", "slot"), None, None, None, None), P("groups", None, None, None)),
        check_vma=False,
    )
```

```python
import jax
import jax.numpy as jnp
from jax import lax
from jax.sharding import PartitionSpec as P
from jax.experimental import pallas as pl
from jax.experimental.pallas import tpu as pltpu

GROUPS = 32
DT = 50


NORM_EPS = 1e-05
GUIDANCE_SCALE = 5.0


def alpha_bar(step_value):
    phase_angle = (step_value / 1000.0 + 0.008) / 1.008 * (jnp.pi / 2.0)
    cosine = jnp.cos(phase_angle)
    return cosine * cosine


def layer_norm(values):
    average = jnp.mean(values)
    spread = jnp.mean((values - average) ** 2)
    return (values - average) * lax.rsqrt(spread + NORM_EPS)


def group_norm(values, axes):
    batch, channels = (values.shape[0], values.shape[1])
    shaped = values.reshape((batch, GROUPS, channels // GROUPS) + values.shape[2:])
    average = jnp.mean(shaped, axis=axes, keepdims=True)
    spread = jnp.mean((shaped - average) ** 2, axis=axes, keepdims=True)
    return ((shaped - average) * lax.rsqrt(spread + NORM_EPS)).reshape(values.shape)


def shift_columns(inputs, offset):
    if offset == 0:
        return inputs
    blank = jnp.zeros(inputs.shape[:-1] + (1,), inputs.dtype)
    if offset == 1:
        return jnp.concatenate([inputs[..., 1:], blank], axis=-1)
    return jnp.concatenate([blank, inputs[..., :-1]], axis=-1)


def conv_space(inputs, weight):
    row_count = inputs.shape[3]
    result = None
    for col_step in range(3):
        moved = shift_columns(inputs, col_step - 1)
        padded = jnp.pad(moved, ((0, 0), (0, 0), (0, 0), (1, 1), (0, 0)))
        for row_step in range(3):
            window = padded[:, :, :, row_step : row_step + row_count]
            term = jnp.einsum(
                "oc,bcfrw->bofrw",
                weight[row_step * 3 + col_step],
                window,
                preferred_element_type=jnp.float32,
            )
            result = term if result is None else result + term
    return result


def conv_time(inputs, weight):
    padded = jnp.pad(inputs, ((0, 0), (0, 0), (1, 1), (0, 0), (0, 0)))
    frame_count = inputs.shape[2]
    result = None
    for tap_index in range(3):
        window = padded[:, :, tap_index : tap_index + frame_count]
        term = jnp.einsum(
            "oc,bcfrw->bofrw", weight[tap_index], window, preferred_element_type=jnp.float32
        )
        result = term if result is None else result + term
    return result


def unet_body(state_ref, wsp_ref, wt_ref, same_ref, batch_ref, out_ref):
    rows, blocks, cols, chans = state_ref.shape
    frames = blocks // 2
    same = same_ref[...]
    batch_mix = batch_ref[...]
    hi = lax.Precision.HIGHEST

    def group_stats(sums, count, mix):
        if mix is not None:
            sums = jnp.dot(mix, sums, precision=hi, preferred_element_type=jnp.float32)
        return jnp.dot(sums, same, precision=hi, preferred_element_type=jnp.float32) / count

    def norm_silu(x, mix, count):
        colsum = jnp.sum(x[0], axis=1) + jnp.sum(x[1], axis=1)
        mean = group_stats(colsum, count, mix)
        d = x - mean[None, :, None, :]
        sq = d * d
        var = group_stats(jnp.sum(sq[0], axis=1) + jnp.sum(sq[1], axis=1), count, mix)
        v = d * lax.rsqrt(var + NORM_EPS)[None, :, None, :]
        return (v * (0.5 + 0.5 * jnp.tanh(0.5 * v))).astype(jnp.bfloat16)

    def mm(a, w):
        return lax.dot_general(a, w, (((1,), (1,)), ((), ())), preferred_element_type=jnp.float32)

    col = lax.broadcasted_iota(jnp.int32, (blocks, cols, chans), 1)

    def conv_sp(n, section):
        x0 = n[0].reshape(blocks * cols, chans)
        x1 = n[1].reshape(blocks * cols, chans)
        outs = []
        for row in range(rows):
            own, other = (x0, x1) if row == 0 else (x1, x0)
            other_dr = 1 if row == 0 else -1
            acc = None
            for dc in (-1, 0, 1):
                y = mm(own, wsp_ref[section, 3 + dc + 1]) + mm(other, wsp_ref[section, (other_dr + 1) * 3 + dc + 1])
                y = y.reshape(blocks, cols, chans)
                if dc == -1:
                    y = jnp.where(col == 0, 0.0, pltpu.roll(y, 1, 1))
                elif dc == 1:
                    y = jnp.where(col == cols - 1, 0.0, pltpu.roll(y, cols - 1, 1))
                acc = y if acc is None else acc + y
            outs.append(acc)
        return jnp.stack(outs)

    def conv_tm(n, section):
        n5 = n.reshape(rows, 2, frames, cols, chans)
        blank = jnp.zeros((rows, 2, 1, cols, chans), n.dtype)
        before = jnp.concatenate([blank, n5[:, :, :-1]], axis=2)
        after = jnp.concatenate([n5[:, :, 1:], blank], axis=2)
        flat = rows * blocks * cols
        acc = mm(before.reshape(flat, chans), wt_ref[section, 0])
        acc = acc + mm(n.reshape(flat, chans), wt_ref[section, 1])
        acc = acc + mm(after.reshape(flat, chans), wt_ref[section, 2])
        return acc.reshape(rows, blocks, cols, chans)

    per_frame = float(chans // GROUPS * rows * cols)
    per_sample = per_frame * frames
    state = state_ref[...]
    for section in range(wsp_ref.shape[0]):
        x = state.astype(jnp.float32)
        normed = norm_silu(x, None, per_frame)
        state = (x + conv_sp(normed, section)).astype(jnp.bfloat16)
        x = state.astype(jnp.float32)
        normed = norm_silu(x, batch_mix, per_sample)
        state = (x + conv_tm(normed, section)).astype(jnp.bfloat16)
    out_ref[...] = norm_silu(state.astype(jnp.float32), None, per_frame)


def unet_sections(state, spatial_weights, temporal_weights):
    rows, blocks, cols, chans = state.shape
    group = jnp.arange(chans) // (chans // GROUPS)
    same = (group[:, None] == group[None, :]).astype(jnp.float32)
    block_of = jnp.arange(blocks) // (blocks // 2)
    batch_mix = (block_of[:, None] == block_of[None, :]).astype(jnp.float32)
    return pl.pallas_call(
        unet_body,
        out_shape=jax.ShapeDtypeStruct(state.shape, jnp.bfloat16),
        compiler_params=pltpu.CompilerParams(vmem_limit_bytes=100 * 1024 * 1024 // 2),
    )(state, spatial_weights, temporal_weights, same, batch_mix)


def butterfly_sum(x, axis):
    peers = lax.axis_size(axis)
    if peers & (peers - 1):
        return jnp.sum(lax.all_gather(x, axis), axis=0)
    k = 1
    while k < peers:
        x = x + lax.ppermute(x, axis, [(i, i ^ k) for i in range(peers)])
        k *= 2
    return x


def butterfly_scan(x, axis):
    peers, me = lax.axis_size(axis), lax.axis_index(axis)
    if peers & (peers - 1):
        everything = lax.all_gather(x, axis)
        lower = (jnp.arange(peers) < me).reshape((peers,) + (1,) * x.ndim)
        return jnp.sum(jnp.where(lower, everything, 0.0), axis=0), jnp.sum(everything, axis=0)
    total, before = x, jnp.zeros_like(x)
    k = 1
    while k < peers:
        got = lax.ppermute(total, axis, [(i, i ^ k) for i in range(peers)])
        before = jnp.where((me & k) != 0, before + got, before)
        total = total + got
        k *= 2
    return before, total


def local(
    timesteps,
    prompt_ids,
    start_latent,
    iterate,
    fresh_noise,
    token_table,
    empty_text,
    time_in,
    time_out,
    text_proj,
    conv_first,
    spatial_weights,
    temporal_weights,
    conv_last,
):
    shard_rows = token_table.shape[0]
    first_row = lax.axis_index("slot") * shard_rows
    local_ids = prompt_ids - first_row
    hits = local_ids[:, None] == jnp.arange(shard_rows, dtype=jnp.int32)[None, :]
    counts = jnp.sum(hits.astype(jnp.float32), axis=0).astype(jnp.bfloat16)[None]
    partial = jnp.dot(counts, token_table, preferred_element_type=jnp.float32)[0]
    pooled = butterfly_sum(partial, "slot") / prompt_ids.shape[0]
    text_pair = jnp.stack([layer_norm(pooled), layer_norm(empty_text)]).astype(jnp.bfloat16)
    text_vector = jnp.dot(text_pair, text_proj, preferred_element_type=jnp.float32)
    half_width = time_in.shape[0] // 2
    frequency = jnp.exp(-jnp.log(10000.0) * jnp.arange(half_width, dtype=jnp.float32) / half_width)
    step_value = timesteps[0].astype(jnp.float32)
    angles = step_value * frequency
    feature = jnp.concatenate([jnp.cos(angles), jnp.sin(angles)]).astype(jnp.bfloat16)[None, :]
    hidden = jax.nn.silu(jnp.dot(feature, time_in, preferred_element_type=jnp.float32)).astype(
        jnp.bfloat16
    )
    time_vector = jnp.dot(hidden, time_out, preferred_element_type=jnp.float32)
    embedding = text_vector + time_vector
    latent = iterate[0]
    state = (
        conv_space(latent.astype(jnp.bfloat16)[None], conv_first)
        + embedding[:, :, None, None, None]
    ).astype(jnp.bfloat16)
    batch, chans, frames, rows, cols = state.shape
    laid = state.transpose(3, 0, 2, 4, 1).reshape(rows, batch * frames, cols, chans)
    normed = unet_sections(laid, spatial_weights, temporal_weights)
    normed = normed.reshape(rows, batch, frames, cols, chans).transpose(1, 4, 2, 0, 3)
    predicted = conv_space(normed, conv_last)
    guided = predicted[1] + GUIDANCE_SCALE * (predicted[0] - predicted[1])
    alpha_now = alpha_bar(step_value)
    alpha_prev = alpha_bar(step_value - DT)
    scale_ratio = jnp.sqrt(alpha_prev / alpha_now)
    noise_square = (1.0 - alpha_prev) * (1.0 - alpha_now / alpha_prev) / (1.0 - alpha_now)
    kept_square = (1.0 - alpha_prev) * (alpha_now / alpha_prev - alpha_now) / (1.0 - alpha_now)
    eps_factor = jnp.sqrt(kept_square) - scale_ratio * jnp.sqrt(1.0 - alpha_now)
    drift_term = (
        (scale_ratio - 1.0) * latent + eps_factor * guided + jnp.sqrt(noise_square) * fresh_noise[0]
    )[None]
    earlier, total_drift = butterfly_scan(drift_term[0], "slot")
    new_iterate = start_latent[None] + earlier[None]
    final_latent = start_latent + total_drift
    return (new_iterate, final_latent)


def solution(mesh):
    placed = (
        P(("groups", "slot")),
        P("groups"),
        P("groups", None, None, None),
        P(("groups", "slot"), None, None, None, None),
        P(("groups", "slot"), None, None, None, None),
        P("slot", None),
        P(),
        P(),
        P(),
        P(),
        P(),
        P(),
        P(),
        P(),
    )
    return jax.shard_map(
        local,
        mesh=mesh,
        in_specs=placed,
        out_specs=(P(("groups", "slot"), None, None, None, None), P("groups", None, None, None)),
        check_vma=False,
    )
```

```python
import jax
import jax.numpy as jnp
from jax import lax
from jax.sharding import PartitionSpec as P
from jax.experimental import pallas as pl
from jax.experimental.pallas import tpu as pltpu

GROUPS = 32
DT = 50


NORM_EPS = 1e-05
GUIDANCE_SCALE = 5.0


def alpha_bar(step_value):
    phase_angle = (step_value / 1000.0 + 0.008) / 1.008 * (jnp.pi / 2.0)
    cosine = jnp.cos(phase_angle)
    return cosine * cosine


def layer_norm(values):
    average = jnp.mean(values)
    spread = jnp.mean((values - average) ** 2)
    return (values - average) * lax.rsqrt(spread + NORM_EPS)


def group_norm(values, axes):
    batch, channels = (values.shape[0], values.shape[1])
    shaped = values.reshape((batch, GROUPS, channels // GROUPS) + values.shape[2:])
    average = jnp.mean(shaped, axis=axes, keepdims=True)
    spread = jnp.mean((shaped - average) ** 2, axis=axes, keepdims=True)
    return ((shaped - average) * lax.rsqrt(spread + NORM_EPS)).reshape(values.shape)


def shift_columns(inputs, offset):
    if offset == 0:
        return inputs
    blank = jnp.zeros(inputs.shape[:-1] + (1,), inputs.dtype)
    if offset == 1:
        return jnp.concatenate([inputs[..., 1:], blank], axis=-1)
    return jnp.concatenate([blank, inputs[..., :-1]], axis=-1)


def conv_space(inputs, weight):
    row_count = inputs.shape[3]
    result = None
    for col_step in range(3):
        moved = shift_columns(inputs, col_step - 1)
        padded = jnp.pad(moved, ((0, 0), (0, 0), (0, 0), (1, 1), (0, 0)))
        for row_step in range(3):
            window = padded[:, :, :, row_step : row_step + row_count]
            term = jnp.einsum(
                "oc,bcfrw->bofrw",
                weight[row_step * 3 + col_step],
                window,
                preferred_element_type=jnp.float32,
            )
            result = term if result is None else result + term
    return result


def conv_time(inputs, weight):
    padded = jnp.pad(inputs, ((0, 0), (0, 0), (1, 1), (0, 0), (0, 0)))
    frame_count = inputs.shape[2]
    result = None
    for tap_index in range(3):
        window = padded[:, :, tap_index : tap_index + frame_count]
        term = jnp.einsum(
            "oc,bcfrw->bofrw", weight[tap_index], window, preferred_element_type=jnp.float32
        )
        result = term if result is None else result + term
    return result


def unet_body(state_ref, wsp_ref, wt_ref, wl_ref, same_ref, batch_ref, out_ref):
    rows, blocks, cols, chans = state_ref.shape
    frames = blocks // 2
    same = same_ref[...]
    batch_mix = batch_ref[...]
    hi = lax.Precision.HIGHEST

    def group_stats(sums, count, mix):
        if mix is not None:
            sums = jnp.dot(mix, sums, precision=hi, preferred_element_type=jnp.float32)
        return jnp.dot(sums, same, precision=hi, preferred_element_type=jnp.float32) / count

    def norm_silu(x, mix, count):
        colsum = jnp.sum(x[0], axis=1) + jnp.sum(x[1], axis=1)
        mean = group_stats(colsum, count, mix)
        d = x - mean[None, :, None, :]
        sq = d * d
        var = group_stats(jnp.sum(sq[0], axis=1) + jnp.sum(sq[1], axis=1), count, mix)
        v = d * lax.rsqrt(var + NORM_EPS)[None, :, None, :]
        return (v * (0.5 + 0.5 * jnp.tanh(0.5 * v))).astype(jnp.bfloat16)

    def mm(a, w):
        return lax.dot_general(a, w, (((1,), (1,)), ((), ())), preferred_element_type=jnp.float32)

    col = lax.broadcasted_iota(jnp.int32, (blocks, cols, chans), 1)

    def conv_sp(n, section):
        x0 = n[0].reshape(blocks * cols, chans)
        x1 = n[1].reshape(blocks * cols, chans)
        outs = []
        for row in range(rows):
            own, other = (x0, x1) if row == 0 else (x1, x0)
            other_dr = 1 if row == 0 else -1
            acc = None
            for dc in (-1, 0, 1):
                y = mm(own, wsp_ref[section, 3 + dc + 1]) + mm(other, wsp_ref[section, (other_dr + 1) * 3 + dc + 1])
                y = y.reshape(blocks, cols, chans)
                if dc == -1:
                    y = jnp.where(col == 0, 0.0, pltpu.roll(y, 1, 1))
                elif dc == 1:
                    y = jnp.where(col == cols - 1, 0.0, pltpu.roll(y, cols - 1, 1))
                acc = y if acc is None else acc + y
            outs.append(acc)
        return jnp.stack(outs)

    def conv_tm(n, section):
        n5 = n.reshape(rows, 2, frames, cols, chans)
        blank = jnp.zeros((rows, 2, 1, cols, chans), n.dtype)
        before = jnp.concatenate([blank, n5[:, :, :-1]], axis=2)
        after = jnp.concatenate([n5[:, :, 1:], blank], axis=2)
        flat = rows * blocks * cols
        acc = mm(before.reshape(flat, chans), wt_ref[section, 0])
        acc = acc + mm(n.reshape(flat, chans), wt_ref[section, 1])
        acc = acc + mm(after.reshape(flat, chans), wt_ref[section, 2])
        return acc.reshape(rows, blocks, cols, chans)

    per_frame = float(chans // GROUPS * rows * cols)
    per_sample = per_frame * frames
    state = state_ref[...]
    for section in range(wsp_ref.shape[0]):
        x = state.astype(jnp.float32)
        normed = norm_silu(x, None, per_frame)
        state = (x + conv_sp(normed, section)).astype(jnp.bfloat16)
        x = state.astype(jnp.float32)
        normed = norm_silu(x, batch_mix, per_sample)
        state = (x + conv_tm(normed, section)).astype(jnp.bfloat16)
    last = norm_silu(state.astype(jnp.float32), None, per_frame)
    x0 = last[0].reshape(blocks * cols, chans)
    x1 = last[1].reshape(blocks * cols, chans)
    lane = lax.broadcasted_iota(jnp.int32, (wl_ref.shape[1], blocks * cols), 1) % cols

    def mm_t(w, a):
        return lax.dot_general(w, a, (((1,), (1,)), ((), ())), preferred_element_type=jnp.float32)

    for row in range(rows):
        own, other = (x0, x1) if row == 0 else (x1, x0)
        other_dr = 1 if row == 0 else -1
        acc = None
        for dc in (-1, 0, 1):
            y = mm_t(wl_ref[3 + dc + 1], own) + mm_t(wl_ref[(other_dr + 1) * 3 + dc + 1], other)
            if dc == -1:
                y = jnp.where(lane == 0, 0.0, pltpu.roll(y, 1, 1))
            elif dc == 1:
                y = jnp.where(lane == cols - 1, 0.0, pltpu.roll(y, blocks * cols - 1, 1))
            acc = y if acc is None else acc + y
        out_ref[row] = acc


def unet_sections(state, spatial_weights, temporal_weights, conv_last):
    rows, blocks, cols, chans = state.shape
    taps, outs, _ = conv_last.shape
    padded = -(-outs // 16) * 16
    last = jnp.concatenate([conv_last, jnp.zeros((taps, padded - outs, chans), conv_last.dtype)], axis=1)
    group = jnp.arange(chans) // (chans // GROUPS)
    same = (group[:, None] == group[None, :]).astype(jnp.float32)
    block_of = jnp.arange(blocks) // (blocks // 2)
    batch_mix = (block_of[:, None] == block_of[None, :]).astype(jnp.float32)
    return pl.pallas_call(
        unet_body,
        out_shape=jax.ShapeDtypeStruct((rows, padded, blocks * cols), jnp.float32),
        compiler_params=pltpu.CompilerParams(vmem_limit_bytes=100 * 1024 * 1024 // 2),
    )(state, spatial_weights, temporal_weights, last, same, batch_mix)[:, :outs]


def butterfly_sum(x, axis):
    peers = lax.axis_size(axis)
    if peers & (peers - 1):
        return jnp.sum(lax.all_gather(x, axis), axis=0)
    k = 1
    while k < peers:
        x = x + lax.ppermute(x, axis, [(i, i ^ k) for i in range(peers)])
        k *= 2
    return x


def butterfly_scan(x, axis):
    peers, me = lax.axis_size(axis), lax.axis_index(axis)
    if peers & (peers - 1):
        everything = lax.all_gather(x, axis)
        lower = (jnp.arange(peers) < me).reshape((peers,) + (1,) * x.ndim)
        return jnp.sum(jnp.where(lower, everything, 0.0), axis=0), jnp.sum(everything, axis=0)
    total, before = x, jnp.zeros_like(x)
    k = 1
    while k < peers:
        got = lax.ppermute(total, axis, [(i, i ^ k) for i in range(peers)])
        before = jnp.where((me & k) != 0, before + got, before)
        total = total + got
        k *= 2
    return before, total


def local(
    timesteps,
    prompt_ids,
    start_latent,
    iterate,
    fresh_noise,
    token_table,
    empty_text,
    time_in,
    time_out,
    text_proj,
    conv_first,
    spatial_weights,
    temporal_weights,
    conv_last,
):
    shard_rows = token_table.shape[0]
    first_row = lax.axis_index("slot") * shard_rows
    local_ids = prompt_ids - first_row
    hits = local_ids[:, None] == jnp.arange(shard_rows, dtype=jnp.int32)[None, :]
    counts = jnp.sum(hits.astype(jnp.float32), axis=0).astype(jnp.bfloat16)[None]
    partial = jnp.dot(counts, token_table, preferred_element_type=jnp.float32)[0]
    pooled = butterfly_sum(partial, "slot") / prompt_ids.shape[0]
    text_pair = jnp.stack([layer_norm(pooled), layer_norm(empty_text)]).astype(jnp.bfloat16)
    text_vector = jnp.dot(text_pair, text_proj, preferred_element_type=jnp.float32)
    half_width = time_in.shape[0] // 2
    frequency = jnp.exp(-jnp.log(10000.0) * jnp.arange(half_width, dtype=jnp.float32) / half_width)
    step_value = timesteps[0].astype(jnp.float32)
    angles = step_value * frequency
    feature = jnp.concatenate([jnp.cos(angles), jnp.sin(angles)]).astype(jnp.bfloat16)[None, :]
    hidden = jax.nn.silu(jnp.dot(feature, time_in, preferred_element_type=jnp.float32)).astype(
        jnp.bfloat16
    )
    time_vector = jnp.dot(hidden, time_out, preferred_element_type=jnp.float32)
    embedding = text_vector + time_vector
    latent = iterate[0]
    state = (
        conv_space(latent.astype(jnp.bfloat16)[None], conv_first)
        + embedding[:, :, None, None, None]
    ).astype(jnp.bfloat16)
    batch, chans, frames, rows, cols = state.shape
    laid = state.transpose(3, 0, 2, 4, 1).reshape(rows, batch * frames, cols, chans)
    predicted = unet_sections(laid, spatial_weights, temporal_weights, conv_last)
    predicted = predicted.reshape(rows, -1, batch, frames, cols).transpose(2, 1, 3, 0, 4)
    guided = predicted[1] + GUIDANCE_SCALE * (predicted[0] - predicted[1])
    alpha_now = alpha_bar(step_value)
    alpha_prev = alpha_bar(step_value - DT)
    scale_ratio = jnp.sqrt(alpha_prev / alpha_now)
    noise_square = (1.0 - alpha_prev) * (1.0 - alpha_now / alpha_prev) / (1.0 - alpha_now)
    kept_square = (1.0 - alpha_prev) * (alpha_now / alpha_prev - alpha_now) / (1.0 - alpha_now)
    eps_factor = jnp.sqrt(kept_square) - scale_ratio * jnp.sqrt(1.0 - alpha_now)
    drift_term = (
        (scale_ratio - 1.0) * latent + eps_factor * guided + jnp.sqrt(noise_square) * fresh_noise[0]
    )[None]
    earlier, total_drift = butterfly_scan(drift_term[0], "slot")
    new_iterate = start_latent[None] + earlier[None]
    final_latent = start_latent + total_drift
    return (new_iterate, final_latent)


def solution(mesh):
    placed = (
        P(("groups", "slot")),
        P("groups"),
        P("groups", None, None, None),
        P(("groups", "slot"), None, None, None, None),
        P(("groups", "slot"), None, None, None, None),
        P("slot", None),
        P(),
        P(),
        P(),
        P(),
        P(),
        P(),
        P(),
        P(),
    )
    return jax.shard_map(
        local,
        mesh=mesh,
        in_specs=placed,
        out_specs=(P(("groups", "slot"), None, None, None, None), P("groups", None, None, None)),
        check_vma=False,
    )
```

```python
import functools

import jax
import jax.numpy as jnp
from jax import lax
from jax.sharding import PartitionSpec as P
from jax.experimental import pallas as pl
from jax.experimental.pallas import tpu as pltpu

GROUPS = 32
DT = 50


NORM_EPS = 1e-05
GUIDANCE_SCALE = 5.0


def alpha_bar(step_value):
    phase_angle = (step_value / 1000.0 + 0.008) / 1.008 * (jnp.pi / 2.0)
    cosine = jnp.cos(phase_angle)
    return cosine * cosine


def layer_norm(values):
    average = jnp.mean(values)
    spread = jnp.mean((values - average) ** 2)
    return (values - average) * lax.rsqrt(spread + NORM_EPS)


def group_norm(values, axes):
    batch, channels = (values.shape[0], values.shape[1])
    shaped = values.reshape((batch, GROUPS, channels // GROUPS) + values.shape[2:])
    average = jnp.mean(shaped, axis=axes, keepdims=True)
    spread = jnp.mean((shaped - average) ** 2, axis=axes, keepdims=True)
    return ((shaped - average) * lax.rsqrt(spread + NORM_EPS)).reshape(values.shape)


def shift_columns(inputs, offset):
    if offset == 0:
        return inputs
    blank = jnp.zeros(inputs.shape[:-1] + (1,), inputs.dtype)
    if offset == 1:
        return jnp.concatenate([inputs[..., 1:], blank], axis=-1)
    return jnp.concatenate([blank, inputs[..., :-1]], axis=-1)


def conv_space(inputs, weight):
    row_count = inputs.shape[3]
    result = None
    for col_step in range(3):
        moved = shift_columns(inputs, col_step - 1)
        padded = jnp.pad(moved, ((0, 0), (0, 0), (0, 0), (1, 1), (0, 0)))
        for row_step in range(3):
            window = padded[:, :, :, row_step : row_step + row_count]
            term = jnp.einsum(
                "oc,bcfrw->bofrw",
                weight[row_step * 3 + col_step],
                window,
                preferred_element_type=jnp.float32,
            )
            result = term if result is None else result + term
    return result


def conv_time(inputs, weight):
    padded = jnp.pad(inputs, ((0, 0), (0, 0), (1, 1), (0, 0), (0, 0)))
    frame_count = inputs.shape[2]
    result = None
    for tap_index in range(3):
        window = padded[:, :, tap_index : tap_index + frame_count]
        term = jnp.einsum(
            "oc,bcfrw->bofrw", weight[tap_index], window, preferred_element_type=jnp.float32
        )
        result = term if result is None else result + term
    return result


def unet_body(
    first_ref, emb_u_ref, time_ref, pooled_ref, tproj_ref, wl_ref, same_ref, batch_ref,
    wsp_hbm, wt_hbm, out_ref, wsp_ref, wt_ref, sems, *, count
):
    rows, frames, cols, chans = first_ref.shape
    blocks = 2 * frames
    copy_sp = pltpu.make_async_copy(wsp_hbm, wsp_ref, sems.at[0])
    copy_sp.start()
    copy_tm = pltpu.make_async_copy(wt_hbm, wt_ref, sems.at[1])
    copy_tm.start()
    same = same_ref[...]
    batch_mix = batch_ref[...]
    hi = lax.Precision.HIGHEST

    pooled = pooled_ref[...] / count
    average = jnp.mean(pooled, axis=1, keepdims=True)
    spread = jnp.mean((pooled - average) ** 2, axis=1, keepdims=True)
    text = ((pooled - average) * lax.rsqrt(spread + NORM_EPS)).astype(jnp.bfloat16)
    text = jnp.broadcast_to(text, (8, text.shape[1]))
    vector = jnp.dot(text, tproj_ref[...], preferred_element_type=jnp.float32)[0:1]
    emb_c = (vector + time_ref[...]).reshape(1, 1, 1, chans)
    emb_u = emb_u_ref[...].reshape(1, 1, 1, chans)
    first = first_ref[...]
    state = jnp.concatenate(
        [(first + emb_c).astype(jnp.bfloat16), (first + emb_u).astype(jnp.bfloat16)], axis=1
    )

    def group_stats(sums, count, mix):
        if mix is not None:
            sums = jnp.dot(mix, sums, precision=hi, preferred_element_type=jnp.float32)
        return jnp.dot(sums, same, precision=hi, preferred_element_type=jnp.float32) / count

    def norm_silu(x, mix, count):
        colsum = jnp.sum(x[0], axis=1) + jnp.sum(x[1], axis=1)
        mean = group_stats(colsum, count, mix)
        d = x - mean[None, :, None, :]
        sq = d * d
        var = group_stats(jnp.sum(sq[0], axis=1) + jnp.sum(sq[1], axis=1), count, mix)
        v = d * lax.rsqrt(var + NORM_EPS)[None, :, None, :]
        return (v * (0.5 + 0.5 * jnp.tanh(0.5 * v))).astype(jnp.bfloat16)

    def mm(a, w):
        return lax.dot_general(a, w, (((1,), (1,)), ((), ())), preferred_element_type=jnp.float32)

    col = lax.broadcasted_iota(jnp.int32, (blocks, cols, chans), 1)

    def conv_sp(n, section):
        x0 = n[0].reshape(blocks * cols, chans)
        x1 = n[1].reshape(blocks * cols, chans)
        outs = []
        for row in range(rows):
            own, other = (x0, x1) if row == 0 else (x1, x0)
            other_dr = 1 if row == 0 else -1
            acc = None
            for dc in (-1, 0, 1):
                y = mm(own, wsp_ref[section, 3 + dc + 1]) + mm(other, wsp_ref[section, (other_dr + 1) * 3 + dc + 1])
                y = y.reshape(blocks, cols, chans)
                if dc == -1:
                    y = jnp.where(col == 0, 0.0, pltpu.roll(y, 1, 1))
                elif dc == 1:
                    y = jnp.where(col == cols - 1, 0.0, pltpu.roll(y, cols - 1, 1))
                acc = y if acc is None else acc + y
            outs.append(acc)
        return jnp.stack(outs)

    def conv_tm(n, section):
        n5 = n.reshape(rows, 2, frames, cols, chans)
        blank = jnp.zeros((rows, 2, 1, cols, chans), n.dtype)
        before = jnp.concatenate([blank, n5[:, :, :-1]], axis=2)
        after = jnp.concatenate([n5[:, :, 1:], blank], axis=2)
        flat = rows * blocks * cols
        acc = mm(before.reshape(flat, chans), wt_ref[section, 0])
        acc = acc + mm(n.reshape(flat, chans), wt_ref[section, 1])
        acc = acc + mm(after.reshape(flat, chans), wt_ref[section, 2])
        return acc.reshape(rows, blocks, cols, chans)

    per_frame = float(chans // GROUPS * rows * cols)
    per_sample = per_frame * frames
    for section in range(wsp_ref.shape[0]):
        x = state.astype(jnp.float32)
        normed = norm_silu(x, None, per_frame)
        if section == 0:
            copy_sp.wait()
        state = (x + conv_sp(normed, section)).astype(jnp.bfloat16)
        x = state.astype(jnp.float32)
        normed = norm_silu(x, batch_mix, per_sample)
        if section == 0:
            copy_tm.wait()
        state = (x + conv_tm(normed, section)).astype(jnp.bfloat16)
    last = norm_silu(state.astype(jnp.float32), None, per_frame)
    x0 = last[0].reshape(blocks * cols, chans)
    x1 = last[1].reshape(blocks * cols, chans)
    stride = out_ref.shape[1]
    lane = lax.broadcasted_iota(jnp.int32, (stride, blocks * cols), 1) % cols

    def mm_t(w, a):
        return lax.dot_general(w, a, (((1,), (1,)), ((), ())), preferred_element_type=jnp.float32)

    for row in range(rows):
        own, other = (x0, x1) if row == 0 else (x1, x0)
        other_dr = 1 if row == 0 else -1
        y = mm_t(wl_ref[3 * stride : 6 * stride], own)
        y = y + mm_t(wl_ref[(other_dr + 1) * 3 * stride : (other_dr + 2) * 3 * stride], other)
        acc = None
        for dc in (-1, 0, 1):
            part = y[(dc + 1) * stride : (dc + 2) * stride]
            if dc == -1:
                part = jnp.where(lane == 0, 0.0, pltpu.roll(part, 1, 1))
            elif dc == 1:
                part = jnp.where(lane == cols - 1, 0.0, pltpu.roll(part, blocks * cols - 1, 1))
            acc = part if acc is None else acc + part
        out_ref[row] = acc


def unet(first, emb_u, time_vector, pooled, text_proj, spatial_weights, temporal_weights, conv_last, count):
    rows, frames, cols, chans = first.shape
    blocks = 2 * frames
    taps, outs, _ = conv_last.shape
    padded = -(-outs // 16) * 16
    last = jnp.concatenate([conv_last, jnp.zeros((taps, padded - outs, chans), conv_last.dtype)], axis=1)
    last = last.reshape(taps * padded, chans)
    group = jnp.arange(chans) // (chans // GROUPS)
    same = (group[:, None] == group[None, :]).astype(jnp.float32)
    block_of = jnp.arange(blocks) // frames
    batch_mix = (block_of[:, None] == block_of[None, :]).astype(jnp.float32)
    vmem = pl.BlockSpec(memory_space=pltpu.MemorySpace.VMEM)
    anywhere = pl.BlockSpec(memory_space=pl.ANY)
    return pl.pallas_call(
        functools.partial(unet_body, count=float(count)),
        out_shape=jax.ShapeDtypeStruct((rows, padded, blocks * cols), jnp.float32),
        in_specs=[vmem] * 8 + [anywhere, anywhere],
        out_specs=vmem,
        scratch_shapes=[
            pltpu.VMEM(spatial_weights.shape, spatial_weights.dtype),
            pltpu.VMEM(temporal_weights.shape, temporal_weights.dtype),
            pltpu.SemaphoreType.DMA((2,)),
        ],
        compiler_params=pltpu.CompilerParams(vmem_limit_bytes=100 * 1024 * 1024 // 2),
        cost_estimate=pl.CostEstimate(
            flops=2 * rows * blocks * cols * chans * chans * 9 * spatial_weights.shape[0],
            transcendentals=rows * blocks * cols * chans * 5,
            bytes_accessed=spatial_weights.size * 2 + temporal_weights.size * 2 + first.size * 4,
        ),
    )(first, emb_u, time_vector, pooled, text_proj, last, same, batch_mix, spatial_weights, temporal_weights)[:, :outs]


def butterfly_sum(x, axis):
    peers = lax.axis_size(axis)
    if peers & (peers - 1):
        return jnp.sum(lax.all_gather(x, axis), axis=0)
    k = 1
    while k < peers:
        x = x + lax.ppermute(x, axis, [(i, i ^ k) for i in range(peers)])
        k *= 2
    return x


def butterfly_scan(x, axis):
    peers, me = lax.axis_size(axis), lax.axis_index(axis)
    if peers & (peers - 1):
        everything = lax.all_gather(x, axis)
        lower = (jnp.arange(peers) < me).reshape((peers,) + (1,) * x.ndim)
        return jnp.sum(jnp.where(lower, everything, 0.0), axis=0), jnp.sum(everything, axis=0)
    total, before = x, jnp.zeros_like(x)
    k = 1
    while k < peers:
        got = lax.ppermute(total, axis, [(i, i ^ k) for i in range(peers)])
        before = jnp.where((me & k) != 0, before + got, before)
        total = total + got
        k *= 2
    return before, total


def local(
    timesteps,
    prompt_ids,
    start_latent,
    iterate,
    fresh_noise,
    token_table,
    empty_text,
    time_in,
    time_out,
    text_proj,
    conv_first,
    spatial_weights,
    temporal_weights,
    conv_last,
):
    shard_rows = token_table.shape[0]
    first_row = lax.axis_index("slot") * shard_rows
    local_ids = prompt_ids - first_row
    hits = local_ids[:, None] == jnp.arange(shard_rows, dtype=jnp.int32)[None, :]
    counts = jnp.sum(hits.astype(jnp.float32), axis=0).astype(jnp.bfloat16)[None]
    partial = jnp.dot(counts, token_table, preferred_element_type=jnp.float32)[0]
    pooled = butterfly_sum(partial, "slot")[None]
    text_uncond = layer_norm(empty_text).astype(jnp.bfloat16)[None]
    vector_uncond = jnp.dot(text_uncond, text_proj, preferred_element_type=jnp.float32)
    half_width = time_in.shape[0] // 2
    frequency = jnp.exp(-jnp.log(10000.0) * jnp.arange(half_width, dtype=jnp.float32) / half_width)
    step_value = timesteps[0].astype(jnp.float32)
    angles = step_value * frequency
    feature = jnp.concatenate([jnp.cos(angles), jnp.sin(angles)]).astype(jnp.bfloat16)[None, :]
    hidden = jax.nn.silu(jnp.dot(feature, time_in, preferred_element_type=jnp.float32)).astype(
        jnp.bfloat16
    )
    time_vector = jnp.dot(hidden, time_out, preferred_element_type=jnp.float32)
    latent = iterate[0]
    first = conv_space(latent.astype(jnp.bfloat16)[None], conv_first)[0].transpose(2, 1, 3, 0)
    rows, frames, cols, chans = first.shape
    predicted = unet(
        first, vector_uncond + time_vector, time_vector, pooled, text_proj,
        spatial_weights, temporal_weights, conv_last, prompt_ids.shape[0],
    )
    predicted = predicted.reshape(rows, -1, 2, frames, cols).transpose(2, 1, 3, 0, 4)
    guided = predicted[1] + GUIDANCE_SCALE * (predicted[0] - predicted[1])
    alpha_now = alpha_bar(step_value)
    alpha_prev = alpha_bar(step_value - DT)
    scale_ratio = jnp.sqrt(alpha_prev / alpha_now)
    noise_square = (1.0 - alpha_prev) * (1.0 - alpha_now / alpha_prev) / (1.0 - alpha_now)
    kept_square = (1.0 - alpha_prev) * (alpha_now / alpha_prev - alpha_now) / (1.0 - alpha_now)
    eps_factor = jnp.sqrt(kept_square) - scale_ratio * jnp.sqrt(1.0 - alpha_now)
    drift_term = (
        (scale_ratio - 1.0) * latent + eps_factor * guided + jnp.sqrt(noise_square) * fresh_noise[0]
    )[None]
    earlier, total_drift = butterfly_scan(drift_term[0], "slot")
    new_iterate = start_latent[None] + earlier[None]
    final_latent = start_latent + total_drift
    return (new_iterate, final_latent)


def solution(mesh):
    placed = (
        P(("groups", "slot")),
        P("groups"),
        P("groups", None, None, None),
        P(("groups", "slot"), None, None, None, None),
        P(("groups", "slot"), None, None, None, None),
        P("slot", None),
        P(),
        P(),
        P(),
        P(),
        P(),
        P(),
        P(),
        P(),
    )
    return jax.shard_map(
        local,
        mesh=mesh,
        in_specs=placed,
        out_specs=(P(("groups", "slot"), None, None, None, None), P("groups", None, None, None)),
        check_vma=False,
    )
```

```python
import functools

import jax
import jax.numpy as jnp
from jax import lax
from jax.sharding import PartitionSpec as P
from jax.experimental import pallas as pl
from jax.experimental.pallas import tpu as pltpu

GROUPS = 32
DT = 50


NORM_EPS = 1e-05
GUIDANCE_SCALE = 5.0


def alpha_bar(step_value):
    phase_angle = (step_value / 1000.0 + 0.008) / 1.008 * (jnp.pi / 2.0)
    cosine = jnp.cos(phase_angle)
    return cosine * cosine


def layer_norm(values):
    average = jnp.mean(values)
    spread = jnp.mean((values - average) ** 2)
    return (values - average) * lax.rsqrt(spread + NORM_EPS)


def group_norm(values, axes):
    batch, channels = (values.shape[0], values.shape[1])
    shaped = values.reshape((batch, GROUPS, channels // GROUPS) + values.shape[2:])
    average = jnp.mean(shaped, axis=axes, keepdims=True)
    spread = jnp.mean((shaped - average) ** 2, axis=axes, keepdims=True)
    return ((shaped - average) * lax.rsqrt(spread + NORM_EPS)).reshape(values.shape)


def shift_columns(inputs, offset):
    if offset == 0:
        return inputs
    blank = jnp.zeros(inputs.shape[:-1] + (1,), inputs.dtype)
    if offset == 1:
        return jnp.concatenate([inputs[..., 1:], blank], axis=-1)
    return jnp.concatenate([blank, inputs[..., :-1]], axis=-1)


def conv_space(inputs, weight):
    row_count = inputs.shape[3]
    result = None
    for col_step in range(3):
        moved = shift_columns(inputs, col_step - 1)
        padded = jnp.pad(moved, ((0, 0), (0, 0), (0, 0), (1, 1), (0, 0)))
        for row_step in range(3):
            window = padded[:, :, :, row_step : row_step + row_count]
            term = jnp.einsum(
                "oc,bcfrw->bofrw",
                weight[row_step * 3 + col_step],
                window,
                preferred_element_type=jnp.float32,
            )
            result = term if result is None else result + term
    return result


def conv_lifted(inputs, weight):
    row_count, col_count = inputs.shape[2], inputs.shape[3]
    padded = jnp.pad(inputs, ((0, 0), (0, 0), (1, 1), (1, 1)))
    windows = jnp.concatenate(
        [padded[:, :, tap // 3 : tap // 3 + row_count, tap % 3 : tap % 3 + col_count] for tap in range(9)],
        axis=0,
    )
    stacked = weight.transpose(1, 0, 2).reshape(weight.shape[1], -1)
    result = lax.dot_general(windows, stacked, (((0,), (1,)), ((), ())), preferred_element_type=jnp.float32)
    return result.transpose(1, 0, 2, 3)


def conv_time(inputs, weight):
    padded = jnp.pad(inputs, ((0, 0), (0, 0), (1, 1), (0, 0), (0, 0)))
    frame_count = inputs.shape[2]
    result = None
    for tap_index in range(3):
        window = padded[:, :, tap_index : tap_index + frame_count]
        term = jnp.einsum(
            "oc,bcfrw->bofrw", weight[tap_index], window, preferred_element_type=jnp.float32
        )
        result = term if result is None else result + term
    return result


def unet_body(
    first_ref, emb_u_ref, time_ref, pooled_ref, tproj_ref, wl_ref, same_ref, batch_ref,
    wsp_hbm, wt_hbm, out_ref, wsp_ref, wt_ref, sems, *, count
):
    rows, frames, cols, chans = first_ref.shape
    blocks = 2 * frames
    copy_sp = pltpu.make_async_copy(wsp_hbm, wsp_ref, sems.at[0])
    copy_sp.start()
    copy_tm = pltpu.make_async_copy(wt_hbm, wt_ref, sems.at[1])
    copy_tm.start()
    same = same_ref[...]
    batch_mix = batch_ref[...]
    hi = lax.Precision.HIGHEST

    pooled = pooled_ref[...] / count
    average = jnp.mean(pooled, axis=1, keepdims=True)
    spread = jnp.mean((pooled - average) ** 2, axis=1, keepdims=True)
    text = ((pooled - average) * lax.rsqrt(spread + NORM_EPS)).astype(jnp.bfloat16)
    text = jnp.broadcast_to(text, (8, text.shape[1]))
    vector = jnp.dot(text, tproj_ref[...], preferred_element_type=jnp.float32)[0:1]
    emb_c = (vector + time_ref[...]).reshape(1, 1, 1, chans)
    emb_u = emb_u_ref[...].reshape(1, 1, 1, chans)
    first = first_ref[...]
    state = jnp.concatenate(
        [(first + emb_c).astype(jnp.bfloat16), (first + emb_u).astype(jnp.bfloat16)], axis=1
    )

    def group_stats(sums, count, mix):
        if mix is not None:
            sums = jnp.dot(mix, sums, precision=hi, preferred_element_type=jnp.float32)
        return jnp.dot(sums, same, precision=hi, preferred_element_type=jnp.float32) / count

    def norm_silu(x, mix, count):
        colsum = jnp.sum(x[0], axis=1) + jnp.sum(x[1], axis=1)
        mean = group_stats(colsum, count, mix)
        d = x - mean[None, :, None, :]
        sq = d * d
        var = group_stats(jnp.sum(sq[0], axis=1) + jnp.sum(sq[1], axis=1), count, mix)
        v = d * lax.rsqrt(var + NORM_EPS)[None, :, None, :]
        return (v * (0.5 + 0.5 * jnp.tanh(0.5 * v))).astype(jnp.bfloat16)

    def mm(a, w):
        return lax.dot_general(a, w, (((1,), (1,)), ((), ())), preferred_element_type=jnp.float32)

    col = lax.broadcasted_iota(jnp.int32, (blocks, cols, chans), 1)

    def conv_sp(n, section):
        x0 = n[0].reshape(blocks * cols, chans)
        x1 = n[1].reshape(blocks * cols, chans)
        outs = []
        for row in range(rows):
            own, other = (x0, x1) if row == 0 else (x1, x0)
            other_dr = 1 if row == 0 else -1
            acc = None
            for dc in (-1, 0, 1):
                y = mm(own, wsp_ref[section, 3 + dc + 1]) + mm(other, wsp_ref[section, (other_dr + 1) * 3 + dc + 1])
                y = y.reshape(blocks, cols, chans)
                if dc == -1:
                    y = jnp.where(col == 0, 0.0, pltpu.roll(y, 1, 1))
                elif dc == 1:
                    y = jnp.where(col == cols - 1, 0.0, pltpu.roll(y, cols - 1, 1))
                acc = y if acc is None else acc + y
            outs.append(acc)
        return jnp.stack(outs)

    def conv_tm(n, section):
        n5 = n.reshape(rows, 2, frames, cols, chans)
        blank = jnp.zeros((rows, 2, 1, cols, chans), n.dtype)
        before = jnp.concatenate([blank, n5[:, :, :-1]], axis=2)
        after = jnp.concatenate([n5[:, :, 1:], blank], axis=2)
        flat = rows * blocks * cols
        acc = mm(before.reshape(flat, chans), wt_ref[section, 0])
        acc = acc + mm(n.reshape(flat, chans), wt_ref[section, 1])
        acc = acc + mm(after.reshape(flat, chans), wt_ref[section, 2])
        return acc.reshape(rows, blocks, cols, chans)

    per_frame = float(chans // GROUPS * rows * cols)
    per_sample = per_frame * frames
    for section in range(wsp_ref.shape[0]):
        x = state.astype(jnp.float32)
        normed = norm_silu(x, None, per_frame)
        if section == 0:
            copy_sp.wait()
        state = (x + conv_sp(normed, section)).astype(jnp.bfloat16)
        x = state.astype(jnp.float32)
        normed = norm_silu(x, batch_mix, per_sample)
        if section == 0:
            copy_tm.wait()
        state = (x + conv_tm(normed, section)).astype(jnp.bfloat16)
    last = norm_silu(state.astype(jnp.float32), None, per_frame)
    x0 = last[0].reshape(blocks * cols, chans)
    x1 = last[1].reshape(blocks * cols, chans)
    stride = out_ref.shape[1]
    lane = lax.broadcasted_iota(jnp.int32, (stride, blocks * cols), 1) % cols

    def mm_t(w, a):
        return lax.dot_general(w, a, (((1,), (1,)), ((), ())), preferred_element_type=jnp.float32)

    for row in range(rows):
        own, other = (x0, x1) if row == 0 else (x1, x0)
        other_dr = 1 if row == 0 else -1
        y = mm_t(wl_ref[3 * stride : 6 * stride], own)
        y = y + mm_t(wl_ref[(other_dr + 1) * 3 * stride : (other_dr + 2) * 3 * stride], other)
        acc = None
        for dc in (-1, 0, 1):
            part = y[(dc + 1) * stride : (dc + 2) * stride]
            if dc == -1:
                part = jnp.where(lane == 0, 0.0, pltpu.roll(part, 1, 1))
            elif dc == 1:
                part = jnp.where(lane == cols - 1, 0.0, pltpu.roll(part, blocks * cols - 1, 1))
            acc = part if acc is None else acc + part
        out_ref[row] = acc


def unet(first, emb_u, time_vector, pooled, text_proj, spatial_weights, temporal_weights, conv_last, count):
    rows, frames, cols, chans = first.shape
    blocks = 2 * frames
    taps, outs, _ = conv_last.shape
    padded = -(-outs // 16) * 16
    last = jnp.concatenate([conv_last, jnp.zeros((taps, padded - outs, chans), conv_last.dtype)], axis=1)
    last = last.reshape(taps * padded, chans)
    group = jnp.arange(chans) // (chans // GROUPS)
    same = (group[:, None] == group[None, :]).astype(jnp.float32)
    block_of = jnp.arange(blocks) // frames
    batch_mix = (block_of[:, None] == block_of[None, :]).astype(jnp.float32)
    vmem = pl.BlockSpec(memory_space=pltpu.MemorySpace.VMEM)
    anywhere = pl.BlockSpec(memory_space=pl.ANY)
    return pl.pallas_call(
        functools.partial(unet_body, count=float(count)),
        out_shape=jax.ShapeDtypeStruct((rows, padded, blocks * cols), jnp.float32),
        in_specs=[vmem] * 8 + [anywhere, anywhere],
        out_specs=vmem,
        scratch_shapes=[
            pltpu.VMEM(spatial_weights.shape, spatial_weights.dtype),
            pltpu.VMEM(temporal_weights.shape, temporal_weights.dtype),
            pltpu.SemaphoreType.DMA((2,)),
        ],
        compiler_params=pltpu.CompilerParams(vmem_limit_bytes=100 * 1024 * 1024 // 2),
        cost_estimate=pl.CostEstimate(
            flops=2 * rows * blocks * cols * chans * chans * 9 * spatial_weights.shape[0],
            transcendentals=rows * blocks * cols * chans * 5,
            bytes_accessed=spatial_weights.size * 2 + temporal_weights.size * 2 + first.size * 4,
        ),
    )(first, emb_u, time_vector, pooled, text_proj, last, same, batch_mix, spatial_weights, temporal_weights)[:, :outs]


def butterfly_sum(x, axis):
    peers = lax.axis_size(axis)
    if peers & (peers - 1):
        return jnp.sum(lax.all_gather(x, axis), axis=0)
    k = 1
    while k < peers:
        x = x + lax.ppermute(x, axis, [(i, i ^ k) for i in range(peers)])
        k *= 2
    return x


def butterfly_scan(x, axis):
    peers, me = lax.axis_size(axis), lax.axis_index(axis)
    if peers & (peers - 1):
        everything = lax.all_gather(x, axis)
        lower = (jnp.arange(peers) < me).reshape((peers,) + (1,) * x.ndim)
        return jnp.sum(jnp.where(lower, everything, 0.0), axis=0), jnp.sum(everything, axis=0)
    total, before = x, jnp.zeros_like(x)
    k = 1
    while k < peers:
        got = lax.ppermute(total, axis, [(i, i ^ k) for i in range(peers)])
        before = jnp.where((me & k) != 0, before + got, before)
        total = total + got
        k *= 2
    return before, total


def local(
    timesteps,
    prompt_ids,
    start_latent,
    iterate,
    fresh_noise,
    token_table,
    empty_text,
    time_in,
    time_out,
    text_proj,
    conv_first,
    spatial_weights,
    temporal_weights,
    conv_last,
):
    shard_rows = token_table.shape[0]
    first_row = lax.axis_index("slot") * shard_rows
    local_ids = prompt_ids - first_row
    hits = local_ids[:, None] == jnp.arange(shard_rows, dtype=jnp.int32)[None, :]
    counts = jnp.sum(hits.astype(jnp.float32), axis=0).astype(jnp.bfloat16)[None]
    partial = jnp.dot(counts, token_table, preferred_element_type=jnp.float32)[0]
    pooled = butterfly_sum(partial, "slot")[None]
    text_uncond = layer_norm(empty_text).astype(jnp.bfloat16)[None]
    vector_uncond = jnp.dot(text_uncond, text_proj, preferred_element_type=jnp.float32)
    half_width = time_in.shape[0] // 2
    frequency = jnp.exp(-jnp.log(10000.0) * jnp.arange(half_width, dtype=jnp.float32) / half_width)
    step_value = timesteps[0].astype(jnp.float32)
    angles = step_value * frequency
    feature = jnp.concatenate([jnp.cos(angles), jnp.sin(angles)]).astype(jnp.bfloat16)[None, :]
    hidden = jax.nn.silu(jnp.dot(feature, time_in, preferred_element_type=jnp.float32)).astype(
        jnp.bfloat16
    )
    time_vector = jnp.dot(hidden, time_out, preferred_element_type=jnp.float32)
    latent = iterate[0]
    first = conv_lifted(latent.astype(jnp.bfloat16), conv_first)
    rows, frames, cols, chans = first.shape
    predicted = unet(
        first, vector_uncond + time_vector, time_vector, pooled, text_proj,
        spatial_weights, temporal_weights, conv_last, prompt_ids.shape[0],
    )
    predicted = predicted.reshape(rows, -1, 2, frames, cols).transpose(2, 1, 3, 0, 4)
    guided = predicted[1] + GUIDANCE_SCALE * (predicted[0] - predicted[1])
    alpha_now = alpha_bar(step_value)
    alpha_prev = alpha_bar(step_value - DT)
    scale_ratio = jnp.sqrt(alpha_prev / alpha_now)
    noise_square = (1.0 - alpha_prev) * (1.0 - alpha_now / alpha_prev) / (1.0 - alpha_now)
    kept_square = (1.0 - alpha_prev) * (alpha_now / alpha_prev - alpha_now) / (1.0 - alpha_now)
    eps_factor = jnp.sqrt(kept_square) - scale_ratio * jnp.sqrt(1.0 - alpha_now)
    drift_term = (
        (scale_ratio - 1.0) * latent + eps_factor * guided + jnp.sqrt(noise_square) * fresh_noise[0]
    )[None]
    earlier, total_drift = butterfly_scan(drift_term[0], "slot")
    new_iterate = start_latent[None] + earlier[None]
    final_latent = start_latent + total_drift
    return (new_iterate, final_latent)


def solution(mesh):
    placed = (
        P(("groups", "slot")),
        P("groups"),
        P("groups", None, None, None),
        P(("groups", "slot"), None, None, None, None),
        P(("groups", "slot"), None, None, None, None),
        P("slot", None),
        P(),
        P(),
        P(),
        P(),
        P(),
        P(),
        P(),
        P(),
    )
    return jax.shard_map(
        local,
        mesh=mesh,
        in_specs=placed,
        out_specs=(P(("groups", "slot"), None, None, None, None), P("groups", None, None, None)),
        check_vma=False,
    )
```

```python
import functools

import jax
import jax.numpy as jnp
from jax import lax
from jax.sharding import PartitionSpec as P
from jax.experimental import pallas as pl
from jax.experimental.pallas import tpu as pltpu

GROUPS = 32
DT = 50


NORM_EPS = 1e-05
GUIDANCE_SCALE = 5.0


def alpha_bar(step_value):
    phase_angle = (step_value / 1000.0 + 0.008) / 1.008 * (jnp.pi / 2.0)
    cosine = jnp.cos(phase_angle)
    return cosine * cosine


def layer_norm(values):
    average = jnp.mean(values)
    spread = jnp.mean((values - average) ** 2)
    return (values - average) * lax.rsqrt(spread + NORM_EPS)


def group_norm(values, axes):
    batch, channels = (values.shape[0], values.shape[1])
    shaped = values.reshape((batch, GROUPS, channels // GROUPS) + values.shape[2:])
    average = jnp.mean(shaped, axis=axes, keepdims=True)
    spread = jnp.mean((shaped - average) ** 2, axis=axes, keepdims=True)
    return ((shaped - average) * lax.rsqrt(spread + NORM_EPS)).reshape(values.shape)


def shift_columns(inputs, offset):
    if offset == 0:
        return inputs
    blank = jnp.zeros(inputs.shape[:-1] + (1,), inputs.dtype)
    if offset == 1:
        return jnp.concatenate([inputs[..., 1:], blank], axis=-1)
    return jnp.concatenate([blank, inputs[..., :-1]], axis=-1)


def conv_space(inputs, weight):
    row_count = inputs.shape[3]
    result = None
    for col_step in range(3):
        moved = shift_columns(inputs, col_step - 1)
        padded = jnp.pad(moved, ((0, 0), (0, 0), (0, 0), (1, 1), (0, 0)))
        for row_step in range(3):
            window = padded[:, :, :, row_step : row_step + row_count]
            term = jnp.einsum(
                "oc,bcfrw->bofrw",
                weight[row_step * 3 + col_step],
                window,
                preferred_element_type=jnp.float32,
            )
            result = term if result is None else result + term
    return result


def conv_lifted(inputs, weight):
    row_count, col_count = inputs.shape[2], inputs.shape[3]
    padded = jnp.pad(inputs, ((0, 0), (0, 0), (1, 1), (1, 1)))
    windows = jnp.concatenate(
        [padded[:, :, tap // 3 : tap // 3 + row_count, tap % 3 : tap % 3 + col_count] for tap in range(9)],
        axis=0,
    )
    stacked = weight.transpose(1, 0, 2).reshape(weight.shape[1], -1)
    result = lax.dot_general(windows, stacked, (((0,), (1,)), ((), ())), preferred_element_type=jnp.float32)
    return result.transpose(1, 0, 2, 3)


def conv_time(inputs, weight):
    padded = jnp.pad(inputs, ((0, 0), (0, 0), (1, 1), (0, 0), (0, 0)))
    frame_count = inputs.shape[2]
    result = None
    for tap_index in range(3):
        window = padded[:, :, tap_index : tap_index + frame_count]
        term = jnp.einsum(
            "oc,bcfrw->bofrw", weight[tap_index], window, preferred_element_type=jnp.float32
        )
        result = term if result is None else result + term
    return result


def unet_body(
    first_ref, emb_ref, time_ref, pooled_ref, tproj_ref, wl_ref, same_ref, batch_ref,
    wsp_hbm, wt_hbm, out_ref, wsp_ref, wt_ref, sems, *, count, conditional
):
    rows, frames, cols, chans = first_ref.shape
    blocks = frames
    copy_sp = pltpu.make_async_copy(wsp_hbm, wsp_ref, sems.at[0])
    copy_sp.start()
    copy_tm = pltpu.make_async_copy(wt_hbm, wt_ref, sems.at[1])
    copy_tm.start()
    same = same_ref[...]
    batch_mix = batch_ref[...]
    hi = lax.Precision.HIGHEST

    if conditional:
        pooled = pooled_ref[...] / count
        average = jnp.mean(pooled, axis=1, keepdims=True)
        spread = jnp.mean((pooled - average) ** 2, axis=1, keepdims=True)
        text = ((pooled - average) * lax.rsqrt(spread + NORM_EPS)).astype(jnp.bfloat16)
        text = jnp.broadcast_to(text, (8, text.shape[1]))
        vector = jnp.dot(text, tproj_ref[...], preferred_element_type=jnp.float32)[0:1]
        embedding = vector + time_ref[...]
    else:
        embedding = emb_ref[...]
    state = (first_ref[...] + embedding.reshape(1, 1, 1, chans)).astype(jnp.bfloat16)

    def group_stats(sums, count, mix):
        if mix is not None:
            sums = jnp.dot(mix, sums, precision=hi, preferred_element_type=jnp.float32)
        return jnp.dot(sums, same, precision=hi, preferred_element_type=jnp.float32) / count

    def norm_silu(x, mix, count):
        colsum = jnp.sum(x[0], axis=1) + jnp.sum(x[1], axis=1)
        mean = group_stats(colsum, count, mix)
        d = x - mean[None, :, None, :]
        sq = d * d
        var = group_stats(jnp.sum(sq[0], axis=1) + jnp.sum(sq[1], axis=1), count, mix)
        v = d * lax.rsqrt(var + NORM_EPS)[None, :, None, :]
        return (v * (0.5 + 0.5 * jnp.tanh(0.5 * v))).astype(jnp.bfloat16)

    def mm(a, w):
        return lax.dot_general(a, w, (((1,), (1,)), ((), ())), preferred_element_type=jnp.float32)

    col = lax.broadcasted_iota(jnp.int32, (blocks, cols, chans), 1)

    def conv_sp(n, section):
        x0 = n[0].reshape(blocks * cols, chans)
        x1 = n[1].reshape(blocks * cols, chans)
        outs = []
        for row in range(rows):
            own, other = (x0, x1) if row == 0 else (x1, x0)
            other_dr = 1 if row == 0 else -1
            acc = None
            for dc in (-1, 0, 1):
                y = mm(own, wsp_ref[section, 3 + dc + 1]) + mm(other, wsp_ref[section, (other_dr + 1) * 3 + dc + 1])
                y = y.reshape(blocks, cols, chans)
                if dc == -1:
                    y = jnp.where(col == 0, 0.0, pltpu.roll(y, 1, 1))
                elif dc == 1:
                    y = jnp.where(col == cols - 1, 0.0, pltpu.roll(y, cols - 1, 1))
                acc = y if acc is None else acc + y
            outs.append(acc)
        return jnp.stack(outs)

    def conv_tm(n, section):
        blank = jnp.zeros((rows, 1, cols, chans), n.dtype)
        before = jnp.concatenate([blank, n[:, :-1]], axis=1)
        after = jnp.concatenate([n[:, 1:], blank], axis=1)
        flat = rows * blocks * cols
        acc = mm(before.reshape(flat, chans), wt_ref[section, 0])
        acc = acc + mm(n.reshape(flat, chans), wt_ref[section, 1])
        acc = acc + mm(after.reshape(flat, chans), wt_ref[section, 2])
        return acc.reshape(rows, blocks, cols, chans)

    per_frame = float(chans // GROUPS * rows * cols)
    per_sample = per_frame * frames
    for section in range(wsp_ref.shape[0]):
        x = state.astype(jnp.float32)
        normed = norm_silu(x, None, per_frame)
        if section == 0:
            copy_sp.wait()
        state = (x + conv_sp(normed, section)).astype(jnp.bfloat16)
        x = state.astype(jnp.float32)
        normed = norm_silu(x, batch_mix, per_sample)
        if section == 0:
            copy_tm.wait()
        state = (x + conv_tm(normed, section)).astype(jnp.bfloat16)
    last = norm_silu(state.astype(jnp.float32), None, per_frame)
    x0 = last[0].reshape(blocks * cols, chans)
    x1 = last[1].reshape(blocks * cols, chans)
    stride = out_ref.shape[1]
    lane = lax.broadcasted_iota(jnp.int32, (stride, blocks * cols), 1) % cols

    def mm_t(w, a):
        return lax.dot_general(w, a, (((1,), (1,)), ((), ())), preferred_element_type=jnp.float32)

    for row in range(rows):
        own, other = (x0, x1) if row == 0 else (x1, x0)
        other_dr = 1 if row == 0 else -1
        y = mm_t(wl_ref[3 * stride : 6 * stride], own)
        y = y + mm_t(wl_ref[(other_dr + 1) * 3 * stride : (other_dr + 2) * 3 * stride], other)
        acc = None
        for dc in (-1, 0, 1):
            part = y[(dc + 1) * stride : (dc + 2) * stride]
            if dc == -1:
                part = jnp.where(lane == 0, 0.0, pltpu.roll(part, 1, 1))
            elif dc == 1:
                part = jnp.where(lane == cols - 1, 0.0, pltpu.roll(part, blocks * cols - 1, 1))
            acc = part if acc is None else acc + part
        out_ref[row] = acc


def unet(first, emb, time_vector, pooled, text_proj, spatial_weights, temporal_weights, conv_last, count, conditional):
    rows, frames, cols, chans = first.shape
    blocks = frames
    taps, outs, _ = conv_last.shape
    padded = -(-outs // 16) * 16
    last = jnp.concatenate([conv_last, jnp.zeros((taps, padded - outs, chans), conv_last.dtype)], axis=1)
    last = last.reshape(taps * padded, chans)
    group = jnp.arange(chans) // (chans // GROUPS)
    same = (group[:, None] == group[None, :]).astype(jnp.float32)
    block_of = jnp.arange(blocks) // frames
    batch_mix = (block_of[:, None] == block_of[None, :]).astype(jnp.float32)
    vmem = pl.BlockSpec(memory_space=pltpu.MemorySpace.VMEM)
    anywhere = pl.BlockSpec(memory_space=pl.ANY)
    return pl.pallas_call(
        functools.partial(unet_body, count=float(count), conditional=conditional),
        out_shape=jax.ShapeDtypeStruct((rows, padded, blocks * cols), jnp.float32),
        in_specs=[vmem] * 8 + [anywhere, anywhere],
        out_specs=vmem,
        scratch_shapes=[
            pltpu.VMEM(spatial_weights.shape, spatial_weights.dtype),
            pltpu.VMEM(temporal_weights.shape, temporal_weights.dtype),
            pltpu.SemaphoreType.DMA((2,)),
        ],
        compiler_params=pltpu.CompilerParams(vmem_limit_bytes=100 * 1024 * 1024 // 2),
        cost_estimate=pl.CostEstimate(
            flops=2 * rows * blocks * cols * chans * chans * 9 * spatial_weights.shape[0],
            transcendentals=rows * blocks * cols * chans * 5,
            bytes_accessed=spatial_weights.size * 2 + temporal_weights.size * 2 + first.size * 4,
        ),
    )(first, emb, time_vector, pooled, text_proj, last, same, batch_mix, spatial_weights, temporal_weights)[:, :outs]


def butterfly_sum(x, axis, cover):
    peers = lax.axis_size(axis)
    if peers & (peers - 1):
        return jnp.sum(lax.all_gather(x, axis), axis=0), cover
    k = 1
    while k < peers:
        got = lax.ppermute(x, axis, [(i, i ^ k) for i in range(peers)])
        if k == 1:
            got, cover = lax.optimization_barrier((got, cover))
        x = x + got
        k *= 2
    return x, cover


def butterfly_scan(x, axis):
    peers, me = lax.axis_size(axis), lax.axis_index(axis)
    if peers & (peers - 1):
        everything = lax.all_gather(x, axis)
        lower = (jnp.arange(peers) < me).reshape((peers,) + (1,) * x.ndim)
        return jnp.sum(jnp.where(lower, everything, 0.0), axis=0), jnp.sum(everything, axis=0)
    total, before = x, jnp.zeros_like(x)
    k = 1
    while k < peers:
        got = lax.ppermute(total, axis, [(i, i ^ k) for i in range(peers)])
        before = jnp.where((me & k) != 0, before + got, before)
        total = total + got
        k *= 2
    return before, total


def local(
    timesteps,
    prompt_ids,
    start_latent,
    iterate,
    fresh_noise,
    token_table,
    empty_text,
    time_in,
    time_out,
    text_proj,
    conv_first,
    spatial_weights,
    temporal_weights,
    conv_last,
):
    shard_rows = token_table.shape[0]
    first_row = lax.axis_index("slot") * shard_rows
    local_ids = prompt_ids - first_row
    hits = local_ids[:, None] == jnp.arange(shard_rows, dtype=jnp.int32)[None, :]
    counts = jnp.sum(hits.astype(jnp.float32), axis=0).astype(jnp.bfloat16)[None]
    partial = jnp.dot(counts, token_table, preferred_element_type=jnp.float32)[0]
    text_uncond = layer_norm(empty_text).astype(jnp.bfloat16)[None]
    vector_uncond = jnp.dot(text_uncond, text_proj, preferred_element_type=jnp.float32)
    half_width = time_in.shape[0] // 2
    frequency = jnp.exp(-jnp.log(10000.0) * jnp.arange(half_width, dtype=jnp.float32) / half_width)
    step_value = timesteps[0].astype(jnp.float32)
    angles = step_value * frequency
    feature = jnp.concatenate([jnp.cos(angles), jnp.sin(angles)]).astype(jnp.bfloat16)[None, :]
    hidden = jax.nn.silu(jnp.dot(feature, time_in, preferred_element_type=jnp.float32)).astype(
        jnp.bfloat16
    )
    time_vector = jnp.dot(hidden, time_out, preferred_element_type=jnp.float32)
    latent = iterate[0]
    first = conv_lifted(latent.astype(jnp.bfloat16), conv_first)
    rows, frames, cols, chans = first.shape
    weights = (spatial_weights, temporal_weights, conv_last, prompt_ids.shape[0])
    emb_uncond = vector_uncond + time_vector
    predicted_uncond = unet(first, emb_uncond, time_vector, emb_uncond, emb_uncond, *weights, False)
    pooled, predicted_uncond = butterfly_sum(partial, "slot", predicted_uncond)
    predicted_cond = unet(first, time_vector, time_vector, pooled[None], text_proj, *weights, True)
    predicted = jnp.stack([predicted_cond, predicted_uncond])
    predicted = predicted.reshape(2, rows, -1, frames, cols).transpose(0, 2, 3, 1, 4)
    guided = predicted[1] + GUIDANCE_SCALE * (predicted[0] - predicted[1])
    alpha_now = alpha_bar(step_value)
    alpha_prev = alpha_bar(step_value - DT)
    scale_ratio = jnp.sqrt(alpha_prev / alpha_now)
    noise_square = (1.0 - alpha_prev) * (1.0 - alpha_now / alpha_prev) / (1.0 - alpha_now)
    kept_square = (1.0 - alpha_prev) * (alpha_now / alpha_prev - alpha_now) / (1.0 - alpha_now)
    eps_factor = jnp.sqrt(kept_square) - scale_ratio * jnp.sqrt(1.0 - alpha_now)
    drift_term = (
        (scale_ratio - 1.0) * latent + eps_factor * guided + jnp.sqrt(noise_square) * fresh_noise[0]
    )[None]
    earlier, total_drift = butterfly_scan(drift_term[0], "slot")
    new_iterate = start_latent[None] + earlier[None]
    final_latent = start_latent + total_drift
    return (new_iterate, final_latent)


def solution(mesh):
    placed = (
        P(("groups", "slot")),
        P("groups"),
        P("groups", None, None, None),
        P(("groups", "slot"), None, None, None, None),
        P(("groups", "slot"), None, None, None, None),
        P("slot", None),
        P(),
        P(),
        P(),
        P(),
        P(),
        P(),
        P(),
        P(),
    )
    return jax.shard_map(
        local,
        mesh=mesh,
        in_specs=placed,
        out_specs=(P(("groups", "slot"), None, None, None, None), P("groups", None, None, None)),
        check_vma=False,
    )
```

```python
import functools

import jax
import jax.numpy as jnp
from jax import lax
from jax.sharding import PartitionSpec as P
from jax.experimental import pallas as pl
from jax.experimental.pallas import tpu as pltpu

GROUPS = 32
DT = 50


NORM_EPS = 1e-05
GUIDANCE_SCALE = 5.0


def alpha_bar(step_value):
    phase_angle = (step_value / 1000.0 + 0.008) / 1.008 * (jnp.pi / 2.0)
    cosine = jnp.cos(phase_angle)
    return cosine * cosine


def layer_norm(values):
    average = jnp.mean(values)
    spread = jnp.mean((values - average) ** 2)
    return (values - average) * lax.rsqrt(spread + NORM_EPS)


def group_norm(values, axes):
    batch, channels = (values.shape[0], values.shape[1])
    shaped = values.reshape((batch, GROUPS, channels // GROUPS) + values.shape[2:])
    average = jnp.mean(shaped, axis=axes, keepdims=True)
    spread = jnp.mean((shaped - average) ** 2, axis=axes, keepdims=True)
    return ((shaped - average) * lax.rsqrt(spread + NORM_EPS)).reshape(values.shape)


def shift_columns(inputs, offset):
    if offset == 0:
        return inputs
    blank = jnp.zeros(inputs.shape[:-1] + (1,), inputs.dtype)
    if offset == 1:
        return jnp.concatenate([inputs[..., 1:], blank], axis=-1)
    return jnp.concatenate([blank, inputs[..., :-1]], axis=-1)


def conv_space(inputs, weight):
    row_count = inputs.shape[3]
    result = None
    for col_step in range(3):
        moved = shift_columns(inputs, col_step - 1)
        padded = jnp.pad(moved, ((0, 0), (0, 0), (0, 0), (1, 1), (0, 0)))
        for row_step in range(3):
            window = padded[:, :, :, row_step : row_step + row_count]
            term = jnp.einsum(
                "oc,bcfrw->bofrw",
                weight[row_step * 3 + col_step],
                window,
                preferred_element_type=jnp.float32,
            )
            result = term if result is None else result + term
    return result


def conv_lifted(inputs, weight):
    row_count, col_count = inputs.shape[2], inputs.shape[3]
    padded = jnp.pad(inputs, ((0, 0), (0, 0), (1, 1), (1, 1)))
    windows = jnp.concatenate(
        [padded[:, :, tap // 3 : tap // 3 + row_count, tap % 3 : tap % 3 + col_count] for tap in range(9)],
        axis=0,
    )
    stacked = weight.transpose(1, 0, 2).reshape(weight.shape[1], -1)
    result = lax.dot_general(windows, stacked, (((0,), (1,)), ((), ())), preferred_element_type=jnp.float32)
    return result.transpose(1, 0, 2, 3)


def conv_time(inputs, weight):
    padded = jnp.pad(inputs, ((0, 0), (0, 0), (1, 1), (0, 0), (0, 0)))
    frame_count = inputs.shape[2]
    result = None
    for tap_index in range(3):
        window = padded[:, :, tap_index : tap_index + frame_count]
        term = jnp.einsum(
            "oc,bcfrw->bofrw", weight[tap_index], window, preferred_element_type=jnp.float32
        )
        result = term if result is None else result + term
    return result


def unet_body(
    first_ref, emb_u_ref, time_ref, pooled_ref, tproj_ref, wl_ref, same_ref, batch_ref,
    wsp_hbm, wt_hbm, out_ref, wsp_ref, wt_ref, sems, *, count
):
    rows, frames, cols, chans = first_ref.shape
    blocks = 2 * frames
    copy_sp = pltpu.make_async_copy(wsp_hbm, wsp_ref, sems.at[0])
    copy_sp.start()
    copy_tm = pltpu.make_async_copy(wt_hbm, wt_ref, sems.at[1])
    copy_tm.start()
    same = same_ref[...]
    batch_mix = batch_ref[...]
    hi = lax.Precision.HIGHEST

    pooled = pooled_ref[...] / count
    average = jnp.mean(pooled, axis=1, keepdims=True)
    spread = jnp.mean((pooled - average) ** 2, axis=1, keepdims=True)
    text = ((pooled - average) * lax.rsqrt(spread + NORM_EPS)).astype(jnp.bfloat16)
    text = jnp.broadcast_to(text, (8, text.shape[1]))
    vector = jnp.dot(text, tproj_ref[...], preferred_element_type=jnp.float32)[0:1]
    emb_c = (vector + time_ref[...]).reshape(1, 1, 1, chans)
    emb_u = emb_u_ref[...].reshape(1, 1, 1, chans)
    first = first_ref[...]
    state = jnp.concatenate(
        [(first + emb_c).astype(jnp.bfloat16), (first + emb_u).astype(jnp.bfloat16)], axis=1
    )

    def group_stats(sums, count, mix):
        if mix is not None:
            sums = jnp.dot(mix, sums, precision=hi, preferred_element_type=jnp.float32)
        return jnp.dot(sums, same, precision=hi, preferred_element_type=jnp.float32) / count

    def norm_silu(x, mix, count):
        colsum = jnp.sum(x[0], axis=1) + jnp.sum(x[1], axis=1)
        mean = group_stats(colsum, count, mix)
        d = x - mean[None, :, None, :]
        sq = d * d
        var = group_stats(jnp.sum(sq[0], axis=1) + jnp.sum(sq[1], axis=1), count, mix)
        v = d * lax.rsqrt(var + NORM_EPS)[None, :, None, :]
        return (v * (0.5 + 0.5 * jnp.tanh(0.5 * v))).astype(jnp.bfloat16)

    def mm(a, w):
        return lax.dot_general(a, w, (((1,), (1,)), ((), ())), preferred_element_type=jnp.float32)

    col = lax.broadcasted_iota(jnp.int32, (blocks, cols, chans), 1)

    def conv_sp(n, section):
        x0 = n[0].reshape(blocks * cols, chans)
        x1 = n[1].reshape(blocks * cols, chans)
        outs = []
        for row in range(rows):
            own, other = (x0, x1) if row == 0 else (x1, x0)
            other_dr = 1 if row == 0 else -1
            acc = None
            for dc in (-1, 0, 1):
                y = mm(own, wsp_ref[section, 3 + dc + 1]) + mm(other, wsp_ref[section, (other_dr + 1) * 3 + dc + 1])
                y = y.reshape(blocks, cols, chans)
                if dc == -1:
                    y = jnp.where(col == 0, 0.0, pltpu.roll(y, 1, 1))
                elif dc == 1:
                    y = jnp.where(col == cols - 1, 0.0, pltpu.roll(y, cols - 1, 1))
                acc = y if acc is None else acc + y
            outs.append(acc)
        return jnp.stack(outs)

    def conv_tm(n, section):
        n5 = n.reshape(rows, 2, frames, cols, chans)
        blank = jnp.zeros((rows, 2, 1, cols, chans), n.dtype)
        before = jnp.concatenate([blank, n5[:, :, :-1]], axis=2)
        after = jnp.concatenate([n5[:, :, 1:], blank], axis=2)
        flat = rows * blocks * cols
        acc = mm(before.reshape(flat, chans), wt_ref[section, 0])
        acc = acc + mm(n.reshape(flat, chans), wt_ref[section, 1])
        acc = acc + mm(after.reshape(flat, chans), wt_ref[section, 2])
        return acc.reshape(rows, blocks, cols, chans)

    per_frame = float(chans // GROUPS * rows * cols)
    per_sample = per_frame * frames
    for section in range(wsp_ref.shape[0]):
        x = state.astype(jnp.float32)
        normed = norm_silu(x, None, per_frame)
        if section == 0:
            copy_sp.wait()
        state = (x + conv_sp(normed, section)).astype(jnp.bfloat16)
        x = state.astype(jnp.float32)
        normed = norm_silu(x, batch_mix, per_sample)
        if section == 0:
            copy_tm.wait()
        state = (x + conv_tm(normed, section)).astype(jnp.bfloat16)
    last = norm_silu(state.astype(jnp.float32), None, per_frame)
    x0 = last[0].reshape(blocks * cols, chans)
    x1 = last[1].reshape(blocks * cols, chans)
    stride = out_ref.shape[1]
    lane = lax.broadcasted_iota(jnp.int32, (stride, blocks * cols), 1) % cols

    def mm_t(w, a):
        return lax.dot_general(w, a, (((1,), (1,)), ((), ())), preferred_element_type=jnp.float32)

    for row in range(rows):
        own, other = (x0, x1) if row == 0 else (x1, x0)
        other_dr = 1 if row == 0 else -1
        y = mm_t(wl_ref[3 * stride : 6 * stride], own)
        y = y + mm_t(wl_ref[(other_dr + 1) * 3 * stride : (other_dr + 2) * 3 * stride], other)
        acc = None
        for dc in (-1, 0, 1):
            part = y[(dc + 1) * stride : (dc + 2) * stride]
            if dc == -1:
                part = jnp.where(lane == 0, 0.0, pltpu.roll(part, 1, 1))
            elif dc == 1:
                part = jnp.where(lane == cols - 1, 0.0, pltpu.roll(part, blocks * cols - 1, 1))
            acc = part if acc is None else acc + part
        out_ref[row] = acc


def unet(first, emb_u, time_vector, pooled, text_proj, spatial_weights, temporal_weights, conv_last, count):
    rows, frames, cols, chans = first.shape
    blocks = 2 * frames
    taps, outs, _ = conv_last.shape
    padded = -(-outs // 16) * 16
    last = jnp.concatenate([conv_last, jnp.zeros((taps, padded - outs, chans), conv_last.dtype)], axis=1)
    last = last.reshape(taps * padded, chans)
    group = jnp.arange(chans) // (chans // GROUPS)
    same = (group[:, None] == group[None, :]).astype(jnp.float32)
    block_of = jnp.arange(blocks) // frames
    batch_mix = (block_of[:, None] == block_of[None, :]).astype(jnp.float32)
    vmem = pl.BlockSpec(memory_space=pltpu.MemorySpace.VMEM)
    anywhere = pl.BlockSpec(memory_space=pl.ANY)
    return pl.pallas_call(
        functools.partial(unet_body, count=float(count)),
        out_shape=jax.ShapeDtypeStruct((rows, padded, blocks * cols), jnp.float32),
        in_specs=[vmem] * 8 + [anywhere, anywhere],
        out_specs=vmem,
        scratch_shapes=[
            pltpu.VMEM(spatial_weights.shape, spatial_weights.dtype),
            pltpu.VMEM(temporal_weights.shape, temporal_weights.dtype),
            pltpu.SemaphoreType.DMA((2,)),
        ],
        compiler_params=pltpu.CompilerParams(vmem_limit_bytes=100 * 1024 * 1024 // 2),
        cost_estimate=pl.CostEstimate(
            flops=2 * rows * blocks * cols * chans * chans * 9 * spatial_weights.shape[0],
            transcendentals=rows * blocks * cols * chans * 5,
            bytes_accessed=spatial_weights.size * 2 + temporal_weights.size * 2 + first.size * 4,
        ),
    )(first, emb_u, time_vector, pooled, text_proj, last, same, batch_mix, spatial_weights, temporal_weights)[:, :outs]


def gather_body(starts_ref, pick_ref, table_hbm, out_ref, buf, sems):
    count = starts_ref.shape[0]
    span = buf.shape[1]

    def start(t, carry):
        first = pl.multiple_of(starts_ref[t], span)
        pltpu.make_async_copy(table_hbm.at[pl.ds(first, span)], buf.at[t], sems.at[t]).start()
        return carry

    def finish(t, carry):
        pltpu.make_async_copy(table_hbm.at[pl.ds(0, span)], buf.at[t], sems.at[t]).wait()
        return carry

    lax.fori_loop(0, count, start, 0)
    lax.fori_loop(0, count, finish, 0)
    rows = jnp.where(pick_ref[...] > 0.0, buf[...].astype(jnp.float32), 0.0)
    out_ref[...] = jnp.sum(jnp.sum(rows, axis=0), axis=0, keepdims=True)


def pool_rows(local_ids, table):
    span = 16
    count = local_ids.shape[0]
    shard_rows = table.shape[0]
    if shard_rows % span:
        hits = local_ids[:, None] == jnp.arange(shard_rows, dtype=jnp.int32)[None, :]
        counts = jnp.sum(hits.astype(jnp.float32), axis=0).astype(jnp.bfloat16)[None]
        return jnp.dot(counts, table, preferred_element_type=jnp.float32)[0]
    held = (local_ids >= 0) & (local_ids < shard_rows)
    row = jnp.clip(local_ids, 0, shard_rows - 1)
    starts = (row // span) * span
    pick = (jnp.arange(span)[None, :] == (row - starts)[:, None]) & held[:, None]
    padded = -(-count // 8) * 8
    pick = jnp.zeros((padded, span, 1), jnp.float32).at[:count, :, 0].set(pick.astype(jnp.float32))
    return pl.pallas_call(
        gather_body,
        out_shape=jax.ShapeDtypeStruct((1, table.shape[1]), jnp.float32),
        in_specs=[
            pl.BlockSpec(memory_space=pltpu.MemorySpace.SMEM),
            pl.BlockSpec(memory_space=pltpu.MemorySpace.VMEM),
            pl.BlockSpec(memory_space=pl.ANY),
        ],
        out_specs=pl.BlockSpec(memory_space=pltpu.MemorySpace.VMEM),
        scratch_shapes=[pltpu.VMEM((padded, span, table.shape[1]), table.dtype), pltpu.SemaphoreType.DMA((count,))],
    )(starts, pick, table)[0]


def butterfly_sum(x, axis):
    peers = lax.axis_size(axis)
    if peers & (peers - 1):
        return jnp.sum(lax.all_gather(x, axis), axis=0)
    k = 1
    while k < peers:
        x = x + lax.ppermute(x, axis, [(i, i ^ k) for i in range(peers)])
        k *= 2
    return x


def butterfly_scan(x, axis):
    peers, me = lax.axis_size(axis), lax.axis_index(axis)
    if peers & (peers - 1):
        everything = lax.all_gather(x, axis)
        lower = (jnp.arange(peers) < me).reshape((peers,) + (1,) * x.ndim)
        return jnp.sum(jnp.where(lower, everything, 0.0), axis=0), jnp.sum(everything, axis=0)
    total, before = x, jnp.zeros_like(x)
    k = 1
    while k < peers:
        got = lax.ppermute(total, axis, [(i, i ^ k) for i in range(peers)])
        before = jnp.where((me & k) != 0, before + got, before)
        total = total + got
        k *= 2
    return before, total


def local(
    timesteps,
    prompt_ids,
    start_latent,
    iterate,
    fresh_noise,
    token_table,
    empty_text,
    time_in,
    time_out,
    text_proj,
    conv_first,
    spatial_weights,
    temporal_weights,
    conv_last,
):
    shard_rows = token_table.shape[0]
    first_row = lax.axis_index("slot") * shard_rows
    local_ids = prompt_ids - first_row
    partial = pool_rows(local_ids, token_table)
    pooled = butterfly_sum(partial, "slot")[None]
    text_uncond = layer_norm(empty_text).astype(jnp.bfloat16)[None]
    vector_uncond = jnp.dot(text_uncond, text_proj, preferred_element_type=jnp.float32)
    half_width = time_in.shape[0] // 2
    frequency = jnp.exp(-jnp.log(10000.0) * jnp.arange(half_width, dtype=jnp.float32) / half_width)
    step_value = timesteps[0].astype(jnp.float32)
    angles = step_value * frequency
    feature = jnp.concatenate([jnp.cos(angles), jnp.sin(angles)]).astype(jnp.bfloat16)[None, :]
    hidden = jax.nn.silu(jnp.dot(feature, time_in, preferred_element_type=jnp.float32)).astype(
        jnp.bfloat16
    )
    time_vector = jnp.dot(hidden, time_out, preferred_element_type=jnp.float32)
    latent = iterate[0]
    first = conv_lifted(latent.astype(jnp.bfloat16), conv_first)
    rows, frames, cols, chans = first.shape
    predicted = unet(
        first, vector_uncond + time_vector, time_vector, pooled, text_proj,
        spatial_weights, temporal_weights, conv_last, prompt_ids.shape[0],
    )
    predicted = predicted.reshape(rows, -1, 2, frames, cols).transpose(2, 1, 3, 0, 4)
    guided = predicted[1] + GUIDANCE_SCALE * (predicted[0] - predicted[1])
    alpha_now = alpha_bar(step_value)
    alpha_prev = alpha_bar(step_value - DT)
    scale_ratio = jnp.sqrt(alpha_prev / alpha_now)
    noise_square = (1.0 - alpha_prev) * (1.0 - alpha_now / alpha_prev) / (1.0 - alpha_now)
    kept_square = (1.0 - alpha_prev) * (alpha_now / alpha_prev - alpha_now) / (1.0 - alpha_now)
    eps_factor = jnp.sqrt(kept_square) - scale_ratio * jnp.sqrt(1.0 - alpha_now)
    drift_term = (
        (scale_ratio - 1.0) * latent + eps_factor * guided + jnp.sqrt(noise_square) * fresh_noise[0]
    )[None]
    earlier, total_drift = butterfly_scan(drift_term[0], "slot")
    new_iterate = start_latent[None] + earlier[None]
    final_latent = start_latent + total_drift
    return (new_iterate, final_latent)


def solution(mesh):
    placed = (
        P(("groups", "slot")),
        P("groups"),
        P("groups", None, None, None),
        P(("groups", "slot"), None, None, None, None),
        P(("groups", "slot"), None, None, None, None),
        P("slot", None),
        P(),
        P(),
        P(),
        P(),
        P(),
        P(),
        P(),
        P(),
    )
    return jax.shard_map(
        local,
        mesh=mesh,
        in_specs=placed,
        out_specs=(P(("groups", "slot"), None, None, None, None), P("groups", None, None, None)),
        check_vma=False,
    )
```

```python
import functools

import jax
import jax.numpy as jnp
from jax import lax
from jax.sharding import PartitionSpec as P
from jax.experimental import pallas as pl
from jax.experimental.pallas import tpu as pltpu

GROUPS = 32
DT = 50


NORM_EPS = 1e-05
GUIDANCE_SCALE = 5.0


def alpha_bar(step_value):
    phase_angle = (step_value / 1000.0 + 0.008) / 1.008 * (jnp.pi / 2.0)
    cosine = jnp.cos(phase_angle)
    return cosine * cosine


def layer_norm(values):
    average = jnp.mean(values)
    spread = jnp.mean((values - average) ** 2)
    return (values - average) * lax.rsqrt(spread + NORM_EPS)


def group_norm(values, axes):
    batch, channels = (values.shape[0], values.shape[1])
    shaped = values.reshape((batch, GROUPS, channels // GROUPS) + values.shape[2:])
    average = jnp.mean(shaped, axis=axes, keepdims=True)
    spread = jnp.mean((shaped - average) ** 2, axis=axes, keepdims=True)
    return ((shaped - average) * lax.rsqrt(spread + NORM_EPS)).reshape(values.shape)


def shift_columns(inputs, offset):
    if offset == 0:
        return inputs
    blank = jnp.zeros(inputs.shape[:-1] + (1,), inputs.dtype)
    if offset == 1:
        return jnp.concatenate([inputs[..., 1:], blank], axis=-1)
    return jnp.concatenate([blank, inputs[..., :-1]], axis=-1)


def conv_space(inputs, weight):
    row_count = inputs.shape[3]
    result = None
    for col_step in range(3):
        moved = shift_columns(inputs, col_step - 1)
        padded = jnp.pad(moved, ((0, 0), (0, 0), (0, 0), (1, 1), (0, 0)))
        for row_step in range(3):
            window = padded[:, :, :, row_step : row_step + row_count]
            term = jnp.einsum(
                "oc,bcfrw->bofrw",
                weight[row_step * 3 + col_step],
                window,
                preferred_element_type=jnp.float32,
            )
            result = term if result is None else result + term
    return result


def conv_lifted(inputs, weight):
    row_count, col_count = inputs.shape[2], inputs.shape[3]
    padded = jnp.pad(inputs, ((0, 0), (0, 0), (1, 1), (1, 1)))
    windows = jnp.concatenate(
        [padded[:, :, tap // 3 : tap // 3 + row_count, tap % 3 : tap % 3 + col_count] for tap in range(9)],
        axis=0,
    )
    stacked = weight.transpose(1, 0, 2).reshape(weight.shape[1], -1)
    result = lax.dot_general(windows, stacked, (((0,), (1,)), ((), ())), preferred_element_type=jnp.float32)
    return result.transpose(1, 0, 2, 3)


def conv_time(inputs, weight):
    padded = jnp.pad(inputs, ((0, 0), (0, 0), (1, 1), (0, 0), (0, 0)))
    frame_count = inputs.shape[2]
    result = None
    for tap_index in range(3):
        window = padded[:, :, tap_index : tap_index + frame_count]
        term = jnp.einsum(
            "oc,bcfrw->bofrw", weight[tap_index], window, preferred_element_type=jnp.float32
        )
        result = term if result is None else result + term
    return result


def unet_body(
    first_ref, emb_u_ref, time_ref, pooled_ref, tproj_ref, wl_ref, same_ref, batch_ref,
    wsp_hbm, wt_hbm, out_ref, wsp_ref, wt_ref, sems, *, count
):
    rows, frames, cols, chans = first_ref.shape
    blocks = 2 * frames
    copy_sp = pltpu.make_async_copy(wsp_hbm, wsp_ref, sems.at[0])
    copy_sp.start()
    copy_tm = pltpu.make_async_copy(wt_hbm, wt_ref, sems.at[1])
    copy_tm.start()
    same = same_ref[...]
    batch_mix = batch_ref[...]
    hi = lax.Precision.HIGHEST

    pooled = pooled_ref[...] / count
    average = jnp.mean(pooled, axis=1, keepdims=True)
    spread = jnp.mean((pooled - average) ** 2, axis=1, keepdims=True)
    text = ((pooled - average) * lax.rsqrt(spread + NORM_EPS)).astype(jnp.bfloat16)
    text = jnp.broadcast_to(text, (8, text.shape[1]))
    vector = jnp.dot(text, tproj_ref[...], preferred_element_type=jnp.float32)[0:1]
    emb_c = (vector + time_ref[...]).reshape(1, 1, 1, chans)
    emb_u = emb_u_ref[...].reshape(1, 1, 1, chans)
    first = first_ref[...]
    state = jnp.concatenate(
        [(first + emb_c).astype(jnp.bfloat16), (first + emb_u).astype(jnp.bfloat16)], axis=1
    )

    def group_stats(sums, count, mix):
        if mix is not None:
            sums = jnp.dot(mix, sums, precision=hi, preferred_element_type=jnp.float32)
        return jnp.dot(sums, same, precision=hi, preferred_element_type=jnp.float32) / count

    def norm_silu(x, mix, count):
        colsum = jnp.sum(x[0], axis=1) + jnp.sum(x[1], axis=1)
        mean = group_stats(colsum, count, mix)
        d = x - mean[None, :, None, :]
        sq = d * d
        var = group_stats(jnp.sum(sq[0], axis=1) + jnp.sum(sq[1], axis=1), count, mix)
        v = d * lax.rsqrt(var + NORM_EPS)[None, :, None, :]
        return (v * (0.5 + 0.5 * jnp.tanh(0.5 * v))).astype(jnp.bfloat16)

    def mm(a, w):
        return jnp.dot(a, w, preferred_element_type=jnp.float32)

    col = lax.broadcasted_iota(jnp.int32, (blocks, cols, chans), 1)

    def conv_sp(n, section):
        x0 = n[0].reshape(blocks * cols, chans)
        x1 = n[1].reshape(blocks * cols, chans)
        outs = []
        for row in range(rows):
            own, other = (x0, x1) if row == 0 else (x1, x0)
            other_dr = 1 if row == 0 else -1
            acc = None
            for dc in (-1, 0, 1):
                y = mm(own, wsp_ref[section, 3 + dc + 1]) + mm(other, wsp_ref[section, (other_dr + 1) * 3 + dc + 1])
                y = y.reshape(blocks, cols, chans)
                if dc == -1:
                    y = jnp.where(col == 0, 0.0, pltpu.roll(y, 1, 1))
                elif dc == 1:
                    y = jnp.where(col == cols - 1, 0.0, pltpu.roll(y, cols - 1, 1))
                acc = y if acc is None else acc + y
            outs.append(acc)
        return jnp.stack(outs)

    def conv_tm(n, section):
        n5 = n.reshape(rows, 2, frames, cols, chans)
        blank = jnp.zeros((rows, 2, 1, cols, chans), n.dtype)
        before = jnp.concatenate([blank, n5[:, :, :-1]], axis=2)
        after = jnp.concatenate([n5[:, :, 1:], blank], axis=2)
        flat = rows * blocks * cols
        acc = mm(before.reshape(flat, chans), wt_ref[section, 0])
        acc = acc + mm(n.reshape(flat, chans), wt_ref[section, 1])
        acc = acc + mm(after.reshape(flat, chans), wt_ref[section, 2])
        return acc.reshape(rows, blocks, cols, chans)

    per_frame = float(chans // GROUPS * rows * cols)
    per_sample = per_frame * frames
    for section in range(wsp_ref.shape[0]):
        x = state.astype(jnp.float32)
        normed = norm_silu(x, None, per_frame)
        if section == 0:
            copy_sp.wait()
        state = (x + conv_sp(normed, section)).astype(jnp.bfloat16)
        x = state.astype(jnp.float32)
        normed = norm_silu(x, batch_mix, per_sample)
        if section == 0:
            copy_tm.wait()
        state = (x + conv_tm(normed, section)).astype(jnp.bfloat16)
    last = norm_silu(state.astype(jnp.float32), None, per_frame)
    x0 = last[0].reshape(blocks * cols, chans)
    x1 = last[1].reshape(blocks * cols, chans)
    stride = out_ref.shape[1]
    lane = lax.broadcasted_iota(jnp.int32, (stride, blocks * cols), 1) % cols

    def mm_t(w, a):
        return lax.dot_general(w, a, (((1,), (1,)), ((), ())), preferred_element_type=jnp.float32)

    for row in range(rows):
        own, other = (x0, x1) if row == 0 else (x1, x0)
        other_dr = 1 if row == 0 else -1
        y = mm_t(wl_ref[3 * stride : 6 * stride], own)
        y = y + mm_t(wl_ref[(other_dr + 1) * 3 * stride : (other_dr + 2) * 3 * stride], other)
        acc = None
        for dc in (-1, 0, 1):
            part = y[(dc + 1) * stride : (dc + 2) * stride]
            if dc == -1:
                part = jnp.where(lane == 0, 0.0, pltpu.roll(part, 1, 1))
            elif dc == 1:
                part = jnp.where(lane == cols - 1, 0.0, pltpu.roll(part, blocks * cols - 1, 1))
            acc = part if acc is None else acc + part
        out_ref[row] = acc


def unet(first, emb_u, time_vector, pooled, text_proj, spatial_weights, temporal_weights, conv_last, count):
    rows, frames, cols, chans = first.shape
    blocks = 2 * frames
    taps, outs, _ = conv_last.shape
    padded = -(-outs // 16) * 16
    last = jnp.concatenate([conv_last, jnp.zeros((taps, padded - outs, chans), conv_last.dtype)], axis=1)
    last = last.reshape(taps * padded, chans)
    group = jnp.arange(chans) // (chans // GROUPS)
    same = (group[:, None] == group[None, :]).astype(jnp.float32)
    block_of = jnp.arange(blocks) // frames
    batch_mix = (block_of[:, None] == block_of[None, :]).astype(jnp.float32)
    vmem = pl.BlockSpec(memory_space=pltpu.MemorySpace.VMEM)
    anywhere = pl.BlockSpec(memory_space=pl.ANY)
    return pl.pallas_call(
        functools.partial(unet_body, count=float(count)),
        out_shape=jax.ShapeDtypeStruct((rows, padded, blocks * cols), jnp.float32),
        in_specs=[vmem] * 8 + [anywhere, anywhere],
        out_specs=vmem,
        scratch_shapes=[
            pltpu.VMEM(spatial_weights.shape, spatial_weights.dtype),
            pltpu.VMEM(temporal_weights.shape, temporal_weights.dtype),
            pltpu.SemaphoreType.DMA((2,)),
        ],
        compiler_params=pltpu.CompilerParams(vmem_limit_bytes=100 * 1024 * 1024 // 2),
        cost_estimate=pl.CostEstimate(
            flops=2 * rows * blocks * cols * chans * chans * 9 * spatial_weights.shape[0],
            transcendentals=rows * blocks * cols * chans * 5,
            bytes_accessed=spatial_weights.size * 2 + temporal_weights.size * 2 + first.size * 4,
        ),
    )(first, emb_u, time_vector, pooled, text_proj, last, same, batch_mix, spatial_weights.swapaxes(2, 3), temporal_weights.swapaxes(2, 3))[:, :outs]


def butterfly_sum(x, axis):
    peers = lax.axis_size(axis)
    if peers & (peers - 1):
        return jnp.sum(lax.all_gather(x, axis), axis=0)
    k = 1
    while k < peers:
        x = x + lax.ppermute(x, axis, [(i, i ^ k) for i in range(peers)])
        k *= 2
    return x


def butterfly_scan(x, axis):
    peers, me = lax.axis_size(axis), lax.axis_index(axis)
    if peers & (peers - 1):
        everything = lax.all_gather(x, axis)
        lower = (jnp.arange(peers) < me).reshape((peers,) + (1,) * x.ndim)
        return jnp.sum(jnp.where(lower, everything, 0.0), axis=0), jnp.sum(everything, axis=0)
    total, before = x, jnp.zeros_like(x)
    k = 1
    while k < peers:
        got = lax.ppermute(total, axis, [(i, i ^ k) for i in range(peers)])
        before = jnp.where((me & k) != 0, before + got, before)
        total = total + got
        k *= 2
    return before, total


def local(
    timesteps,
    prompt_ids,
    start_latent,
    iterate,
    fresh_noise,
    token_table,
    empty_text,
    time_in,
    time_out,
    text_proj,
    conv_first,
    spatial_weights,
    temporal_weights,
    conv_last,
):
    shard_rows = token_table.shape[0]
    first_row = lax.axis_index("slot") * shard_rows
    local_ids = prompt_ids - first_row
    hits = local_ids[:, None] == jnp.arange(shard_rows, dtype=jnp.int32)[None, :]
    counts = jnp.sum(hits.astype(jnp.float32), axis=0).astype(jnp.bfloat16)[None]
    partial = jnp.dot(counts, token_table, preferred_element_type=jnp.float32)[0]
    pooled = butterfly_sum(partial, "slot")[None]
    text_uncond = layer_norm(empty_text).astype(jnp.bfloat16)[None]
    vector_uncond = jnp.dot(text_uncond, text_proj, preferred_element_type=jnp.float32)
    half_width = time_in.shape[0] // 2
    frequency = jnp.exp(-jnp.log(10000.0) * jnp.arange(half_width, dtype=jnp.float32) / half_width)
    step_value = timesteps[0].astype(jnp.float32)
    angles = step_value * frequency
    feature = jnp.concatenate([jnp.cos(angles), jnp.sin(angles)]).astype(jnp.bfloat16)[None, :]
    hidden = jax.nn.silu(jnp.dot(feature, time_in, preferred_element_type=jnp.float32)).astype(
        jnp.bfloat16
    )
    time_vector = jnp.dot(hidden, time_out, preferred_element_type=jnp.float32)
    latent = iterate[0]
    first = conv_lifted(latent.astype(jnp.bfloat16), conv_first)
    rows, frames, cols, chans = first.shape
    predicted = unet(
        first, vector_uncond + time_vector, time_vector, pooled, text_proj,
        spatial_weights, temporal_weights, conv_last, prompt_ids.shape[0],
    )
    predicted = predicted.reshape(rows, -1, 2, frames, cols).transpose(2, 1, 3, 0, 4)
    guided = predicted[1] + GUIDANCE_SCALE * (predicted[0] - predicted[1])
    alpha_now = alpha_bar(step_value)
    alpha_prev = alpha_bar(step_value - DT)
    scale_ratio = jnp.sqrt(alpha_prev / alpha_now)
    noise_square = (1.0 - alpha_prev) * (1.0 - alpha_now / alpha_prev) / (1.0 - alpha_now)
    kept_square = (1.0 - alpha_prev) * (alpha_now / alpha_prev - alpha_now) / (1.0 - alpha_now)
    eps_factor = jnp.sqrt(kept_square) - scale_ratio * jnp.sqrt(1.0 - alpha_now)
    drift_term = (
        (scale_ratio - 1.0) * latent + eps_factor * guided + jnp.sqrt(noise_square) * fresh_noise[0]
    )[None]
    earlier, total_drift = butterfly_scan(drift_term[0], "slot")
    new_iterate = start_latent[None] + earlier[None]
    final_latent = start_latent + total_drift
    return (new_iterate, final_latent)


def solution(mesh):
    placed = (
        P(("groups", "slot")),
        P("groups"),
        P("groups", None, None, None),
        P(("groups", "slot"), None, None, None, None),
        P(("groups", "slot"), None, None, None, None),
        P("slot", None),
        P(),
        P(),
        P(),
        P(),
        P(),
        P(),
        P(),
        P(),
    )
    return jax.shard_map(
        local,
        mesh=mesh,
        in_specs=placed,
        out_specs=(P(("groups", "slot"), None, None, None, None), P("groups", None, None, None)),
        check_vma=False,
    )
```

```python
import functools

import jax
import jax.numpy as jnp
from jax import lax
from jax.sharding import PartitionSpec as P
from jax.experimental import pallas as pl
from jax.experimental.pallas import tpu as pltpu

GROUPS = 32
DT = 50


NORM_EPS = 1e-05
GUIDANCE_SCALE = 5.0


def alpha_bar(step_value):
    phase_angle = (step_value / 1000.0 + 0.008) / 1.008 * (jnp.pi / 2.0)
    cosine = jnp.cos(phase_angle)
    return cosine * cosine


def layer_norm(values):
    average = jnp.mean(values)
    spread = jnp.mean((values - average) ** 2)
    return (values - average) * lax.rsqrt(spread + NORM_EPS)


def group_norm(values, axes):
    batch, channels = (values.shape[0], values.shape[1])
    shaped = values.reshape((batch, GROUPS, channels // GROUPS) + values.shape[2:])
    average = jnp.mean(shaped, axis=axes, keepdims=True)
    spread = jnp.mean((shaped - average) ** 2, axis=axes, keepdims=True)
    return ((shaped - average) * lax.rsqrt(spread + NORM_EPS)).reshape(values.shape)


def shift_columns(inputs, offset):
    if offset == 0:
        return inputs
    blank = jnp.zeros(inputs.shape[:-1] + (1,), inputs.dtype)
    if offset == 1:
        return jnp.concatenate([inputs[..., 1:], blank], axis=-1)
    return jnp.concatenate([blank, inputs[..., :-1]], axis=-1)


def conv_space(inputs, weight):
    row_count = inputs.shape[3]
    result = None
    for col_step in range(3):
        moved = shift_columns(inputs, col_step - 1)
        padded = jnp.pad(moved, ((0, 0), (0, 0), (0, 0), (1, 1), (0, 0)))
        for row_step in range(3):
            window = padded[:, :, :, row_step : row_step + row_count]
            term = jnp.einsum(
                "oc,bcfrw->bofrw",
                weight[row_step * 3 + col_step],
                window,
                preferred_element_type=jnp.float32,
            )
            result = term if result is None else result + term
    return result


def conv_lifted(inputs, weight):
    row_count, col_count = inputs.shape[2], inputs.shape[3]
    padded = jnp.pad(inputs, ((0, 0), (0, 0), (1, 1), (1, 1)))
    windows = jnp.concatenate(
        [padded[:, :, tap // 3 : tap // 3 + row_count, tap % 3 : tap % 3 + col_count] for tap in range(9)],
        axis=0,
    )
    stacked = weight.transpose(1, 0, 2).reshape(weight.shape[1], -1)
    result = lax.dot_general(windows, stacked, (((0,), (1,)), ((), ())), preferred_element_type=jnp.float32)
    return result.transpose(1, 0, 2, 3)


def conv_time(inputs, weight):
    padded = jnp.pad(inputs, ((0, 0), (0, 0), (1, 1), (0, 0), (0, 0)))
    frame_count = inputs.shape[2]
    result = None
    for tap_index in range(3):
        window = padded[:, :, tap_index : tap_index + frame_count]
        term = jnp.einsum(
            "oc,bcfrw->bofrw", weight[tap_index], window, preferred_element_type=jnp.float32
        )
        result = term if result is None else result + term
    return result


def unet_body(
    first_ref, emb_u_ref, time_ref, pooled_ref, tproj_ref, wl_ref, same_ref, batch_ref,
    wsp_hbm, wt_hbm, out_ref, wsp_ref, wt_ref, sems, *, count
):
    rows, frames, cols, chans = first_ref.shape
    blocks = 2 * frames
    copy_sp = pltpu.make_async_copy(wsp_hbm, wsp_ref, sems.at[0])
    copy_sp.start()
    copy_tm = pltpu.make_async_copy(wt_hbm, wt_ref, sems.at[1])
    copy_tm.start()
    same = same_ref[...]
    batch_mix = batch_ref[...]
    hi = lax.Precision.HIGHEST

    pooled = pooled_ref[...] / count
    average = jnp.mean(pooled, axis=1, keepdims=True)
    spread = jnp.mean((pooled - average) ** 2, axis=1, keepdims=True)
    text = ((pooled - average) * lax.rsqrt(spread + NORM_EPS)).astype(jnp.bfloat16)
    text = jnp.broadcast_to(text, (8, text.shape[1]))
    vector = jnp.dot(text, tproj_ref[...], preferred_element_type=jnp.float32)[0:1]
    emb_c = (vector + time_ref[...]).reshape(1, 1, 1, chans)
    emb_u = emb_u_ref[...].reshape(1, 1, 1, chans)
    first = first_ref[...]
    state = jnp.concatenate(
        [(first + emb_c).astype(jnp.bfloat16), (first + emb_u).astype(jnp.bfloat16)], axis=1
    )

    def group_stats(sums, count, mix):
        if mix is not None:
            sums = jnp.dot(mix, sums, precision=hi, preferred_element_type=jnp.float32)
        return jnp.dot(sums, same, precision=hi, preferred_element_type=jnp.float32) / count

    def norm_silu(x, mix, count):
        colsum = jnp.sum(x[0], axis=1) + jnp.sum(x[1], axis=1)
        mean = group_stats(colsum, count, mix)
        d = x - mean[None, :, None, :]
        sq = d * d
        var = group_stats(jnp.sum(sq[0], axis=1) + jnp.sum(sq[1], axis=1), count, mix)
        v = d * lax.rsqrt(var + NORM_EPS)[None, :, None, :]
        return (v * (0.5 + 0.5 * jnp.tanh(0.5 * v))).astype(jnp.bfloat16)

    def mm(a, w):
        return lax.dot_general(a, w, (((1,), (1,)), ((), ())), preferred_element_type=jnp.float32)

    col = lax.broadcasted_iota(jnp.int32, (blocks, cols, chans), 1)

    def conv_sp(n, section):
        x0 = n[0].reshape(blocks * cols, chans)
        x1 = n[1].reshape(blocks * cols, chans)
        outs = []
        for row in range(rows):
            own, other = (x0, x1) if row == 0 else (x1, x0)
            other_dr = 1 if row == 0 else -1
            acc = None
            for dc in (-1, 0, 1):
                y = mm(own, wsp_ref[section, 3 + dc + 1]) + mm(other, wsp_ref[section, (other_dr + 1) * 3 + dc + 1])
                y = y.reshape(blocks, cols, chans)
                if dc == -1:
                    y = jnp.where(col == 0, 0.0, pltpu.roll(y, 1, 1))
                elif dc == 1:
                    y = jnp.where(col == cols - 1, 0.0, pltpu.roll(y, cols - 1, 1))
                acc = y if acc is None else acc + y
            outs.append(acc)
        return jnp.stack(outs)

    def conv_tm(n, section):
        n5 = n.reshape(rows, 2, frames, cols, chans)
        blank = jnp.zeros((rows, 2, 1, cols, chans), n.dtype)
        before = jnp.concatenate([blank, n5[:, :, :-1]], axis=2)
        after = jnp.concatenate([n5[:, :, 1:], blank], axis=2)
        flat = rows * blocks * cols
        acc = mm(before.reshape(flat, chans), wt_ref[section, 0])
        acc = acc + mm(n.reshape(flat, chans), wt_ref[section, 1])
        acc = acc + mm(after.reshape(flat, chans), wt_ref[section, 2])
        return acc.reshape(rows, blocks, cols, chans)

    per_frame = float(chans // GROUPS * rows * cols)
    per_sample = per_frame * frames
    for section in range(wsp_ref.shape[0]):
        x = state.astype(jnp.float32)
        normed = norm_silu(x, None, per_frame)
        if section == 0:
            copy_sp.wait()
        state = (x + conv_sp(normed, section)).astype(jnp.bfloat16)
        x = state.astype(jnp.float32)
        normed = norm_silu(x, batch_mix, per_sample)
        if section == 0:
            copy_tm.wait()
        state = (x + conv_tm(normed, section)).astype(jnp.bfloat16)
    last = norm_silu(state.astype(jnp.float32), None, per_frame)
    x0 = last[0].reshape(blocks * cols, chans)
    x1 = last[1].reshape(blocks * cols, chans)
    stride = out_ref.shape[1]
    lane = lax.broadcasted_iota(jnp.int32, (stride, blocks * cols), 1) % cols

    def mm_t(w, a):
        return lax.dot_general(w, a, (((1,), (1,)), ((), ())), preferred_element_type=jnp.float32)

    for row in range(rows):
        own, other = (x0, x1) if row == 0 else (x1, x0)
        other_dr = 1 if row == 0 else -1
        y = mm_t(wl_ref[3 * stride : 6 * stride], own)
        y = y + mm_t(wl_ref[(other_dr + 1) * 3 * stride : (other_dr + 2) * 3 * stride], other)
        acc = None
        for dc in (-1, 0, 1):
            part = y[(dc + 1) * stride : (dc + 2) * stride]
            if dc == -1:
                part = jnp.where(lane == 0, 0.0, pltpu.roll(part, 1, 1))
            elif dc == 1:
                part = jnp.where(lane == cols - 1, 0.0, pltpu.roll(part, blocks * cols - 1, 1))
            acc = part if acc is None else acc + part
        out_ref[row] = acc


def unet(first, emb_u, time_vector, pooled, text_proj, spatial_weights, temporal_weights, conv_last, count):
    rows, frames, cols, chans = first.shape
    blocks = 2 * frames
    taps, outs, _ = conv_last.shape
    padded = -(-outs // 16) * 16
    last = jnp.concatenate([conv_last, jnp.zeros((taps, padded - outs, chans), conv_last.dtype)], axis=1)
    last = last.reshape(taps * padded, chans)
    group = jnp.arange(chans) // (chans // GROUPS)
    same = (group[:, None] == group[None, :]).astype(jnp.float32)
    block_of = jnp.arange(blocks) // frames
    batch_mix = (block_of[:, None] == block_of[None, :]).astype(jnp.float32)
    vmem = pl.BlockSpec(memory_space=pltpu.MemorySpace.VMEM)
    anywhere = pl.BlockSpec(memory_space=pl.ANY)
    return pl.pallas_call(
        functools.partial(unet_body, count=float(count)),
        out_shape=jax.ShapeDtypeStruct((rows, padded, blocks * cols), jnp.float32),
        in_specs=[vmem] * 8 + [anywhere, anywhere],
        out_specs=vmem,
        scratch_shapes=[
            pltpu.VMEM(spatial_weights.shape, spatial_weights.dtype),
            pltpu.VMEM(temporal_weights.shape, temporal_weights.dtype),
            pltpu.SemaphoreType.DMA((2,)),
        ],
        compiler_params=pltpu.CompilerParams(vmem_limit_bytes=100 * 1024 * 1024 // 2),
        cost_estimate=pl.CostEstimate(
            flops=2 * rows * blocks * cols * chans * chans * 9 * spatial_weights.shape[0],
            transcendentals=rows * blocks * cols * chans * 5,
            bytes_accessed=spatial_weights.size * 2 + temporal_weights.size * 2 + first.size * 4,
        ),
    )(first, emb_u, time_vector, pooled, text_proj, last, same, batch_mix, spatial_weights, temporal_weights)[:, :outs]


def butterfly_sum(x, axis):
    peers = lax.axis_size(axis)
    if peers & (peers - 1):
        return jnp.sum(lax.all_gather(x, axis), axis=0)
    k = 1
    while k < peers:
        x = x + lax.ppermute(x, axis, [(i, i ^ k) for i in range(peers)])
        k *= 2
    return x


def butterfly_scan(x, axis):
    peers, me = lax.axis_size(axis), lax.axis_index(axis)
    if peers & (peers - 1):
        everything = lax.all_gather(x, axis)
        lower = (jnp.arange(peers) < me).reshape((peers,) + (1,) * x.ndim)
        return jnp.sum(jnp.where(lower, everything, 0.0), axis=0), jnp.sum(everything, axis=0)
    total, before = x, jnp.zeros_like(x)
    k = 1
    while k < peers:
        got = lax.ppermute(total, axis, [(i, i ^ k) for i in range(peers)])
        before = jnp.where((me & k) != 0, before + got, before)
        total = total + got
        k *= 2
    return before, total


def local(
    timesteps,
    prompt_ids,
    start_latent,
    iterate,
    fresh_noise,
    token_table,
    empty_text,
    time_in,
    time_out,
    text_proj,
    conv_first,
    spatial_weights,
    temporal_weights,
    conv_last,
):
    shard_rows = token_table.shape[0]
    first_row = lax.axis_index("slot") * shard_rows
    local_ids = prompt_ids - first_row
    hits = local_ids[:, None] == jnp.arange(shard_rows, dtype=jnp.int32)[None, :]
    counts = jnp.sum(hits.astype(jnp.float32), axis=0)
    partial = jnp.sum(token_table.astype(jnp.float32) * counts[:, None], axis=0)
    pooled = butterfly_sum(partial, "slot")[None]
    text_uncond = layer_norm(empty_text).astype(jnp.bfloat16)[None]
    vector_uncond = jnp.dot(text_uncond, text_proj, preferred_element_type=jnp.float32)
    half_width = time_in.shape[0] // 2
    frequency = jnp.exp(-jnp.log(10000.0) * jnp.arange(half_width, dtype=jnp.float32) / half_width)
    step_value = timesteps[0].astype(jnp.float32)
    angles = step_value * frequency
    feature = jnp.concatenate([jnp.cos(angles), jnp.sin(angles)]).astype(jnp.bfloat16)[None, :]
    hidden = jax.nn.silu(jnp.dot(feature, time_in, preferred_element_type=jnp.float32)).astype(
        jnp.bfloat16
    )
    time_vector = jnp.dot(hidden, time_out, preferred_element_type=jnp.float32)
    latent = iterate[0]
    first = conv_lifted(latent.astype(jnp.bfloat16), conv_first)
    rows, frames, cols, chans = first.shape
    predicted = unet(
        first, vector_uncond + time_vector, time_vector, pooled, text_proj,
        spatial_weights, temporal_weights, conv_last, prompt_ids.shape[0],
    )
    predicted = predicted.reshape(rows, -1, 2, frames, cols).transpose(2, 1, 3, 0, 4)
    guided = predicted[1] + GUIDANCE_SCALE * (predicted[0] - predicted[1])
    alpha_now = alpha_bar(step_value)
    alpha_prev = alpha_bar(step_value - DT)
    scale_ratio = jnp.sqrt(alpha_prev / alpha_now)
    noise_square = (1.0 - alpha_prev) * (1.0 - alpha_now / alpha_prev) / (1.0 - alpha_now)
    kept_square = (1.0 - alpha_prev) * (alpha_now / alpha_prev - alpha_now) / (1.0 - alpha_now)
    eps_factor = jnp.sqrt(kept_square) - scale_ratio * jnp.sqrt(1.0 - alpha_now)
    drift_term = (
        (scale_ratio - 1.0) * latent + eps_factor * guided + jnp.sqrt(noise_square) * fresh_noise[0]
    )[None]
    earlier, total_drift = butterfly_scan(drift_term[0], "slot")
    new_iterate = start_latent[None] + earlier[None]
    final_latent = start_latent + total_drift
    return (new_iterate, final_latent)


def solution(mesh):
    placed = (
        P(("groups", "slot")),
        P("groups"),
        P("groups", None, None, None),
        P(("groups", "slot"), None, None, None, None),
        P(("groups", "slot"), None, None, None, None),
        P("slot", None),
        P(),
        P(),
        P(),
        P(),
        P(),
        P(),
        P(),
        P(),
    )
    return jax.shard_map(
        local,
        mesh=mesh,
        in_specs=placed,
        out_specs=(P(("groups", "slot"), None, None, None, None), P("groups", None, None, None)),
        check_vma=False,
    )
```

```python
import functools

import jax
import jax.numpy as jnp
from jax import lax
from jax.sharding import PartitionSpec as P
from jax.experimental import pallas as pl
from jax.experimental.pallas import tpu as pltpu

GROUPS = 32
DT = 50


NORM_EPS = 1e-05
GUIDANCE_SCALE = 5.0


def alpha_bar(step_value):
    phase_angle = (step_value / 1000.0 + 0.008) / 1.008 * (jnp.pi / 2.0)
    cosine = jnp.cos(phase_angle)
    return cosine * cosine


def layer_norm(values):
    average = jnp.mean(values)
    spread = jnp.mean((values - average) ** 2)
    return (values - average) * lax.rsqrt(spread + NORM_EPS)


def group_norm(values, axes):
    batch, channels = (values.shape[0], values.shape[1])
    shaped = values.reshape((batch, GROUPS, channels // GROUPS) + values.shape[2:])
    average = jnp.mean(shaped, axis=axes, keepdims=True)
    spread = jnp.mean((shaped - average) ** 2, axis=axes, keepdims=True)
    return ((shaped - average) * lax.rsqrt(spread + NORM_EPS)).reshape(values.shape)


def shift_columns(inputs, offset):
    if offset == 0:
        return inputs
    blank = jnp.zeros(inputs.shape[:-1] + (1,), inputs.dtype)
    if offset == 1:
        return jnp.concatenate([inputs[..., 1:], blank], axis=-1)
    return jnp.concatenate([blank, inputs[..., :-1]], axis=-1)


def conv_space(inputs, weight):
    row_count = inputs.shape[3]
    result = None
    for col_step in range(3):
        moved = shift_columns(inputs, col_step - 1)
        padded = jnp.pad(moved, ((0, 0), (0, 0), (0, 0), (1, 1), (0, 0)))
        for row_step in range(3):
            window = padded[:, :, :, row_step : row_step + row_count]
            term = jnp.einsum(
                "oc,bcfrw->bofrw",
                weight[row_step * 3 + col_step],
                window,
                preferred_element_type=jnp.float32,
            )
            result = term if result is None else result + term
    return result


def conv_lifted(inputs, weight):
    row_count, col_count = inputs.shape[2], inputs.shape[3]
    padded = jnp.pad(inputs, ((0, 0), (0, 0), (1, 1), (1, 1)))
    windows = jnp.concatenate(
        [padded[:, :, tap // 3 : tap // 3 + row_count, tap % 3 : tap % 3 + col_count] for tap in range(9)],
        axis=0,
    )
    stacked = weight.transpose(1, 0, 2).reshape(weight.shape[1], -1)
    result = lax.dot_general(windows, stacked, (((0,), (1,)), ((), ())), preferred_element_type=jnp.float32)
    return result.transpose(1, 0, 2, 3)


def conv_time(inputs, weight):
    padded = jnp.pad(inputs, ((0, 0), (0, 0), (1, 1), (0, 0), (0, 0)))
    frame_count = inputs.shape[2]
    result = None
    for tap_index in range(3):
        window = padded[:, :, tap_index : tap_index + frame_count]
        term = jnp.einsum(
            "oc,bcfrw->bofrw", weight[tap_index], window, preferred_element_type=jnp.float32
        )
        result = term if result is None else result + term
    return result


def unet_body(
    first_ref, emb_u_ref, time_ref, pooled_ref, tproj_ref, wl_ref, same_ref, batch_ref,
    wsp_hbm, wt_hbm, out_ref, wsp_ref, wt_ref, sems, *, count
):
    rows, frames, cols, chans = first_ref.shape
    blocks = 2 * frames
    copy_sp = pltpu.make_async_copy(wsp_hbm, wsp_ref, sems.at[0])
    copy_sp.start()
    copy_tm = pltpu.make_async_copy(wt_hbm, wt_ref, sems.at[1])
    copy_tm.start()
    same = same_ref[...]
    batch_mix = batch_ref[...]
    hi = lax.Precision.HIGHEST

    pooled = pooled_ref[...] / count
    average = jnp.mean(pooled, axis=1, keepdims=True)
    spread = jnp.mean((pooled - average) ** 2, axis=1, keepdims=True)
    text = ((pooled - average) * lax.rsqrt(spread + NORM_EPS)).astype(jnp.bfloat16)
    text = jnp.broadcast_to(text, (8, text.shape[1]))
    vector = jnp.dot(text, tproj_ref[...], preferred_element_type=jnp.float32)[0:1]
    emb_c = (vector + time_ref[...]).reshape(1, 1, 1, chans)
    emb_u = emb_u_ref[...].reshape(1, 1, 1, chans)
    first = first_ref[...]
    state = jnp.concatenate(
        [(first + emb_c).astype(jnp.bfloat16), (first + emb_u).astype(jnp.bfloat16)], axis=1
    )

    def group_stats(sums, count, mix):
        if mix is not None:
            sums = jnp.dot(mix, sums, precision=hi, preferred_element_type=jnp.float32)
        return jnp.dot(sums, same, precision=hi, preferred_element_type=jnp.float32) / count

    def norm_silu(x, mix, count):
        colsum = jnp.sum(x[0], axis=1) + jnp.sum(x[1], axis=1)
        mean = group_stats(colsum, count, mix)
        d = x - mean[None, :, None, :]
        sq = d * d
        var = group_stats(jnp.sum(sq[0], axis=1) + jnp.sum(sq[1], axis=1), count, mix)
        v = d * lax.rsqrt(var + NORM_EPS)[None, :, None, :]
        return (v * (0.5 + 0.5 * jnp.tanh(0.5 * v))).astype(jnp.bfloat16)

    def mm(a, w):
        return lax.dot_general(a, w, (((1,), (1,)), ((), ())), preferred_element_type=jnp.float32)

    col = lax.broadcasted_iota(jnp.int32, (blocks, cols, chans), 1)

    def conv_sp(n, section):
        x0 = n[0].reshape(blocks * cols, chans)
        x1 = n[1].reshape(blocks * cols, chans)
        outs = []
        for row in range(rows):
            own, other = (x0, x1) if row == 0 else (x1, x0)
            other_dr = 1 if row == 0 else -1
            acc = None
            for dc in (-1, 0, 1):
                y = mm(own, wsp_ref[section, 3 + dc + 1]) + mm(other, wsp_ref[section, (other_dr + 1) * 3 + dc + 1])
                y = y.reshape(blocks, cols, chans)
                if dc == -1:
                    y = jnp.where(col == 0, 0.0, pltpu.roll(y, 1, 1))
                elif dc == 1:
                    y = jnp.where(col == cols - 1, 0.0, pltpu.roll(y, cols - 1, 1))
                acc = y if acc is None else acc + y
            outs.append(acc)
        return jnp.stack(outs)

    def conv_tm(n, section):
        n5 = n.reshape(rows, 2, frames, cols, chans)
        blank = jnp.zeros((rows, 2, 1, cols, chans), n.dtype)
        before = jnp.concatenate([blank, n5[:, :, :-1]], axis=2)
        after = jnp.concatenate([n5[:, :, 1:], blank], axis=2)
        flat = rows * blocks * cols
        acc = mm(before.reshape(flat, chans), wt_ref[section, 0])
        acc = acc + mm(n.reshape(flat, chans), wt_ref[section, 1])
        acc = acc + mm(after.reshape(flat, chans), wt_ref[section, 2])
        return acc.reshape(rows, blocks, cols, chans)

    per_frame = float(chans // GROUPS * rows * cols)
    per_sample = per_frame * frames
    for section in range(wsp_ref.shape[0]):
        x = state.astype(jnp.float32)
        normed = norm_silu(x, None, per_frame)
        if section == 0:
            copy_sp.wait()
        state = (x + conv_sp(normed, section)).astype(jnp.bfloat16)
        x = state.astype(jnp.float32)
        normed = norm_silu(x, batch_mix, per_sample)
        if section == 0:
            copy_tm.wait()
        state = (x + conv_tm(normed, section)).astype(jnp.bfloat16)
    last = norm_silu(state.astype(jnp.float32), None, per_frame)
    x0 = last[0].reshape(blocks * cols, chans)
    x1 = last[1].reshape(blocks * cols, chans)
    stride = out_ref.shape[1]
    lane = lax.broadcasted_iota(jnp.int32, (stride, blocks * cols), 1) % cols

    def mm_t(w, a):
        return lax.dot_general(w, a, (((1,), (1,)), ((), ())), preferred_element_type=jnp.float32)

    for row in range(rows):
        own, other = (x0, x1) if row == 0 else (x1, x0)
        other_dr = 1 if row == 0 else -1
        y = mm_t(wl_ref[3 * stride : 6 * stride], own)
        y = y + mm_t(wl_ref[(other_dr + 1) * 3 * stride : (other_dr + 2) * 3 * stride], other)
        acc = None
        for dc in (-1, 0, 1):
            part = y[(dc + 1) * stride : (dc + 2) * stride]
            if dc == -1:
                part = jnp.where(lane == 0, 0.0, pltpu.roll(part, 1, 1))
            elif dc == 1:
                part = jnp.where(lane == cols - 1, 0.0, pltpu.roll(part, blocks * cols - 1, 1))
            acc = part if acc is None else acc + part
        out_ref[row] = acc


def unet(first, emb_u, time_vector, pooled, text_proj, spatial_weights, temporal_weights, conv_last, count):
    rows, frames, cols, chans = first.shape
    blocks = 2 * frames
    taps, outs, _ = conv_last.shape
    padded = -(-outs // 16) * 16
    last = jnp.concatenate([conv_last, jnp.zeros((taps, padded - outs, chans), conv_last.dtype)], axis=1)
    last = last.reshape(taps * padded, chans)
    group = jnp.arange(chans) // (chans // GROUPS)
    same = (group[:, None] == group[None, :]).astype(jnp.float32)
    block_of = jnp.arange(blocks) // frames
    batch_mix = (block_of[:, None] == block_of[None, :]).astype(jnp.float32)
    vmem = pl.BlockSpec(memory_space=pltpu.MemorySpace.VMEM)
    anywhere = pl.BlockSpec(memory_space=pl.ANY)
    return pl.pallas_call(
        functools.partial(unet_body, count=float(count)),
        out_shape=jax.ShapeDtypeStruct((rows, padded, blocks * cols), jnp.float32),
        in_specs=[vmem] * 8 + [anywhere, anywhere],
        out_specs=vmem,
        scratch_shapes=[
            pltpu.VMEM(spatial_weights.shape, spatial_weights.dtype),
            pltpu.VMEM(temporal_weights.shape, temporal_weights.dtype),
            pltpu.SemaphoreType.DMA((2,)),
        ],
        compiler_params=pltpu.CompilerParams(vmem_limit_bytes=100 * 1024 * 1024 // 2),
        cost_estimate=pl.CostEstimate(
            flops=2 * rows * blocks * cols * chans * chans * 9 * spatial_weights.shape[0],
            transcendentals=rows * blocks * cols * chans * 5,
            bytes_accessed=spatial_weights.size * 2 + temporal_weights.size * 2 + first.size * 4,
        ),
    )(first, emb_u, time_vector, pooled, text_proj, last, same, batch_mix, spatial_weights, temporal_weights)[:, :outs]


def butterfly_sum(x, axis):
    peers = lax.axis_size(axis)
    if peers & (peers - 1):
        return jnp.sum(lax.all_gather(x, axis), axis=0)
    k = peers // 2
    while k:
        x = x + lax.ppermute(x, axis, [(i, i ^ k) for i in range(peers)])
        k //= 2
    return x


def butterfly_scan(x, axis):
    peers, me = lax.axis_size(axis), lax.axis_index(axis)
    if peers & (peers - 1):
        everything = lax.all_gather(x, axis)
        lower = (jnp.arange(peers) < me).reshape((peers,) + (1,) * x.ndim)
        return jnp.sum(jnp.where(lower, everything, 0.0), axis=0), jnp.sum(everything, axis=0)
    total, before = x, jnp.zeros_like(x)
    k = 1
    while k < peers:
        got = lax.ppermute(total, axis, [(i, i ^ k) for i in range(peers)])
        before = jnp.where((me & k) != 0, before + got, before)
        total = total + got
        k *= 2
    return before, total


def local(
    timesteps,
    prompt_ids,
    start_latent,
    iterate,
    fresh_noise,
    token_table,
    empty_text,
    time_in,
    time_out,
    text_proj,
    conv_first,
    spatial_weights,
    temporal_weights,
    conv_last,
):
    shard_rows = token_table.shape[0]
    first_row = lax.axis_index("slot") * shard_rows
    local_ids = prompt_ids - first_row
    hits = local_ids[:, None] == jnp.arange(shard_rows, dtype=jnp.int32)[None, :]
    counts = jnp.sum(hits.astype(jnp.float32), axis=0).astype(jnp.bfloat16)[None]
    partial = jnp.dot(counts, token_table, preferred_element_type=jnp.float32)[0]
    pooled = butterfly_sum(partial, "slot")[None]
    text_uncond = layer_norm(empty_text).astype(jnp.bfloat16)[None]
    vector_uncond = jnp.dot(text_uncond, text_proj, preferred_element_type=jnp.float32)
    half_width = time_in.shape[0] // 2
    frequency = jnp.exp(-jnp.log(10000.0) * jnp.arange(half_width, dtype=jnp.float32) / half_width)
    step_value = timesteps[0].astype(jnp.float32)
    angles = step_value * frequency
    feature = jnp.concatenate([jnp.cos(angles), jnp.sin(angles)]).astype(jnp.bfloat16)[None, :]
    hidden = jax.nn.silu(jnp.dot(feature, time_in, preferred_element_type=jnp.float32)).astype(
        jnp.bfloat16
    )
    time_vector = jnp.dot(hidden, time_out, preferred_element_type=jnp.float32)
    latent = iterate[0]
    first = conv_lifted(latent.astype(jnp.bfloat16), conv_first)
    rows, frames, cols, chans = first.shape
    predicted = unet(
        first, vector_uncond + time_vector, time_vector, pooled, text_proj,
        spatial_weights, temporal_weights, conv_last, prompt_ids.shape[0],
    )
    predicted = predicted.reshape(rows, -1, 2, frames, cols).transpose(2, 1, 3, 0, 4)
    guided = predicted[1] + GUIDANCE_SCALE * (predicted[0] - predicted[1])
    alpha_now = alpha_bar(step_value)
    alpha_prev = alpha_bar(step_value - DT)
    scale_ratio = jnp.sqrt(alpha_prev / alpha_now)
    noise_square = (1.0 - alpha_prev) * (1.0 - alpha_now / alpha_prev) / (1.0 - alpha_now)
    kept_square = (1.0 - alpha_prev) * (alpha_now / alpha_prev - alpha_now) / (1.0 - alpha_now)
    eps_factor = jnp.sqrt(kept_square) - scale_ratio * jnp.sqrt(1.0 - alpha_now)
    drift_term = (
        (scale_ratio - 1.0) * latent + eps_factor * guided + jnp.sqrt(noise_square) * fresh_noise[0]
    )[None]
    earlier, total_drift = butterfly_scan(drift_term[0], "slot")
    new_iterate = start_latent[None] + earlier[None]
    final_latent = start_latent + total_drift
    return (new_iterate, final_latent)


def solution(mesh):
    placed = (
        P(("groups", "slot")),
        P("groups"),
        P("groups", None, None, None),
        P(("groups", "slot"), None, None, None, None),
        P(("groups", "slot"), None, None, None, None),
        P("slot", None),
        P(),
        P(),
        P(),
        P(),
        P(),
        P(),
        P(),
        P(),
    )
    return jax.shard_map(
        local,
        mesh=mesh,
        in_specs=placed,
        out_specs=(P(("groups", "slot"), None, None, None, None), P("groups", None, None, None)),
        check_vma=False,
    )
```

```python
import functools

import jax
import jax.numpy as jnp
from jax import lax
from jax.sharding import PartitionSpec as P
from jax.experimental import pallas as pl
from jax.experimental.pallas import tpu as pltpu

GROUPS = 32
DT = 50


NORM_EPS = 1e-05
GUIDANCE_SCALE = 5.0


def alpha_bar(step_value):
    phase_angle = (step_value / 1000.0 + 0.008) / 1.008 * (jnp.pi / 2.0)
    cosine = jnp.cos(phase_angle)
    return cosine * cosine


def layer_norm(values):
    average = jnp.mean(values)
    spread = jnp.mean((values - average) ** 2)
    return (values - average) * lax.rsqrt(spread + NORM_EPS)


def group_norm(values, axes):
    batch, channels = (values.shape[0], values.shape[1])
    shaped = values.reshape((batch, GROUPS, channels // GROUPS) + values.shape[2:])
    average = jnp.mean(shaped, axis=axes, keepdims=True)
    spread = jnp.mean((shaped - average) ** 2, axis=axes, keepdims=True)
    return ((shaped - average) * lax.rsqrt(spread + NORM_EPS)).reshape(values.shape)


def shift_columns(inputs, offset):
    if offset == 0:
        return inputs
    blank = jnp.zeros(inputs.shape[:-1] + (1,), inputs.dtype)
    if offset == 1:
        return jnp.concatenate([inputs[..., 1:], blank], axis=-1)
    return jnp.concatenate([blank, inputs[..., :-1]], axis=-1)


def conv_space(inputs, weight):
    row_count = inputs.shape[3]
    result = None
    for col_step in range(3):
        moved = shift_columns(inputs, col_step - 1)
        padded = jnp.pad(moved, ((0, 0), (0, 0), (0, 0), (1, 1), (0, 0)))
        for row_step in range(3):
            window = padded[:, :, :, row_step : row_step + row_count]
            term = jnp.einsum(
                "oc,bcfrw->bofrw",
                weight[row_step * 3 + col_step],
                window,
                preferred_element_type=jnp.float32,
            )
            result = term if result is None else result + term
    return result


def conv_lifted(inputs, weight):
    row_count, col_count = inputs.shape[2], inputs.shape[3]
    padded = jnp.pad(inputs, ((0, 0), (0, 0), (1, 1), (1, 1)))
    windows = jnp.concatenate(
        [padded[:, :, tap // 3 : tap // 3 + row_count, tap % 3 : tap % 3 + col_count] for tap in range(9)],
        axis=0,
    )
    stacked = weight.transpose(1, 0, 2).reshape(weight.shape[1], -1)
    result = lax.dot_general(windows, stacked, (((0,), (1,)), ((), ())), preferred_element_type=jnp.float32)
    return result.transpose(1, 0, 2, 3)


def conv_time(inputs, weight):
    padded = jnp.pad(inputs, ((0, 0), (0, 0), (1, 1), (0, 0), (0, 0)))
    frame_count = inputs.shape[2]
    result = None
    for tap_index in range(3):
        window = padded[:, :, tap_index : tap_index + frame_count]
        term = jnp.einsum(
            "oc,bcfrw->bofrw", weight[tap_index], window, preferred_element_type=jnp.float32
        )
        result = term if result is None else result + term
    return result


def unet_body(
    first_ref, emb_u_ref, time_ref, pooled_ref, tproj_ref, wl_ref, same_ref, batch_ref,
    wsp_hbm, wt_hbm, out_ref, wsp_ref, wt_ref, sems, *, count
):
    rows, frames, cols, chans = first_ref.shape
    blocks = 2 * frames
    copy_sp = pltpu.make_async_copy(wsp_hbm, wsp_ref, sems.at[0])
    copy_sp.start()
    copy_tm = pltpu.make_async_copy(wt_hbm, wt_ref, sems.at[1])
    copy_tm.start()
    same = same_ref[...]
    batch_mix = batch_ref[...]
    hi = lax.Precision.HIGH

    pooled = pooled_ref[...] / count
    average = jnp.mean(pooled, axis=1, keepdims=True)
    spread = jnp.mean((pooled - average) ** 2, axis=1, keepdims=True)
    text = ((pooled - average) * lax.rsqrt(spread + NORM_EPS)).astype(jnp.bfloat16)
    text = jnp.broadcast_to(text, (8, text.shape[1]))
    vector = jnp.dot(text, tproj_ref[...], preferred_element_type=jnp.float32)[0:1]
    emb_c = (vector + time_ref[...]).reshape(1, 1, 1, chans)
    emb_u = emb_u_ref[...].reshape(1, 1, 1, chans)
    first = first_ref[...]
    state = jnp.concatenate(
        [(first + emb_c).astype(jnp.bfloat16), (first + emb_u).astype(jnp.bfloat16)], axis=1
    )

    def group_stats(sums, count, mix):
        if mix is not None:
            sums = jnp.dot(mix, sums, precision=hi, preferred_element_type=jnp.float32)
        return jnp.dot(sums, same, precision=hi, preferred_element_type=jnp.float32) / count

    def norm_silu(x, mix, count):
        colsum = jnp.sum(x[0], axis=1) + jnp.sum(x[1], axis=1)
        mean = group_stats(colsum, count, mix)
        d = x - mean[None, :, None, :]
        sq = d * d
        var = group_stats(jnp.sum(sq[0], axis=1) + jnp.sum(sq[1], axis=1), count, mix)
        v = d * lax.rsqrt(var + NORM_EPS)[None, :, None, :]
        return (v * (0.5 + 0.5 * jnp.tanh(0.5 * v))).astype(jnp.bfloat16)

    def mm(a, w):
        return lax.dot_general(a, w, (((1,), (1,)), ((), ())), preferred_element_type=jnp.float32)

    col = lax.broadcasted_iota(jnp.int32, (blocks, cols, chans), 1)

    def conv_sp(n, section):
        x0 = n[0].reshape(blocks * cols, chans)
        x1 = n[1].reshape(blocks * cols, chans)
        outs = []
        for row in range(rows):
            own, other = (x0, x1) if row == 0 else (x1, x0)
            other_dr = 1 if row == 0 else -1
            acc = None
            for dc in (-1, 0, 1):
                y = mm(own, wsp_ref[section, 3 + dc + 1]) + mm(other, wsp_ref[section, (other_dr + 1) * 3 + dc + 1])
                y = y.reshape(blocks, cols, chans)
                if dc == -1:
                    y = jnp.where(col == 0, 0.0, pltpu.roll(y, 1, 1))
                elif dc == 1:
                    y = jnp.where(col == cols - 1, 0.0, pltpu.roll(y, cols - 1, 1))
                acc = y if acc is None else acc + y
            outs.append(acc)
        return jnp.stack(outs)

    def conv_tm(n, section):
        n5 = n.reshape(rows, 2, frames, cols, chans)
        blank = jnp.zeros((rows, 2, 1, cols, chans), n.dtype)
        before = jnp.concatenate([blank, n5[:, :, :-1]], axis=2)
        after = jnp.concatenate([n5[:, :, 1:], blank], axis=2)
        flat = rows * blocks * cols
        acc = mm(before.reshape(flat, chans), wt_ref[section, 0])
        acc = acc + mm(n.reshape(flat, chans), wt_ref[section, 1])
        acc = acc + mm(after.reshape(flat, chans), wt_ref[section, 2])
        return acc.reshape(rows, blocks, cols, chans)

    per_frame = float(chans // GROUPS * rows * cols)
    per_sample = per_frame * frames
    for section in range(wsp_ref.shape[0]):
        x = state.astype(jnp.float32)
        normed = norm_silu(x, None, per_frame)
        if section == 0:
            copy_sp.wait()
        state = (x + conv_sp(normed, section)).astype(jnp.bfloat16)
        x = state.astype(jnp.float32)
        normed = norm_silu(x, batch_mix, per_sample)
        if section == 0:
            copy_tm.wait()
        state = (x + conv_tm(normed, section)).astype(jnp.bfloat16)
    last = norm_silu(state.astype(jnp.float32), None, per_frame)
    x0 = last[0].reshape(blocks * cols, chans)
    x1 = last[1].reshape(blocks * cols, chans)
    stride = out_ref.shape[1]
    lane = lax.broadcasted_iota(jnp.int32, (stride, blocks * cols), 1) % cols

    def mm_t(w, a):
        return lax.dot_general(w, a, (((1,), (1,)), ((), ())), preferred_element_type=jnp.float32)

    for row in range(rows):
        own, other = (x0, x1) if row == 0 else (x1, x0)
        other_dr = 1 if row == 0 else -1
        y = mm_t(wl_ref[3 * stride : 6 * stride], own)
        y = y + mm_t(wl_ref[(other_dr + 1) * 3 * stride : (other_dr + 2) * 3 * stride], other)
        acc = None
        for dc in (-1, 0, 1):
            part = y[(dc + 1) * stride : (dc + 2) * stride]
            if dc == -1:
                part = jnp.where(lane == 0, 0.0, pltpu.roll(part, 1, 1))
            elif dc == 1:
                part = jnp.where(lane == cols - 1, 0.0, pltpu.roll(part, blocks * cols - 1, 1))
            acc = part if acc is None else acc + part
        out_ref[row] = acc


def unet(first, emb_u, time_vector, pooled, text_proj, spatial_weights, temporal_weights, conv_last, count):
    rows, frames, cols, chans = first.shape
    blocks = 2 * frames
    taps, outs, _ = conv_last.shape
    padded = -(-outs // 16) * 16
    last = jnp.concatenate([conv_last, jnp.zeros((taps, padded - outs, chans), conv_last.dtype)], axis=1)
    last = last.reshape(taps * padded, chans)
    group = jnp.arange(chans) // (chans // GROUPS)
    same = (group[:, None] == group[None, :]).astype(jnp.float32)
    block_of = jnp.arange(blocks) // frames
    batch_mix = (block_of[:, None] == block_of[None, :]).astype(jnp.float32)
    vmem = pl.BlockSpec(memory_space=pltpu.MemorySpace.VMEM)
    anywhere = pl.BlockSpec(memory_space=pl.ANY)
    return pl.pallas_call(
        functools.partial(unet_body, count=float(count)),
        out_shape=jax.ShapeDtypeStruct((rows, padded, blocks * cols), jnp.float32),
        in_specs=[vmem] * 8 + [anywhere, anywhere],
        out_specs=vmem,
        scratch_shapes=[
            pltpu.VMEM(spatial_weights.shape, spatial_weights.dtype),
            pltpu.VMEM(temporal_weights.shape, temporal_weights.dtype),
            pltpu.SemaphoreType.DMA((2,)),
        ],
        compiler_params=pltpu.CompilerParams(vmem_limit_bytes=100 * 1024 * 1024 // 2),
        cost_estimate=pl.CostEstimate(
            flops=2 * rows * blocks * cols * chans * chans * 9 * spatial_weights.shape[0],
            transcendentals=rows * blocks * cols * chans * 5,
            bytes_accessed=spatial_weights.size * 2 + temporal_weights.size * 2 + first.size * 4,
        ),
    )(first, emb_u, time_vector, pooled, text_proj, last, same, batch_mix, spatial_weights, temporal_weights)[:, :outs]


def butterfly_sum(x, axis):
    peers = lax.axis_size(axis)
    if peers & (peers - 1):
        return jnp.sum(lax.all_gather(x, axis), axis=0)
    k = peers // 2
    while k:
        x = x + lax.ppermute(x, axis, [(i, i ^ k) for i in range(peers)])
        k //= 2
    return x


def butterfly_scan(x, axis):
    peers, me = lax.axis_size(axis), lax.axis_index(axis)
    if peers & (peers - 1):
        everything = lax.all_gather(x, axis)
        lower = (jnp.arange(peers) < me).reshape((peers,) + (1,) * x.ndim)
        return jnp.sum(jnp.where(lower, everything, 0.0), axis=0), jnp.sum(everything, axis=0)
    total, before = x, jnp.zeros_like(x)
    k = 1
    while k < peers:
        got = lax.ppermute(total, axis, [(i, i ^ k) for i in range(peers)])
        before = jnp.where((me & k) != 0, before + got, before)
        total = total + got
        k *= 2
    return before, total


def local(
    timesteps,
    prompt_ids,
    start_latent,
    iterate,
    fresh_noise,
    token_table,
    empty_text,
    time_in,
    time_out,
    text_proj,
    conv_first,
    spatial_weights,
    temporal_weights,
    conv_last,
):
    shard_rows = token_table.shape[0]
    first_row = lax.axis_index("slot") * shard_rows
    local_ids = prompt_ids - first_row
    hits = local_ids[:, None] == jnp.arange(shard_rows, dtype=jnp.int32)[None, :]
    counts = jnp.sum(hits.astype(jnp.float32), axis=0).astype(jnp.bfloat16)[None]
    partial = jnp.dot(counts, token_table, preferred_element_type=jnp.float32)[0]
    pooled = butterfly_sum(partial, "slot")[None]
    text_uncond = layer_norm(empty_text).astype(jnp.bfloat16)[None]
    vector_uncond = jnp.dot(text_uncond, text_proj, preferred_element_type=jnp.float32)
    half_width = time_in.shape[0] // 2
    frequency = jnp.exp(-jnp.log(10000.0) * jnp.arange(half_width, dtype=jnp.float32) / half_width)
    step_value = timesteps[0].astype(jnp.float32)
    angles = step_value * frequency
    feature = jnp.concatenate([jnp.cos(angles), jnp.sin(angles)]).astype(jnp.bfloat16)[None, :]
    hidden = jax.nn.silu(jnp.dot(feature, time_in, preferred_element_type=jnp.float32)).astype(
        jnp.bfloat16
    )
    time_vector = jnp.dot(hidden, time_out, preferred_element_type=jnp.float32)
    latent = iterate[0]
    first = conv_lifted(latent.astype(jnp.bfloat16), conv_first)
    rows, frames, cols, chans = first.shape
    predicted = unet(
        first, vector_uncond + time_vector, time_vector, pooled, text_proj,
        spatial_weights, temporal_weights, conv_last, prompt_ids.shape[0],
    )
    predicted = predicted.reshape(rows, -1, 2, frames, cols).transpose(2, 1, 3, 0, 4)
    guided = predicted[1] + GUIDANCE_SCALE * (predicted[0] - predicted[1])
    alpha_now = alpha_bar(step_value)
    alpha_prev = alpha_bar(step_value - DT)
    scale_ratio = jnp.sqrt(alpha_prev / alpha_now)
    noise_square = (1.0 - alpha_prev) * (1.0 - alpha_now / alpha_prev) / (1.0 - alpha_now)
    kept_square = (1.0 - alpha_prev) * (alpha_now / alpha_prev - alpha_now) / (1.0 - alpha_now)
    eps_factor = jnp.sqrt(kept_square) - scale_ratio * jnp.sqrt(1.0 - alpha_now)
    drift_term = (
        (scale_ratio - 1.0) * latent + eps_factor * guided + jnp.sqrt(noise_square) * fresh_noise[0]
    )[None]
    earlier, total_drift = butterfly_scan(drift_term[0], "slot")
    new_iterate = start_latent[None] + earlier[None]
    final_latent = start_latent + total_drift
    return (new_iterate, final_latent)


def solution(mesh):
    placed = (
        P(("groups", "slot")),
        P("groups"),
        P("groups", None, None, None),
        P(("groups", "slot"), None, None, None, None),
        P(("groups", "slot"), None, None, None, None),
        P("slot", None),
        P(),
        P(),
        P(),
        P(),
        P(),
        P(),
        P(),
        P(),
    )
    return jax.shard_map(
        local,
        mesh=mesh,
        in_specs=placed,
        out_specs=(P(("groups", "slot"), None, None, None, None), P("groups", None, None, None)),
        check_vma=False,
    )
```

```python
import functools

import jax
import jax.numpy as jnp
from jax import lax
from jax.sharding import PartitionSpec as P
from jax.experimental import pallas as pl
from jax.experimental.pallas import tpu as pltpu

GROUPS = 32
DT = 50


NORM_EPS = 1e-05
GUIDANCE_SCALE = 5.0


def alpha_bar(step_value):
    phase_angle = (step_value / 1000.0 + 0.008) / 1.008 * (jnp.pi / 2.0)
    cosine = jnp.cos(phase_angle)
    return cosine * cosine


def layer_norm(values):
    average = jnp.mean(values)
    spread = jnp.mean((values - average) ** 2)
    return (values - average) * lax.rsqrt(spread + NORM_EPS)


def group_norm(values, axes):
    batch, channels = (values.shape[0], values.shape[1])
    shaped = values.reshape((batch, GROUPS, channels // GROUPS) + values.shape[2:])
    average = jnp.mean(shaped, axis=axes, keepdims=True)
    spread = jnp.mean((shaped - average) ** 2, axis=axes, keepdims=True)
    return ((shaped - average) * lax.rsqrt(spread + NORM_EPS)).reshape(values.shape)


def shift_columns(inputs, offset):
    if offset == 0:
        return inputs
    blank = jnp.zeros(inputs.shape[:-1] + (1,), inputs.dtype)
    if offset == 1:
        return jnp.concatenate([inputs[..., 1:], blank], axis=-1)
    return jnp.concatenate([blank, inputs[..., :-1]], axis=-1)


def conv_space(inputs, weight):
    row_count = inputs.shape[3]
    result = None
    for col_step in range(3):
        moved = shift_columns(inputs, col_step - 1)
        padded = jnp.pad(moved, ((0, 0), (0, 0), (0, 0), (1, 1), (0, 0)))
        for row_step in range(3):
            window = padded[:, :, :, row_step : row_step + row_count]
            term = jnp.einsum(
                "oc,bcfrw->bofrw",
                weight[row_step * 3 + col_step],
                window,
                preferred_element_type=jnp.float32,
            )
            result = term if result is None else result + term
    return result


def conv_lifted(inputs, weight):
    row_count, col_count = inputs.shape[2], inputs.shape[3]
    padded = jnp.pad(inputs, ((0, 0), (0, 0), (1, 1), (1, 1)))
    windows = jnp.concatenate(
        [padded[:, :, tap // 3 : tap // 3 + row_count, tap % 3 : tap % 3 + col_count] for tap in range(9)],
        axis=0,
    )
    stacked = weight.transpose(1, 0, 2).reshape(weight.shape[1], -1)
    result = lax.dot_general(windows, stacked, (((0,), (1,)), ((), ())), preferred_element_type=jnp.float32)
    return result.transpose(1, 0, 2, 3)


def conv_time(inputs, weight):
    padded = jnp.pad(inputs, ((0, 0), (0, 0), (1, 1), (0, 0), (0, 0)))
    frame_count = inputs.shape[2]
    result = None
    for tap_index in range(3):
        window = padded[:, :, tap_index : tap_index + frame_count]
        term = jnp.einsum(
            "oc,bcfrw->bofrw", weight[tap_index], window, preferred_element_type=jnp.float32
        )
        result = term if result is None else result + term
    return result


def unet_body(
    first_ref, emb_u_ref, time_ref, pooled_ref, tproj_ref, wl_ref, same_ref, batch_ref,
    wsp_hbm, wt_hbm, out_ref, wsp_ref, wt_ref, sems, *, count
):
    rows, frames, cols, chans = first_ref.shape
    blocks = 2 * frames
    copy_sp = pltpu.make_async_copy(wsp_hbm, wsp_ref, sems.at[0])
    copy_sp.start()
    copy_tm = pltpu.make_async_copy(wt_hbm, wt_ref, sems.at[1])
    copy_tm.start()
    same = same_ref[...]
    batch_mix = batch_ref[...]
    hi = lax.Precision.HIGH

    pooled = pooled_ref[...] / count
    average = jnp.mean(pooled, axis=1, keepdims=True)
    spread = jnp.mean((pooled - average) ** 2, axis=1, keepdims=True)
    text = ((pooled - average) * lax.rsqrt(spread + NORM_EPS)).astype(jnp.bfloat16)
    text = jnp.broadcast_to(text, (8, text.shape[1]))
    vector = jnp.dot(text, tproj_ref[...], preferred_element_type=jnp.float32)[0:1]
    emb_c = (vector + time_ref[...]).reshape(1, 1, 1, chans)
    emb_u = emb_u_ref[...].reshape(1, 1, 1, chans)
    first = first_ref[...]
    state = jnp.concatenate(
        [(first + emb_c).astype(jnp.bfloat16), (first + emb_u).astype(jnp.bfloat16)], axis=1
    )

    def group_stats(sums, count, mix):
        if mix is not None:
            sums = jnp.dot(mix, sums, precision=hi, preferred_element_type=jnp.float32)
        return jnp.dot(sums, same, precision=hi, preferred_element_type=jnp.float32) / count

    def norm_silu(x, mix, count):
        colsum = jnp.sum(x[0], axis=1) + jnp.sum(x[1], axis=1)
        mean = group_stats(colsum, count, mix)
        d = x - mean[None, :, None, :]
        sq = d * d
        var = group_stats(jnp.sum(sq[0], axis=1) + jnp.sum(sq[1], axis=1), count, mix)
        v = d * lax.rsqrt(var + NORM_EPS)[None, :, None, :]
        return (v * (0.5 + 0.5 * jnp.tanh(0.5 * v))).astype(jnp.bfloat16)

    def mm(a, w):
        return lax.dot_general(a, w, (((1,), (1,)), ((), ())), preferred_element_type=jnp.float32)

    col = lax.broadcasted_iota(jnp.int32, (blocks, cols, chans), 1)

    def conv_sp(n, section):
        x0 = n[0].reshape(blocks * cols, chans)
        x1 = n[1].reshape(blocks * cols, chans)
        outs = []
        for row in range(rows):
            own, other = (x0, x1) if row == 0 else (x1, x0)
            other_dr = 1 if row == 0 else -1
            acc = None
            for dc in (-1, 0, 1):
                y = mm(own, wsp_ref[section, 3 + dc + 1]) + mm(other, wsp_ref[section, (other_dr + 1) * 3 + dc + 1])
                y = y.reshape(blocks, cols, chans)
                if dc == -1:
                    y = jnp.where(col == 0, 0.0, pltpu.roll(y, 1, 1))
                elif dc == 1:
                    y = jnp.where(col == cols - 1, 0.0, pltpu.roll(y, cols - 1, 1))
                acc = y if acc is None else acc + y
            outs.append(acc)
        return jnp.stack(outs)

    def conv_tm(n, section):
        n5 = n.reshape(rows, 2, frames, cols, chans)
        blank = jnp.zeros((rows, 2, 1, cols, chans), n.dtype)
        before = jnp.concatenate([blank, n5[:, :, :-1]], axis=2)
        after = jnp.concatenate([n5[:, :, 1:], blank], axis=2)
        flat = rows * blocks * cols
        acc = mm(before.reshape(flat, chans), wt_ref[section, 0])
        acc = acc + mm(n.reshape(flat, chans), wt_ref[section, 1])
        acc = acc + mm(after.reshape(flat, chans), wt_ref[section, 2])
        return acc.reshape(rows, blocks, cols, chans)

    per_frame = float(chans // GROUPS * rows * cols)
    per_sample = per_frame * frames
    for section in range(wsp_ref.shape[0]):
        x = state.astype(jnp.float32)
        normed = norm_silu(x, None, per_frame)
        if section == 0:
            copy_sp.wait()
        state = (x + conv_sp(normed, section)).astype(jnp.bfloat16)
        x = state.astype(jnp.float32)
        normed = norm_silu(x, batch_mix, per_sample)
        if section == 0:
            copy_tm.wait()
        state = (x + conv_tm(normed, section)).astype(jnp.bfloat16)
    last = norm_silu(state.astype(jnp.float32), None, per_frame)
    x0 = last[0].reshape(blocks * cols, chans)
    x1 = last[1].reshape(blocks * cols, chans)
    stride = out_ref.shape[1]
    lane = lax.broadcasted_iota(jnp.int32, (stride, blocks * cols), 1) % cols

    def mm_t(w, a):
        return lax.dot_general(w, a, (((1,), (1,)), ((), ())), preferred_element_type=jnp.float32)

    for row in range(rows):
        own, other = (x0, x1) if row == 0 else (x1, x0)
        other_dr = 1 if row == 0 else -1
        y = mm_t(wl_ref[3 * stride : 6 * stride], own)
        y = y + mm_t(wl_ref[(other_dr + 1) * 3 * stride : (other_dr + 2) * 3 * stride], other)
        acc = None
        for dc in (-1, 0, 1):
            part = y[(dc + 1) * stride : (dc + 2) * stride]
            if dc == -1:
                part = jnp.where(lane == 0, 0.0, pltpu.roll(part, 1, 1))
            elif dc == 1:
                part = jnp.where(lane == cols - 1, 0.0, pltpu.roll(part, blocks * cols - 1, 1))
            acc = part if acc is None else acc + part
        out_ref[row] = acc


def unet(first, emb_u, time_vector, pooled, text_proj, spatial_weights, temporal_weights, conv_last, count):
    rows, frames, cols, chans = first.shape
    blocks = 2 * frames
    taps, outs, _ = conv_last.shape
    padded = -(-outs // 16) * 16
    last = jnp.concatenate([conv_last, jnp.zeros((taps, padded - outs, chans), conv_last.dtype)], axis=1)
    last = last.reshape(taps * padded, chans)
    group = jnp.arange(chans) // (chans // GROUPS)
    same = (group[:, None] == group[None, :]).astype(jnp.float32)
    block_of = jnp.arange(blocks) // frames
    batch_mix = (block_of[:, None] == block_of[None, :]).astype(jnp.float32)
    vmem = pl.BlockSpec(memory_space=pltpu.MemorySpace.VMEM)
    anywhere = pl.BlockSpec(memory_space=pl.ANY)
    return pl.pallas_call(
        functools.partial(unet_body, count=float(count)),
        out_shape=jax.ShapeDtypeStruct((rows, padded, blocks * cols), jnp.float32),
        in_specs=[vmem] * 8 + [anywhere, anywhere],
        out_specs=vmem,
        scratch_shapes=[
            pltpu.VMEM(spatial_weights.shape, spatial_weights.dtype),
            pltpu.VMEM(temporal_weights.shape, temporal_weights.dtype),
            pltpu.SemaphoreType.DMA((2,)),
        ],
        compiler_params=pltpu.CompilerParams(vmem_limit_bytes=100 * 1024 * 1024 // 2),
        cost_estimate=pl.CostEstimate(
            flops=2 * rows * blocks * cols * chans * chans * 9 * spatial_weights.shape[0],
            transcendentals=rows * blocks * cols * chans * 5,
            bytes_accessed=spatial_weights.size * 2 + temporal_weights.size * 2 + first.size * 4,
        ),
    )(first, emb_u, time_vector, pooled, text_proj, last, same, batch_mix, spatial_weights, temporal_weights)[:, :outs]


def butterfly_sum(x, axis):
    peers = lax.axis_size(axis)
    if peers & (peers - 1):
        return jnp.sum(lax.all_gather(x, axis), axis=0)
    k = peers // 2
    while k:
        x = x + lax.ppermute(x, axis, [(i, i ^ k) for i in range(peers)])
        k //= 2
    return x


def butterfly_scan(x, axis):
    peers, me = lax.axis_size(axis), lax.axis_index(axis)
    if peers & (peers - 1):
        everything = lax.all_gather(x, axis)
        lower = (jnp.arange(peers) < me).reshape((peers,) + (1,) * x.ndim)
        return jnp.sum(jnp.where(lower, everything, 0.0), axis=0), jnp.sum(everything, axis=0)
    total, before = x, jnp.zeros_like(x)
    k = 1
    while k < peers:
        got = lax.ppermute(total, axis, [(i, i ^ k) for i in range(peers)])
        before = jnp.where((me & k) != 0, before + got, before)
        total = total + got
        k *= 2
    return before, total


def local(
    timesteps,
    prompt_ids,
    start_latent,
    iterate,
    fresh_noise,
    token_table,
    empty_text,
    time_in,
    time_out,
    text_proj,
    conv_first,
    spatial_weights,
    temporal_weights,
    conv_last,
):
    shard_rows = token_table.shape[0]
    first_row = lax.axis_index("slot") * shard_rows
    local_ids = prompt_ids - first_row
    hits = local_ids[:, None] == jnp.arange(shard_rows, dtype=jnp.int32)[None, :]
    counts = jnp.sum(hits.astype(jnp.float32), axis=0).astype(jnp.bfloat16)[None]
    partial = jnp.dot(counts, token_table, preferred_element_type=jnp.float32)[0]
    text_uncond = layer_norm(empty_text).astype(jnp.bfloat16)[None]
    vector_uncond = jnp.dot(text_uncond, text_proj, preferred_element_type=jnp.float32)
    half_width = time_in.shape[0] // 2
    frequency = jnp.exp(-jnp.log(10000.0) * jnp.arange(half_width, dtype=jnp.float32) / half_width)
    step_value = timesteps[0].astype(jnp.float32)
    angles = step_value * frequency
    feature = jnp.concatenate([jnp.cos(angles), jnp.sin(angles)]).astype(jnp.bfloat16)[None, :]
    hidden = jax.nn.silu(jnp.dot(feature, time_in, preferred_element_type=jnp.float32)).astype(
        jnp.bfloat16
    )
    time_vector = jnp.dot(hidden, time_out, preferred_element_type=jnp.float32)
    latent = iterate[0]
    first = conv_lifted(latent.astype(jnp.bfloat16), conv_first)
    partial, first, vector_uncond, time_vector = lax.optimization_barrier(
        (partial, first, vector_uncond, time_vector)
    )
    pooled = butterfly_sum(partial, "slot")[None]
    rows, frames, cols, chans = first.shape
    predicted = unet(
        first, vector_uncond + time_vector, time_vector, pooled, text_proj,
        spatial_weights, temporal_weights, conv_last, prompt_ids.shape[0],
    )
    predicted = predicted.reshape(rows, -1, 2, frames, cols).transpose(2, 1, 3, 0, 4)
    guided = predicted[1] + GUIDANCE_SCALE * (predicted[0] - predicted[1])
    alpha_now = alpha_bar(step_value)
    alpha_prev = alpha_bar(step_value - DT)
    scale_ratio = jnp.sqrt(alpha_prev / alpha_now)
    noise_square = (1.0 - alpha_prev) * (1.0 - alpha_now / alpha_prev) / (1.0 - alpha_now)
    kept_square = (1.0 - alpha_prev) * (alpha_now / alpha_prev - alpha_now) / (1.0 - alpha_now)
    eps_factor = jnp.sqrt(kept_square) - scale_ratio * jnp.sqrt(1.0 - alpha_now)
    drift_term = (
        (scale_ratio - 1.0) * latent + eps_factor * guided + jnp.sqrt(noise_square) * fresh_noise[0]
    )[None]
    earlier, total_drift = butterfly_scan(drift_term[0], "slot")
    new_iterate = start_latent[None] + earlier[None]
    final_latent = start_latent + total_drift
    return (new_iterate, final_latent)


def solution(mesh):
    placed = (
        P(("groups", "slot")),
        P("groups"),
        P("groups", None, None, None),
        P(("groups", "slot"), None, None, None, None),
        P(("groups", "slot"), None, None, None, None),
        P("slot", None),
        P(),
        P(),
        P(),
        P(),
        P(),
        P(),
        P(),
        P(),
    )
    return jax.shard_map(
        local,
        mesh=mesh,
        in_specs=placed,
        out_specs=(P(("groups", "slot"), None, None, None, None), P("groups", None, None, None)),
        check_vma=False,
    )
```

```python
import functools

import jax
import jax.numpy as jnp
from jax import lax
from jax.sharding import PartitionSpec as P
from jax.experimental import pallas as pl
from jax.experimental.pallas import tpu as pltpu

GROUPS = 32
DT = 50


NORM_EPS = 1e-05
GUIDANCE_SCALE = 5.0


def alpha_bar(step_value):
    phase_angle = (step_value / 1000.0 + 0.008) / 1.008 * (jnp.pi / 2.0)
    cosine = jnp.cos(phase_angle)
    return cosine * cosine


def layer_norm(values):
    average = jnp.mean(values)
    spread = jnp.mean((values - average) ** 2)
    return (values - average) * lax.rsqrt(spread + NORM_EPS)


def group_norm(values, axes):
    batch, channels = (values.shape[0], values.shape[1])
    shaped = values.reshape((batch, GROUPS, channels // GROUPS) + values.shape[2:])
    average = jnp.mean(shaped, axis=axes, keepdims=True)
    spread = jnp.mean((shaped - average) ** 2, axis=axes, keepdims=True)
    return ((shaped - average) * lax.rsqrt(spread + NORM_EPS)).reshape(values.shape)


def shift_columns(inputs, offset):
    if offset == 0:
        return inputs
    blank = jnp.zeros(inputs.shape[:-1] + (1,), inputs.dtype)
    if offset == 1:
        return jnp.concatenate([inputs[..., 1:], blank], axis=-1)
    return jnp.concatenate([blank, inputs[..., :-1]], axis=-1)


def conv_space(inputs, weight):
    row_count = inputs.shape[3]
    result = None
    for col_step in range(3):
        moved = shift_columns(inputs, col_step - 1)
        padded = jnp.pad(moved, ((0, 0), (0, 0), (0, 0), (1, 1), (0, 0)))
        for row_step in range(3):
            window = padded[:, :, :, row_step : row_step + row_count]
            term = jnp.einsum(
                "oc,bcfrw->bofrw",
                weight[row_step * 3 + col_step],
                window,
                preferred_element_type=jnp.float32,
            )
            result = term if result is None else result + term
    return result


def conv_lifted(inputs, weight):
    row_count, col_count = inputs.shape[2], inputs.shape[3]
    padded = jnp.pad(inputs, ((0, 0), (0, 0), (1, 1), (1, 1)))
    windows = jnp.concatenate(
        [padded[:, :, tap // 3 : tap // 3 + row_count, tap % 3 : tap % 3 + col_count] for tap in range(9)],
        axis=0,
    )
    stacked = weight.transpose(1, 0, 2).reshape(weight.shape[1], -1)
    result = lax.dot_general(windows, stacked, (((0,), (1,)), ((), ())), preferred_element_type=jnp.float32)
    return result.transpose(1, 0, 2, 3)


def conv_time(inputs, weight):
    padded = jnp.pad(inputs, ((0, 0), (0, 0), (1, 1), (0, 0), (0, 0)))
    frame_count = inputs.shape[2]
    result = None
    for tap_index in range(3):
        window = padded[:, :, tap_index : tap_index + frame_count]
        term = jnp.einsum(
            "oc,bcfrw->bofrw", weight[tap_index], window, preferred_element_type=jnp.float32
        )
        result = term if result is None else result + term
    return result


def unet_body(
    first_ref, emb_u_ref, time_ref, pooled_ref, tproj_ref, wl_ref, same_ref, batch_ref,
    wsp_hbm, wt_ref, out_ref, wsp_ref, sems, *, count
):
    rows, frames, cols, chans = first_ref.shape
    blocks = 2 * frames
    copy_sp = pltpu.make_async_copy(wsp_hbm, wsp_ref, sems.at[0])
    copy_sp.start()
    same = same_ref[...]
    batch_mix = batch_ref[...]
    hi = lax.Precision.HIGH

    pooled = pooled_ref[...] / count
    average = jnp.mean(pooled, axis=1, keepdims=True)
    spread = jnp.mean((pooled - average) ** 2, axis=1, keepdims=True)
    text = ((pooled - average) * lax.rsqrt(spread + NORM_EPS)).astype(jnp.bfloat16)
    text = jnp.broadcast_to(text, (8, text.shape[1]))
    vector = jnp.dot(text, tproj_ref[...], preferred_element_type=jnp.float32)[0:1]
    emb_c = (vector + time_ref[...]).reshape(1, 1, 1, chans)
    emb_u = emb_u_ref[...].reshape(1, 1, 1, chans)
    first = first_ref[...]
    state = jnp.concatenate(
        [(first + emb_c).astype(jnp.bfloat16), (first + emb_u).astype(jnp.bfloat16)], axis=1
    )

    def group_stats(sums, count, mix):
        if mix is not None:
            sums = jnp.dot(mix, sums, precision=hi, preferred_element_type=jnp.float32)
        return jnp.dot(sums, same, precision=hi, preferred_element_type=jnp.float32) / count

    def norm_silu(x, mix, count):
        colsum = jnp.sum(x[0], axis=1) + jnp.sum(x[1], axis=1)
        mean = group_stats(colsum, count, mix)
        d = x - mean[None, :, None, :]
        sq = d * d
        var = group_stats(jnp.sum(sq[0], axis=1) + jnp.sum(sq[1], axis=1), count, mix)
        v = d * lax.rsqrt(var + NORM_EPS)[None, :, None, :]
        return (v * (0.5 + 0.5 * jnp.tanh(0.5 * v))).astype(jnp.bfloat16)

    def mm(a, w):
        return lax.dot_general(a, w, (((1,), (1,)), ((), ())), preferred_element_type=jnp.float32)

    col = lax.broadcasted_iota(jnp.int32, (blocks, cols, chans), 1)

    def conv_sp(n, section):
        x0 = n[0].reshape(blocks * cols, chans)
        x1 = n[1].reshape(blocks * cols, chans)
        outs = []
        for row in range(rows):
            own, other = (x0, x1) if row == 0 else (x1, x0)
            other_dr = 1 if row == 0 else -1
            acc = None
            for dc in (-1, 0, 1):
                y = mm(own, wsp_ref[section, 3 + dc + 1]) + mm(other, wsp_ref[section, (other_dr + 1) * 3 + dc + 1])
                y = y.reshape(blocks, cols, chans)
                if dc == -1:
                    y = jnp.where(col == 0, 0.0, pltpu.roll(y, 1, 1))
                elif dc == 1:
                    y = jnp.where(col == cols - 1, 0.0, pltpu.roll(y, cols - 1, 1))
                acc = y if acc is None else acc + y
            outs.append(acc)
        return jnp.stack(outs)

    def conv_tm(n, section):
        n5 = n.reshape(rows, 2, frames, cols, chans)
        blank = jnp.zeros((rows, 2, 1, cols, chans), n.dtype)
        before = jnp.concatenate([blank, n5[:, :, :-1]], axis=2)
        after = jnp.concatenate([n5[:, :, 1:], blank], axis=2)
        flat = rows * blocks * cols
        acc = mm(before.reshape(flat, chans), wt_ref[section, 0])
        acc = acc + mm(n.reshape(flat, chans), wt_ref[section, 1])
        acc = acc + mm(after.reshape(flat, chans), wt_ref[section, 2])
        return acc.reshape(rows, blocks, cols, chans)

    per_frame = float(chans // GROUPS * rows * cols)
    per_sample = per_frame * frames
    for section in range(wsp_ref.shape[0]):
        x = state.astype(jnp.float32)
        normed = norm_silu(x, None, per_frame)
        if section == 0:
            copy_sp.wait()
        state = (x + conv_sp(normed, section)).astype(jnp.bfloat16)
        x = state.astype(jnp.float32)
        normed = norm_silu(x, batch_mix, per_sample)
        state = (x + conv_tm(normed, section)).astype(jnp.bfloat16)
    last = norm_silu(state.astype(jnp.float32), None, per_frame)
    x0 = last[0].reshape(blocks * cols, chans)
    x1 = last[1].reshape(blocks * cols, chans)
    stride = out_ref.shape[1]
    lane = lax.broadcasted_iota(jnp.int32, (stride, blocks * cols), 1) % cols

    def mm_t(w, a):
        return lax.dot_general(w, a, (((1,), (1,)), ((), ())), preferred_element_type=jnp.float32)

    for row in range(rows):
        own, other = (x0, x1) if row == 0 else (x1, x0)
        other_dr = 1 if row == 0 else -1
        y = mm_t(wl_ref[3 * stride : 6 * stride], own)
        y = y + mm_t(wl_ref[(other_dr + 1) * 3 * stride : (other_dr + 2) * 3 * stride], other)
        acc = None
        for dc in (-1, 0, 1):
            part = y[(dc + 1) * stride : (dc + 2) * stride]
            if dc == -1:
                part = jnp.where(lane == 0, 0.0, pltpu.roll(part, 1, 1))
            elif dc == 1:
                part = jnp.where(lane == cols - 1, 0.0, pltpu.roll(part, blocks * cols - 1, 1))
            acc = part if acc is None else acc + part
        out_ref[row] = acc


def unet(first, emb_u, time_vector, pooled, text_proj, spatial_weights, temporal_weights, conv_last, count):
    rows, frames, cols, chans = first.shape
    blocks = 2 * frames
    taps, outs, _ = conv_last.shape
    padded = -(-outs // 16) * 16
    last = jnp.concatenate([conv_last, jnp.zeros((taps, padded - outs, chans), conv_last.dtype)], axis=1)
    last = last.reshape(taps * padded, chans)
    group = jnp.arange(chans) // (chans // GROUPS)
    same = (group[:, None] == group[None, :]).astype(jnp.float32)
    block_of = jnp.arange(blocks) // frames
    batch_mix = (block_of[:, None] == block_of[None, :]).astype(jnp.float32)
    vmem = pl.BlockSpec(memory_space=pltpu.MemorySpace.VMEM)
    anywhere = pl.BlockSpec(memory_space=pl.ANY)
    return pl.pallas_call(
        functools.partial(unet_body, count=float(count)),
        out_shape=jax.ShapeDtypeStruct((rows, padded, blocks * cols), jnp.float32),
        in_specs=[vmem] * 8 + [anywhere, vmem],
        out_specs=vmem,
        scratch_shapes=[
            pltpu.VMEM(spatial_weights.shape, spatial_weights.dtype),
            pltpu.SemaphoreType.DMA((1,)),
        ],
        compiler_params=pltpu.CompilerParams(vmem_limit_bytes=100 * 1024 * 1024 // 2),
        cost_estimate=pl.CostEstimate(
            flops=2 * rows * blocks * cols * chans * chans * 9 * spatial_weights.shape[0],
            transcendentals=rows * blocks * cols * chans * 5,
            bytes_accessed=spatial_weights.size * 2 + temporal_weights.size * 2 + first.size * 4,
        ),
    )(first, emb_u, time_vector, pooled, text_proj, last, same, batch_mix, spatial_weights, temporal_weights)[:, :outs]


def butterfly_sum(x, axis):
    peers = lax.axis_size(axis)
    if peers & (peers - 1):
        return jnp.sum(lax.all_gather(x, axis), axis=0)
    k = peers // 2
    while k:
        x = x + lax.ppermute(x, axis, [(i, i ^ k) for i in range(peers)])
        k //= 2
    return x


def butterfly_scan(x, axis):
    peers, me = lax.axis_size(axis), lax.axis_index(axis)
    if peers & (peers - 1):
        everything = lax.all_gather(x, axis)
        lower = (jnp.arange(peers) < me).reshape((peers,) + (1,) * x.ndim)
        return jnp.sum(jnp.where(lower, everything, 0.0), axis=0), jnp.sum(everything, axis=0)
    total, before = x, jnp.zeros_like(x)
    k = 1
    while k < peers:
        got = lax.ppermute(total, axis, [(i, i ^ k) for i in range(peers)])
        before = jnp.where((me & k) != 0, before + got, before)
        total = total + got
        k *= 2
    return before, total


def local(
    timesteps,
    prompt_ids,
    start_latent,
    iterate,
    fresh_noise,
    token_table,
    empty_text,
    time_in,
    time_out,
    text_proj,
    conv_first,
    spatial_weights,
    temporal_weights,
    conv_last,
):
    shard_rows = token_table.shape[0]
    first_row = lax.axis_index("slot") * shard_rows
    local_ids = prompt_ids - first_row
    hits = local_ids[:, None] == jnp.arange(shard_rows, dtype=jnp.int32)[None, :]
    counts = jnp.sum(hits.astype(jnp.float32), axis=0).astype(jnp.bfloat16)[None]
    partial = jnp.dot(counts, token_table, preferred_element_type=jnp.float32)[0]
    pooled = butterfly_sum(partial, "slot")[None]
    text_uncond = layer_norm(empty_text).astype(jnp.bfloat16)[None]
    vector_uncond = jnp.dot(text_uncond, text_proj, preferred_element_type=jnp.float32)
    half_width = time_in.shape[0] // 2
    frequency = jnp.exp(-jnp.log(10000.0) * jnp.arange(half_width, dtype=jnp.float32) / half_width)
    step_value = timesteps[0].astype(jnp.float32)
    angles = step_value * frequency
    feature = jnp.concatenate([jnp.cos(angles), jnp.sin(angles)]).astype(jnp.bfloat16)[None, :]
    hidden = jax.nn.silu(jnp.dot(feature, time_in, preferred_element_type=jnp.float32)).astype(
        jnp.bfloat16
    )
    time_vector = jnp.dot(hidden, time_out, preferred_element_type=jnp.float32)
    latent = iterate[0]
    first = conv_lifted(latent.astype(jnp.bfloat16), conv_first)
    rows, frames, cols, chans = first.shape
    predicted = unet(
        first, vector_uncond + time_vector, time_vector, pooled, text_proj,
        spatial_weights, temporal_weights, conv_last, prompt_ids.shape[0],
    )
    predicted = predicted.reshape(rows, -1, 2, frames, cols).transpose(2, 1, 3, 0, 4)
    guided = predicted[1] + GUIDANCE_SCALE * (predicted[0] - predicted[1])
    alpha_now = alpha_bar(step_value)
    alpha_prev = alpha_bar(step_value - DT)
    scale_ratio = jnp.sqrt(alpha_prev / alpha_now)
    noise_square = (1.0 - alpha_prev) * (1.0 - alpha_now / alpha_prev) / (1.0 - alpha_now)
    kept_square = (1.0 - alpha_prev) * (alpha_now / alpha_prev - alpha_now) / (1.0 - alpha_now)
    eps_factor = jnp.sqrt(kept_square) - scale_ratio * jnp.sqrt(1.0 - alpha_now)
    drift_term = (
        (scale_ratio - 1.0) * latent + eps_factor * guided + jnp.sqrt(noise_square) * fresh_noise[0]
    )[None]
    earlier, total_drift = butterfly_scan(drift_term[0], "slot")
    new_iterate = start_latent[None] + earlier[None]
    final_latent = start_latent + total_drift
    return (new_iterate, final_latent)


def solution(mesh):
    placed = (
        P(("groups", "slot")),
        P("groups"),
        P("groups", None, None, None),
        P(("groups", "slot"), None, None, None, None),
        P(("groups", "slot"), None, None, None, None),
        P("slot", None),
        P(),
        P(),
        P(),
        P(),
        P(),
        P(),
        P(),
        P(),
    )
    return jax.shard_map(
        local,
        mesh=mesh,
        in_specs=placed,
        out_specs=(P(("groups", "slot"), None, None, None, None), P("groups", None, None, None)),
        check_vma=False,
    )
```
